512 devices in a mesh: section: 4 (over x_lo, core), batch: 128 (over z, y, x_hi).
Axes of the slice: x: 4 (x_hi: 2, x_lo: 2; x = x_hi * 2 + x_lo), y: 8, z: 8, core: 2. Of those that a mesh axis runs over, the one named last changes fastest.
Arguments:
- latents: bfloat16 [4096, 512], P('batch'), may hold values from -6 to 6
- token_slot: int32 [4096], P('batch'), may hold values from 0 to 4095, as said below
- cache_keys: bfloat16 [4096, 128, 512], P('batch', None, 'section'), may hold values from -320 to 320
- cache_values: bfloat16 [4096, 128, 512], P('batch', None, 'section'), may hold values from -6 to 6
- up_state: bfloat16 [4096, 512], P('batch'), may hold values from -6 to 6
- conv_state: bfloat16 [4096, 512], P('batch'), may hold values from -1 to 3
- cache_slot: int32 [4096], P('batch'), may hold values from 0 to 4095, as said below
- positions: int32 [4096], P('batch'), may hold values from 0 to 512
- up_kernel: float32 [4, 512], replicated, may hold values from -4 to 4
- norm_gain_one: float32 [512], replicated, may hold values from 0.1 to 1.9
- qkv_weight: bfloat16 [3, 512, 512], P(None, None, 'section'), may hold values from -0.25 to 0.25
- out_weight: bfloat16 [512, 512], P('section'), may hold values from -0.25 to 0.25
- scale_attention: float32 [512], replicated, may hold values from 0.1 to 1.9
- norm_gain_two: float32 [512], replicated, may hold values from 0.1 to 1.9
- in_weight: bfloat16 [512, 2048], P(None, 'section'), may hold values from -0.25 to 0.25
- down_weight: bfloat16 [2048, 512], P('section'), may hold values from -0.125 to 0.125
- scale_feedforward: float32 [512], replicated, may hold values from 0.1 to 1.9
- conv_weight: bfloat16 [16, 256, 512], P(None, 'section'), may hold values from -0.1875 to 0.1875
- conv_bias: float32 [256], P('section'), may hold values from -3 to 3
Outputs:
- audio_out: float32 [256, 65536], P('section', 'batch')
- new_keys: bfloat16 [4096, 128, 512], P('batch', None, 'section')
- new_values: bfloat16 [4096, 128, 512], P('batch', None, 'section')
- new_up_state: bfloat16 [4096, 512], P('batch')
- new_conv_state: bfloat16 [4096, 512], P('batch')
The draws below stay inside these ranges and needn't reach their ends.
Inputs may be any that keep to these rules, and one draw needn't show every extreme that they name: `token_slot`: every slot receives exactly one token row. The 32 rows of one transformer owner go in groups of exactly 2 rows to 16 different decoder owners; the decoder owner of slot n is n // 32. `cache_slot`: A permutation of the slots. Each batch index keeps all but 2 * 1 of its streams and hands exactly 1 to the index one higher and 1 to the index one lower, cyclically.
All inputs are finite; a program needn't handle non-finite values.
Results may differ from the reference program's by a relative error of at most 0.017.
Values may be sent and summed in bfloat16 or wider, within the bound.
No kernel may reach another device: no remote copies, remote signals or barrier semaphores. Data moves between devices by JAX's collectives and lax.ppermute only.
A program may use at most 64 MiB of HBM per device.

```python
import jax
import jax.numpy as jnp
from jax import lax

D = 512
HEADS = 8
HEAD_DIM = 64
FFN = 2048
WINDOW = 128
STRIDE = 8
C_OUT = 256
MOVE = 1
S_DEV = 32
CONV_IN = 512
KERNEL = 16
CAP = 2
STREAMS = 4096


def device_perms(seed_key, copies, length):
    seed_keys = jax.random.split(seed_key, copies)
    return jax.vmap(lambda single: jax.random.permutation(single, length))(seed_keys)


def draw_token_slot(key, part):
    owners = STREAMS // S_DEV
    groups = S_DEV // CAP
    key_offset, key_rows, key_slots = jax.random.split(jax.random.fold_in(key, 101), 3)
    offset_rank = jax.random.permutation(key_offset, owners).astype(jnp.int32)
    offset_ids = jnp.arange(owners, dtype=jnp.int32)
    required = (offset_ids == owners // 2) | (offset_ids == 1) | (offset_ids == owners - 1)
    priority = offset_rank + jnp.where(required, owners, 0).astype(jnp.int32)
    offsets = jnp.argsort(-priority)[:groups].astype(jnp.int32)
    row_order = device_perms(key_rows, owners, S_DEV)
    slot_order = device_perms(key_slots, owners, S_DEV)
    source = jnp.broadcast_to(jnp.arange(owners, dtype=jnp.int32)[:, None], (owners, S_DEV))
    member = jnp.broadcast_to(jnp.arange(S_DEV, dtype=jnp.int32)[None, :], (owners, S_DEV))
    target = jnp.mod(source + offsets[member // CAP], owners)
    slot_value = target * S_DEV + slot_order[target, member]
    row_index = source * S_DEV + row_order
    result = jnp.zeros((STREAMS,), jnp.int32)
    return result.at[row_index.reshape(-1)].set(slot_value.reshape(-1).astype(jnp.int32))


def draw_cache_slot(key, part):
    owners = STREAMS // S_DEV
    key_send, key_land = jax.random.split(jax.random.fold_in(key, 202), 2)
    send_order = device_perms(key_send, owners, S_DEV)
    land_order = device_perms(key_land, owners, S_DEV)
    source = jnp.broadcast_to(jnp.arange(owners)[:, None], (owners, S_DEV))
    member = jnp.broadcast_to(jnp.arange(S_DEV)[None, :], (owners, S_DEV))
    target = jnp.where(member < MOVE, jnp.mod(source + 1, owners), jnp.where(member < 2 * MOVE, jnp.mod(source + owners - 1, owners), source))
    slot_value = target * S_DEV + land_order[target, member]
    row_index = source * S_DEV + send_order
    result = jnp.zeros((STREAMS,), jnp.int32)
    return result.at[row_index.reshape(-1)].set(slot_value.reshape(-1).astype(jnp.int32))


def draw_positions(key, part):
    largest = 4 * WINDOW
    drawn_values = jax.random.randint(jax.random.fold_in(key, 303), (STREAMS,), 0, largest + 1, dtype=jnp.int32)
    return drawn_values.at[0].set(largest)


def draw_cache_keys(key, part):
    key_main = jax.random.fold_in(jax.random.fold_in(key, 404), 0)
    entries = jnp.clip(jax.random.normal(key_main, (STREAMS, WINDOW, D), jnp.float32), -4.0, 4.0)
    return entries.astype(jnp.bfloat16)


def block_levels(stream_key, dims, pieces, least, top_value):
    gain = 1.0
    for axis_at, parts in pieces:
        heights = jax.random.uniform(jax.random.fold_in(jax.random.fold_in(stream_key, 6), axis_at), (parts,), jnp.float32, least / len(pieces), top_value / len(pieces))
        gain = gain * jnp.repeat(jnp.exp(heights), dims[axis_at] // parts).reshape((-1,) + (1,) * (len(dims) - 1 - axis_at))
    return gain


def gaussian(rng, dims, spread, most, cuts=(), kind=jnp.bfloat16):
    values = jax.random.normal(rng, dims, jnp.float32) * spread
    if len(cuts) > 0:
        values = block_levels(rng, dims, cuts, -0.22, 0.18) * values
    return jnp.clip(values, min=-most, max=most).astype(kind)


def setup_inputs(seed: int = 0) -> dict:
    keys = jax.random.split(jax.random.key(seed), 20)
    return {
        "latents": gaussian(keys[0], (STREAMS, D), 1.0, 6.0, ((0, 128),)),
        "token_slot": draw_token_slot(jax.random.fold_in(keys[19], 71), 0),
        "cache_keys": draw_cache_keys(jax.random.fold_in(keys[19], 71), 0),
        "cache_values": gaussian(keys[3], (STREAMS, WINDOW, D), 1.0, 6.0, ((0, 128), (2, 4))),
        "up_state": gaussian(keys[4], (STREAMS, D), 1.0, 6.0, ((0, 128),)),
        "conv_state": jnp.clip(-1.0 + 4.0 * jax.random.uniform(keys[5], (STREAMS, D), jnp.float32) ** block_levels(keys[5], (STREAMS, D), ((0, 128),), -0.2, 0.2), -1.0, 3.0).astype(jnp.bfloat16),
        "cache_slot": draw_cache_slot(jax.random.fold_in(keys[19], 71), 0),
        "positions": draw_positions(jax.random.fold_in(keys[19], 71), 0),
        "up_kernel": gaussian(keys[8], (4, D), 0.7, 4.0, (), jnp.float32),
        "norm_gain_one": jnp.clip(1.0 + 0.18 * jax.random.normal(keys[9], (D,), jnp.float32), 0.1, 1.9),
        "qkv_weight": gaussian(keys[10], (3, D, D), D ** -0.5, 0.25, ((2, 4),)),
        "out_weight": gaussian(keys[11], (D, D), D ** -0.5, 0.25, ((0, 4),)),
        "scale_attention": jnp.clip(1.0 + 0.18 * jax.random.normal(keys[12], (D,), jnp.float32), 0.1, 1.9),
        "norm_gain_two": jnp.clip(1.0 + 0.18 * jax.random.normal(keys[13], (D,), jnp.float32), 0.1, 1.9),
        "in_weight": gaussian(keys[14], (D, FFN), D ** -0.5, 0.25, ((1, 4),)),
        "down_weight": gaussian(keys[15], (FFN, D), FFN ** -0.5, 0.125, ((0, 4),)),
        "scale_feedforward": jnp.clip(1.0 + 0.18 * jax.random.normal(keys[16], (D,), jnp.float32), 0.1, 1.9),
        "conv_weight": gaussian(keys[17], (KERNEL, C_OUT, CONV_IN), (2 * CONV_IN) ** -0.5, 0.1875, ((1, 4),)),
        "conv_bias": gaussian(keys[18], (C_OUT,), 0.5, 3.0, ((0, 4),), jnp.float32),
    }


EPSILON = 1e-05
MAX_PERIOD = 10000.0

def layer_norm(hidden, weight_gain):
    average = lax.optimization_barrier(jnp.mean(hidden, axis=-1, keepdims=True))
    centred = hidden - average
    variance = lax.optimization_barrier(jnp.mean(centred * centred, axis=-1, keepdims=True))
    return centred * lax.rsqrt(variance + EPSILON) * weight_gain

def rotate(features, times, head_width):
    streams = features.shape[0]
    half = head_width // 2
    freqs = MAX_PERIOD ** (-2.0 * jnp.arange(half, dtype=jnp.float32) / head_width)
    angle = times.astype(jnp.float32)[:, :, None] * freqs[None, None, :]
    cosine = jnp.cos(angle)[:, :, None, :]
    sine = jnp.sin(angle)[:, :, None, :]
    paired = features.reshape(streams, 2, -1, half, 2)
    first = paired[..., 0]
    second = paired[..., 1]
    turned = jnp.stack([first * cosine - second * sine, first * sine + second * cosine], axis=-1)
    return turned.reshape(features.shape)

def attend(queries, fresh_keys, fresh_values, old_keys, old_values, starts):
    streams = queries.shape[0]
    query_heads = queries.astype(jnp.float32).reshape(streams, 2, HEADS, HEAD_DIM)
    cache_heads = old_keys.astype(jnp.float32).reshape(streams, WINDOW, HEADS, HEAD_DIM)
    fresh_heads = fresh_keys.astype(jnp.float32).reshape(streams, 2, HEADS, HEAD_DIM)
    score_scale = HEAD_DIM ** (-0.5)
    cache_scores = jnp.einsum('sfhe,swhe->shfw', query_heads, cache_heads) * score_scale
    fresh_scores = jnp.einsum('sfhe,sghe->shfg', query_heads, fresh_heads) * score_scale
    cycle_slots = jnp.arange(WINDOW, dtype=jnp.int32)
    held_time = starts[:, None] - WINDOW + jnp.mod(cycle_slots[None, :] - starts[:, None], WINDOW)
    query_times = starts[:, None] + jnp.arange(2, dtype=jnp.int32)[None, :]
    cache_ok = (held_time[:, None, :] >= 0) & (held_time[:, None, :] > query_times[:, :, None] - WINDOW)
    frame_ids = jnp.arange(2, dtype=jnp.int32)
    fresh_ok = frame_ids[None, :] <= frame_ids[:, None]
    allowed = jnp.concatenate([jnp.broadcast_to(cache_ok[:, None], (streams, HEADS, 2, WINDOW)), jnp.broadcast_to(fresh_ok, (streams, HEADS, 2, 2))], axis=-1)
    scores = jnp.concatenate([cache_scores, fresh_scores], axis=-1)
    scores = jnp.where(allowed, scores, -jnp.inf)
    score_max = lax.optimization_barrier(jnp.max(scores, axis=-1, keepdims=True))
    weights = jnp.where(allowed, jnp.exp(scores - score_max), 0.0)
    denominator = lax.optimization_barrier(jnp.sum(weights, axis=-1, keepdims=True))
    rounded = weights.astype(jnp.bfloat16)
    all_values = jnp.concatenate([old_values.reshape(streams, WINDOW, HEADS, HEAD_DIM), fresh_values.reshape(streams, 2, HEADS, HEAD_DIM)], axis=1)
    attended = jnp.einsum('shfw,swhe->sfhe', rounded.astype(jnp.float32), all_values.astype(jnp.float32))
    attended = attended / jnp.transpose(denominator, (0, 2, 1, 3))
    return attended.astype(jnp.bfloat16).reshape(streams, 2, HEADS * HEAD_DIM)

def reference(latents, token_slot, cache_keys, cache_values, up_state, conv_state, cache_slot, positions, up_kernel, norm_gain_one, qkv_weight, out_weight, scale_attention, norm_gain_two, in_weight, down_weight, scale_feedforward, conv_weight, conv_bias):
    arrived = jnp.zeros_like(latents).at[token_slot].set(latents)
    keys_old = jnp.zeros_like(cache_keys).at[cache_slot].set(cache_keys)
    values_old = jnp.zeros_like(cache_values).at[cache_slot].set(cache_values)
    up_prev = jnp.zeros_like(up_state).at[cache_slot].set(up_state)
    conv_prev = jnp.zeros_like(conv_state).at[cache_slot].set(conv_state)
    latent_f = arrived.astype(jnp.float32)
    prior_f = up_prev.astype(jnp.float32)
    residual_zero = jnp.stack([latent_f * up_kernel[0] + prior_f * up_kernel[2], latent_f * up_kernel[1] + prior_f * up_kernel[3]], axis=1)
    normed_one = layer_norm(residual_zero, norm_gain_one).astype(jnp.bfloat16)
    projections = jnp.einsum('sfd,kde->ksfe', normed_one.astype(jnp.float32), qkv_weight.astype(jnp.float32))
    times = positions[:, None] + jnp.arange(2, dtype=jnp.int32)[None, :]
    queries = rotate(projections[0], times, HEAD_DIM).astype(jnp.bfloat16)
    fresh_keys = rotate(projections[1], times, HEAD_DIM).astype(jnp.bfloat16)
    fresh_values = projections[2].astype(jnp.bfloat16)
    blocks = STREAMS // S_DEV

    def one_block(block_args):
        return attend(*block_args)
    block_inputs = (queries.reshape(blocks, S_DEV, 2, D), fresh_keys.reshape(blocks, S_DEV, 2, D), fresh_values.reshape(blocks, S_DEV, 2, D), keys_old.reshape(blocks, S_DEV, WINDOW, D), values_old.reshape(blocks, S_DEV, WINDOW, D), positions.reshape(blocks, S_DEV))
    attended = lax.map(one_block, block_inputs).reshape(STREAMS, 2, D)
    mixing = jnp.dot(attended.reshape(STREAMS * 2, D), out_weight, preferred_element_type=jnp.float32)
    residual_one = residual_zero + scale_attention * mixing.reshape(STREAMS, 2, D)
    normed_two = layer_norm(residual_one, norm_gain_two).astype(jnp.bfloat16).reshape(STREAMS * 2, D)
    inner_units = jax.nn.gelu(jnp.dot(normed_two, in_weight, preferred_element_type=jnp.float32), approximate=False).astype(jnp.bfloat16)
    feed = jnp.dot(inner_units, down_weight, preferred_element_type=jnp.float32).reshape(STREAMS, 2, D)
    residual_two = residual_one + scale_feedforward * feed
    excited = jax.nn.elu(residual_two).astype(jnp.bfloat16)
    earlier = jnp.stack([conv_prev, excited[:, 0]], axis=1)
    taps_now = conv_weight[:STRIDE].astype(jnp.float32)
    taps_before = conv_weight[STRIDE:].astype(jnp.float32)
    audio_out = jnp.einsum('sfi,rci->csfr', excited.astype(jnp.float32), taps_now)
    audio_out = audio_out + jnp.einsum('sfi,rci->csfr', earlier.astype(jnp.float32), taps_before)
    audio_out = audio_out + conv_bias[:, None, None, None]
    audio_out = audio_out.reshape(C_OUT, STREAMS * 2 * STRIDE)
    stream_ids = jnp.arange(STREAMS, dtype=jnp.int32)
    slot_first = jnp.mod(positions, WINDOW)
    slot_second = jnp.mod(positions + 1, WINDOW)
    new_keys = keys_old.at[stream_ids, slot_first].set(fresh_keys[:, 0]).at[stream_ids, slot_second].set(fresh_keys[:, 1])
    new_values = values_old.at[stream_ids, slot_first].set(fresh_values[:, 0]).at[stream_ids, slot_second].set(fresh_values[:, 1])
    return (audio_out, new_keys, new_values, arrived, excited[:, 1])
```

```python
import jax
import jax.numpy as jnp
from jax import lax
from jax.sharding import PartitionSpec as P

HEAD_DIM = 64
CAP = 2
CODE_LANES = 128


EPSILON = 1e-05
MAX_PERIOD = 10000.0


def layer_norm(hidden, weight_gain):
    average = jnp.mean(hidden, axis=-1, keepdims=True)
    centred = hidden - average
    variance = jnp.mean(centred * centred, axis=-1, keepdims=True)
    return centred * lax.rsqrt(variance + EPSILON) * weight_gain


def rotate(features, times, head_width):
    streams = features.shape[0]
    half = head_width // 2
    freqs = MAX_PERIOD ** (-2.0 * jnp.arange(half, dtype=jnp.float32) / head_width)
    angle = times.astype(jnp.float32)[:, :, None] * freqs[None, None, :]
    cosine = jnp.cos(angle)[:, :, None, :]
    sine = jnp.sin(angle)[:, :, None, :]
    paired = features.reshape(streams, 2, -1, half, 2)
    first = paired[..., 0]
    second = paired[..., 1]
    turned = jnp.stack([first * cosine - second * sine, first * sine + second * cosine], axis=-1)
    return turned.reshape(features.shape)


def attend(
    queries, fresh_keys, fresh_values, old_keys, old_values, starts, local_heads, head_width
):
    streams = old_keys.shape[0]
    window = old_keys.shape[1]
    query_heads = queries.reshape(streams, 2, local_heads, head_width)
    cache_heads = old_keys.reshape(streams, window, local_heads, head_width)
    fresh_heads = fresh_keys.reshape(streams, 2, local_heads, head_width)
    score_scale = head_width ** (-0.5)
    cache_scores = (
        jnp.einsum("sfhe,swhe->shfw", query_heads, cache_heads, preferred_element_type=jnp.float32)
        * score_scale
    )
    fresh_scores = (
        jnp.einsum("sfhe,sghe->shfg", query_heads, fresh_heads, preferred_element_type=jnp.float32)
        * score_scale
    )
    cycle_slots = jnp.arange(window, dtype=jnp.int32)
    held_time = starts[:, None] - window + jnp.mod(cycle_slots[None, :] - starts[:, None], window)
    query_times = starts[:, None] + jnp.arange(2, dtype=jnp.int32)[None, :]
    cache_ok = (held_time[:, None, :] >= 0) & (
        held_time[:, None, :] > query_times[:, :, None] - window
    )
    frame_ids = jnp.arange(2, dtype=jnp.int32)
    fresh_ok = frame_ids[None, :] <= frame_ids[:, None]
    allowed = jnp.concatenate(
        [
            jnp.broadcast_to(cache_ok[:, None], (streams, local_heads, 2, window)),
            jnp.broadcast_to(fresh_ok, (streams, local_heads, 2, 2)),
        ],
        axis=-1,
    )
    scores = jnp.concatenate([cache_scores, fresh_scores], axis=-1)
    scores = jnp.where(allowed, scores, -jnp.inf)
    score_max = jnp.max(scores, axis=-1, keepdims=True)
    weights = jnp.where(allowed, jnp.exp(scores - score_max), 0.0)
    denominator = jnp.sum(weights, axis=-1, keepdims=True)
    rounded = weights.astype(jnp.bfloat16)
    value_heads = old_values.reshape(streams, window, local_heads, head_width)
    fresh_value_heads = fresh_values.reshape(streams, 2, local_heads, head_width)
    attended = jnp.einsum(
        "shfw,swhe->sfhe", rounded[..., :window], value_heads, preferred_element_type=jnp.float32
    )
    attended = attended + jnp.einsum(
        "shfg,sghe->sfhe",
        rounded[..., window:],
        fresh_value_heads,
        preferred_element_type=jnp.float32,
    )
    attended = attended / jnp.transpose(denominator, (0, 2, 1, 3))
    return attended.astype(jnp.bfloat16).reshape(streams, 2, local_heads * head_width)


def section_sum(partial):
    size = lax.axis_size("section")
    if size & (size - 1):
        return lax.psum(partial.astype(jnp.bfloat16), "section").astype(jnp.float32)
    total = partial.astype(jnp.bfloat16)
    bit = size // 2
    while bit >= 1:
        route = [(i, i ^ bit) for i in range(size)]
        other = lax.ppermute(total, "section", route)
        total = total.astype(jnp.float32) + other.astype(jnp.float32)
        bit //= 2
    return total


def one_hot(rows, columns):
    return (rows[:, None] == columns[None, :]).astype(jnp.bfloat16)


def local(
    latents,
    token_slot,
    cache_keys,
    cache_values,
    up_state,
    conv_state,
    cache_slot,
    positions,
    up_kernel,
    norm_gain_one,
    qkv_weight,
    out_weight,
    scale_attention,
    norm_gain_two,
    in_weight,
    down_weight,
    scale_feedforward,
    conv_weight,
    conv_bias,
):
    owners = lax.axis_size("batch")
    own_index = lax.axis_index("batch")
    streams = latents.shape[0]
    model_width = latents.shape[1]
    window = cache_keys.shape[1]
    head_share = cache_keys.shape[2]
    capacity = max(CAP, streams // owners)
    slot_ids = jnp.arange(streams, dtype=jnp.int32)

    dest_owner = cache_slot // streams
    dest_local = cache_slot % streams
    right_owner = jnp.mod(own_index + 1, owners)
    left_owner = jnp.mod(own_index + owners - 1, owners)
    state_rows = model_width // head_share

    def pack(direction_owner):
        chosen = jnp.sum(jnp.where(dest_owner == direction_owner, slot_ids, 0))
        code = lax.dynamic_index_in_dim(dest_local, chosen, 0, keepdims=False) + 1
        pieces = [
            lax.dynamic_index_in_dim(cache_keys, chosen, 0, keepdims=False),
            lax.dynamic_index_in_dim(cache_values, chosen, 0, keepdims=False),
            lax.dynamic_index_in_dim(up_state, chosen, 0, keepdims=False).reshape(
                state_rows, head_share
            ),
            lax.dynamic_index_in_dim(conv_state, chosen, 0, keepdims=False).reshape(
                state_rows, head_share
            ),
            jnp.full((8, head_share), code, jnp.int32).astype(jnp.bfloat16),
        ]
        return jnp.concatenate(pieces, axis=0)

    def unpack(box):
        keys = box[:window]
        values = box[window : 2 * window]
        up = box[2 * window : 2 * window + state_rows].reshape(model_width)
        conv = box[2 * window + state_rows : 2 * window + 2 * state_rows].reshape(model_width)
        code = box[2 * window + 2 * state_rows, 0].astype(jnp.int32) - 1
        return keys, values, up, conv, code

    from_left = unpack(
        lax.ppermute(pack(right_owner), "batch", [(i, (i + 1) % owners) for i in range(owners)])
    )
    from_right = unpack(
        lax.ppermute(pack(left_owner), "batch", [(i, (i - 1) % owners) for i in range(owners)])
    )

    target = token_slot // streams
    landing = token_slot % streams
    same_before = (target[None, :] == target[:, None]) & (slot_ids[None, :] < slot_ids[:, None])
    arrival_rank = jnp.sum(same_before.astype(jnp.int32), axis=1)
    box_ids = target * capacity + arrival_rank
    payload = jnp.concatenate(
        [
            latents,
            jnp.broadcast_to((landing + 1).astype(jnp.bfloat16)[:, None], (streams, CODE_LANES)),
        ],
        axis=1,
    )
    placing = one_hot(jnp.arange(owners * capacity, dtype=jnp.int32), box_ids)
    send_rows = jnp.dot(placing, payload, preferred_element_type=jnp.float32).astype(jnp.bfloat16)
    got = lax.all_to_all(
        send_rows.reshape(owners, capacity, model_width + CODE_LANES),
        "batch",
        split_axis=0,
        concat_axis=0,
        tiled=True,
    ).reshape(owners * capacity, model_width + CODE_LANES)
    got_codes = got[:, model_width].astype(jnp.int32) - 1
    arrived = jnp.dot(
        one_hot(slot_ids, got_codes), got[:, :model_width], preferred_element_type=jnp.float32
    ).astype(jnp.bfloat16)

    staying = dest_owner == own_index
    source_of = (dest_local[None, :] == slot_ids[:, None]) & staying[None, :]
    picking = source_of.astype(jnp.bfloat16)
    from_l = slot_ids == from_left[4]
    from_r = slot_ids == from_right[4]

    def gathered(own_rows, left_row, right_row):
        flat = own_rows.reshape(streams, -1)
        rows = jnp.dot(picking, flat, preferred_element_type=jnp.float32).astype(own_rows.dtype)
        rows = rows.reshape(own_rows.shape)
        shape = (streams,) + (1,) * (own_rows.ndim - 1)
        rows = jnp.where(from_l.reshape(shape), left_row[None], rows)
        return jnp.where(from_r.reshape(shape), right_row[None], rows)

    keys_old = gathered(cache_keys, from_left[0], from_right[0])
    values_old = gathered(cache_values, from_left[1], from_right[1])
    up_prev = gathered(up_state, from_left[2], from_right[2])
    conv_prev = gathered(conv_state, from_left[3], from_right[3])

    latent_f = arrived.astype(jnp.float32)
    prior_f = up_prev.astype(jnp.float32)
    residual_zero = jnp.stack(
        [
            latent_f * up_kernel[0] + prior_f * up_kernel[2],
            latent_f * up_kernel[1] + prior_f * up_kernel[3],
        ],
        axis=1,
    )
    normed_one = layer_norm(residual_zero, norm_gain_one).astype(jnp.bfloat16)
    projections = jnp.einsum(
        "sfd,kde->ksfe", normed_one, qkv_weight, preferred_element_type=jnp.float32
    )
    times = positions[:, None] + jnp.arange(2, dtype=jnp.int32)[None, :]
    queries = rotate(projections[0], times, HEAD_DIM).astype(jnp.bfloat16)
    fresh_keys = rotate(projections[1], times, HEAD_DIM).astype(jnp.bfloat16)
    fresh_values = projections[2].astype(jnp.bfloat16)
    attended = attend(
        queries,
        fresh_keys,
        fresh_values,
        keys_old,
        values_old,
        positions,
        head_share // HEAD_DIM,
        HEAD_DIM,
    )
    partial_heads = jnp.dot(
        attended.reshape(2 * streams, head_share), out_weight, preferred_element_type=jnp.float32
    )
    mixing = section_sum(partial_heads)
    residual_one = residual_zero + scale_attention * mixing.reshape(streams, 2, model_width)
    normed_two = (
        layer_norm(residual_one, norm_gain_two)
        .astype(jnp.bfloat16)
        .reshape(2 * streams, model_width)
    )
    inner_units = jax.nn.gelu(
        jnp.dot(normed_two, in_weight, preferred_element_type=jnp.float32), approximate=False
    ).astype(jnp.bfloat16)
    partial_units = jnp.dot(inner_units, down_weight, preferred_element_type=jnp.float32)
    feed_forward = section_sum(partial_units)
    residual_two = residual_one + scale_feedforward * feed_forward.reshape(streams, 2, model_width)
    excited = jax.nn.elu(residual_two).astype(jnp.bfloat16)
    earlier = jnp.stack([conv_prev, excited[:, 0]], axis=1)
    stride = conv_weight.shape[0] // 2
    audio_out = jnp.einsum(
        "sfi,rci->csfr", excited, conv_weight[:stride], preferred_element_type=jnp.float32
    )
    audio_out = audio_out + jnp.einsum(
        "sfi,rci->csfr", earlier, conv_weight[stride:], preferred_element_type=jnp.float32
    )
    audio_out = audio_out + conv_bias[:, None, None, None]
    audio_out = audio_out.reshape(conv_bias.shape[0], streams * 2 * stride)
    cycle = jnp.arange(window, dtype=jnp.int32)
    hit_first = (cycle[None, :] == jnp.mod(positions, window)[:, None])[..., None]
    hit_second = (cycle[None, :] == jnp.mod(positions + 1, window)[:, None])[..., None]
    new_keys = jnp.where(
        hit_second,
        fresh_keys[:, 1][:, None, :],
        jnp.where(hit_first, fresh_keys[:, 0][:, None, :], keys_old),
    )
    new_values = jnp.where(
        hit_second,
        fresh_values[:, 1][:, None, :],
        jnp.where(hit_first, fresh_values[:, 0][:, None, :], values_old),
    )
    return (audio_out, new_keys, new_values, arrived, excited[:, 1])
def solution(mesh):
    placed = (
        P("batch", None),
        P("batch"),
        P("batch", None, "section"),
        P("batch", None, "section"),
        P("batch", None),
        P("batch", None),
        P("batch"),
        P("batch"),
        P(),
        P(),
        P(None, None, "section"),
        P("section", None),
        P(),
        P(),
        P(None, "section"),
        P("section", None),
        P(),
        P(None, "section", None),
        P("section"),
    )
    return jax.shard_map(
        local,
        mesh=mesh,
        in_specs=placed,
        out_specs=(
            P("section", "batch"),
            P("batch", None, "section"),
            P("batch", None, "section"),
            P("batch", None),
            P("batch", None),
        ),
        check_vma=False,
    )
```

```python
import jax
import jax.numpy as jnp
from jax import lax
from jax.sharding import PartitionSpec as P

HEAD_DIM = 64
CAP = 2
CODE_LANES = 128


EPSILON = 1e-05
MAX_PERIOD = 10000.0


def layer_norm(hidden, weight_gain):
    average = jnp.mean(hidden, axis=-1, keepdims=True)
    centred = hidden - average
    variance = jnp.mean(centred * centred, axis=-1, keepdims=True)
    return centred * lax.rsqrt(variance + EPSILON) * weight_gain


def rotate(features, times, head_width):
    streams = features.shape[0]
    half = head_width // 2
    freqs = MAX_PERIOD ** (-2.0 * jnp.arange(half, dtype=jnp.float32) / head_width)
    angle = times.astype(jnp.float32)[:, :, None] * freqs[None, None, :]
    cosine = jnp.cos(angle)[:, :, None, :]
    sine = jnp.sin(angle)[:, :, None, :]
    paired = features.reshape(streams, 2, -1, half, 2)
    first = paired[..., 0]
    second = paired[..., 1]
    turned = jnp.stack([first * cosine - second * sine, first * sine + second * cosine], axis=-1)
    return turned.reshape(features.shape)


def attend(queries, fresh_keys, fresh_values, old_keys, old_values, starts, local_heads, head_width):
    streams, window, share = old_keys.shape
    head_of = jnp.arange(share, dtype=jnp.int32) // head_width
    head_ids = jnp.arange(local_heads, dtype=jnp.int32)
    in_head = head_of[None, :] == head_ids[:, None]
    lanes = in_head[None, :, None, :]
    masked = jnp.where(lanes, queries[:, None], jnp.zeros((), queries.dtype))
    masked = masked.reshape(streams, local_heads * 2, share)
    score_scale = head_width ** (-0.5)
    cache_scores = (
        jnp.einsum("sxd,swd->sxw", masked, old_keys, preferred_element_type=jnp.float32)
        * score_scale
    )
    fresh_scores = (
        jnp.einsum("sxd,sgd->sxg", masked, fresh_keys, preferred_element_type=jnp.float32)
        * score_scale
    )
    cycle_slots = jnp.arange(window, dtype=jnp.int32)
    held_time = starts[:, None] - window + jnp.mod(cycle_slots[None, :] - starts[:, None], window)
    query_times = starts[:, None] + jnp.arange(2, dtype=jnp.int32)[None, :]
    cache_ok = (held_time[:, None, :] >= 0) & (
        held_time[:, None, :] > query_times[:, :, None] - window
    )
    cache_ok = jnp.broadcast_to(cache_ok[:, None], (streams, local_heads, 2, window)).reshape(
        streams, local_heads * 2, window
    )
    frame_ids = jnp.arange(2, dtype=jnp.int32)
    fresh_ok = jnp.tile(frame_ids[None, :] <= frame_ids[:, None], (local_heads, 1))[None]
    cache_scores = jnp.where(cache_ok, cache_scores, -jnp.inf)
    fresh_scores = jnp.where(fresh_ok, fresh_scores, -jnp.inf)
    score_max = jnp.maximum(
        jnp.max(cache_scores, axis=-1, keepdims=True), jnp.max(fresh_scores, axis=-1, keepdims=True)
    )
    cache_weights = jnp.where(cache_ok, jnp.exp(cache_scores - score_max), 0.0)
    fresh_weights = jnp.where(fresh_ok, jnp.exp(fresh_scores - score_max), 0.0)
    denominator = jnp.sum(cache_weights, axis=-1, keepdims=True) + jnp.sum(
        fresh_weights, axis=-1, keepdims=True
    )
    spread = jnp.einsum(
        "sxw,swd->sxd",
        cache_weights.astype(jnp.bfloat16),
        old_values,
        preferred_element_type=jnp.float32,
    )
    spread = spread + jnp.einsum(
        "sxg,sgd->sxd",
        fresh_weights.astype(jnp.bfloat16),
        fresh_values,
        preferred_element_type=jnp.float32,
    )
    spread = (spread / denominator).reshape(streams, local_heads, 2, share)
    attended = jnp.sum(jnp.where(lanes, spread, 0.0), axis=1)
    return attended.astype(jnp.bfloat16)


def section_sum(partial):
    size = lax.axis_size("section")
    if size & (size - 1):
        return lax.psum(partial.astype(jnp.bfloat16), "section").astype(jnp.float32)
    total = partial.astype(jnp.bfloat16)
    bit = size // 2
    while bit >= 1:
        route = [(i, i ^ bit) for i in range(size)]
        other = lax.ppermute(total, "section", route)
        total = total.astype(jnp.float32) + other.astype(jnp.float32)
        bit //= 2
    return total


def one_hot(rows, columns):
    return (rows[:, None] == columns[None, :]).astype(jnp.bfloat16)


def local(
    latents,
    token_slot,
    cache_keys,
    cache_values,
    up_state,
    conv_state,
    cache_slot,
    positions,
    up_kernel,
    norm_gain_one,
    qkv_weight,
    out_weight,
    scale_attention,
    norm_gain_two,
    in_weight,
    down_weight,
    scale_feedforward,
    conv_weight,
    conv_bias,
):
    owners = lax.axis_size("batch")
    own_index = lax.axis_index("batch")
    streams = latents.shape[0]
    model_width = latents.shape[1]
    window = cache_keys.shape[1]
    head_share = cache_keys.shape[2]
    capacity = max(CAP, streams // owners)
    slot_ids = jnp.arange(streams, dtype=jnp.int32)

    dest_owner = cache_slot // streams
    dest_local = cache_slot % streams
    right_owner = jnp.mod(own_index + 1, owners)
    left_owner = jnp.mod(own_index + owners - 1, owners)
    state_rows = model_width // head_share

    def pack(direction_owner):
        chosen = dest_owner == direction_owner
        code = jnp.sum(jnp.where(chosen, dest_local + 1, 0))

        def pick(rows):
            shape = (streams,) + (1,) * (rows.ndim - 1)
            return jnp.sum(jnp.where(chosen.reshape(shape), rows, jnp.zeros((), rows.dtype)), axis=0)

        pieces = [
            pick(cache_keys),
            pick(cache_values),
            pick(up_state).reshape(state_rows, head_share),
            pick(conv_state).reshape(state_rows, head_share),
            jnp.full((8, head_share), code, jnp.int32).astype(jnp.bfloat16),
        ]
        return jnp.concatenate(pieces, axis=0)

    def unpack(box):
        keys = box[:window]
        values = box[window : 2 * window]
        up = box[2 * window : 2 * window + state_rows].reshape(model_width)
        conv = box[2 * window + state_rows : 2 * window + 2 * state_rows].reshape(model_width)
        code = box[2 * window + 2 * state_rows, 0].astype(jnp.int32) - 1
        return keys, values, up, conv, code

    from_left = unpack(
        lax.ppermute(pack(right_owner), "batch", [(i, (i + 1) % owners) for i in range(owners)])
    )
    from_right = unpack(
        lax.ppermute(pack(left_owner), "batch", [(i, (i - 1) % owners) for i in range(owners)])
    )

    target = token_slot // streams
    landing = token_slot % streams
    same_before = (target[None, :] == target[:, None]) & (slot_ids[None, :] < slot_ids[:, None])
    arrival_rank = jnp.sum(same_before.astype(jnp.int32), axis=1)
    box_ids = target * capacity + arrival_rank
    payload = jnp.concatenate(
        [
            latents,
            jnp.broadcast_to((landing + 1).astype(jnp.bfloat16)[:, None], (streams, CODE_LANES)),
        ],
        axis=1,
    )
    placing = one_hot(jnp.arange(owners * capacity, dtype=jnp.int32), box_ids)
    send_rows = jnp.dot(placing, payload, preferred_element_type=jnp.float32).astype(jnp.bfloat16)
    got = lax.all_to_all(
        send_rows.reshape(owners, capacity, model_width + CODE_LANES),
        "batch",
        split_axis=0,
        concat_axis=0,
        tiled=True,
    ).reshape(owners * capacity, model_width + CODE_LANES)
    got_codes = got[:, model_width].astype(jnp.int32) - 1
    arrived = jnp.dot(
        one_hot(slot_ids, got_codes), got[:, :model_width], preferred_element_type=jnp.float32
    ).astype(jnp.bfloat16)

    staying = dest_owner == own_index
    source_of = (dest_local[None, :] == slot_ids[:, None]) & staying[None, :]
    picking = source_of.astype(jnp.bfloat16)
    from_l = slot_ids == from_left[4]
    from_r = slot_ids == from_right[4]

    def gathered(own_rows, left_row, right_row):
        rows = jnp.tensordot(picking, own_rows, axes=1, preferred_element_type=jnp.float32)
        rows = rows.astype(own_rows.dtype)
        shape = (streams,) + (1,) * (own_rows.ndim - 1)
        rows = jnp.where(from_l.reshape(shape), left_row[None], rows)
        return jnp.where(from_r.reshape(shape), right_row[None], rows)

    keys_old = gathered(cache_keys, from_left[0], from_right[0])
    values_old = gathered(cache_values, from_left[1], from_right[1])
    up_prev = gathered(up_state, from_left[2], from_right[2])
    conv_prev = gathered(conv_state, from_left[3], from_right[3])

    latent_f = arrived.astype(jnp.float32)
    prior_f = up_prev.astype(jnp.float32)
    residual_zero = jnp.stack(
        [
            latent_f * up_kernel[0] + prior_f * up_kernel[2],
            latent_f * up_kernel[1] + prior_f * up_kernel[3],
        ],
        axis=1,
    )
    normed_one = layer_norm(residual_zero, norm_gain_one).astype(jnp.bfloat16)
    projections = jnp.einsum(
        "sfd,kde->ksfe", normed_one, qkv_weight, preferred_element_type=jnp.float32
    )
    times = positions[:, None] + jnp.arange(2, dtype=jnp.int32)[None, :]
    queries = rotate(projections[0], times, HEAD_DIM).astype(jnp.bfloat16)
    fresh_keys = rotate(projections[1], times, HEAD_DIM).astype(jnp.bfloat16)
    fresh_values = projections[2].astype(jnp.bfloat16)
    attended = attend(
        queries,
        fresh_keys,
        fresh_values,
        keys_old,
        values_old,
        positions,
        head_share // HEAD_DIM,
        HEAD_DIM,
    )
    partial_heads = jnp.dot(
        attended.reshape(2 * streams, head_share), out_weight, preferred_element_type=jnp.float32
    )
    mixing = section_sum(partial_heads)
    residual_one = residual_zero + scale_attention * mixing.reshape(streams, 2, model_width)
    normed_two = (
        layer_norm(residual_one, norm_gain_two)
        .astype(jnp.bfloat16)
        .reshape(2 * streams, model_width)
    )
    inner_units = jax.nn.gelu(
        jnp.dot(normed_two, in_weight, preferred_element_type=jnp.float32), approximate=False
    ).astype(jnp.bfloat16)
    partial_units = jnp.dot(inner_units, down_weight, preferred_element_type=jnp.float32)
    feed_forward = section_sum(partial_units)
    residual_two = residual_one + scale_feedforward * feed_forward.reshape(streams, 2, model_width)
    excited = jax.nn.elu(residual_two).astype(jnp.bfloat16)
    earlier = jnp.stack([conv_prev, excited[:, 0]], axis=1)
    stride = conv_weight.shape[0] // 2
    audio_out = jnp.einsum(
        "sfi,rci->csfr", excited, conv_weight[:stride], preferred_element_type=jnp.float32
    )
    audio_out = audio_out + jnp.einsum(
        "sfi,rci->csfr", earlier, conv_weight[stride:], preferred_element_type=jnp.float32
    )
    audio_out = audio_out + conv_bias[:, None, None, None]
    audio_out = audio_out.reshape(conv_bias.shape[0], streams * 2 * stride)
    cycle = jnp.arange(window, dtype=jnp.int32)
    hit_first = (cycle[None, :] == jnp.mod(positions, window)[:, None])[..., None]
    hit_second = (cycle[None, :] == jnp.mod(positions + 1, window)[:, None])[..., None]
    new_keys = jnp.where(
        hit_second,
        fresh_keys[:, 1][:, None, :],
        jnp.where(hit_first, fresh_keys[:, 0][:, None, :], keys_old),
    )
    new_values = jnp.where(
        hit_second,
        fresh_values[:, 1][:, None, :],
        jnp.where(hit_first, fresh_values[:, 0][:, None, :], values_old),
    )
    return (audio_out, new_keys, new_values, arrived, excited[:, 1])
def solution(mesh):
    placed = (
        P("batch", None),
        P("batch"),
        P("batch", None, "section"),
        P("batch", None, "section"),
        P("batch", None),
        P("batch", None),
        P("batch"),
        P("batch"),
        P(),
        P(),
        P(None, None, "section"),
        P("section", None),
        P(),
        P(),
        P(None, "section"),
        P("section", None),
        P(),
        P(None, "section", None),
        P("section"),
    )
    return jax.shard_map(
        local,
        mesh=mesh,
        in_specs=placed,
        out_specs=(
            P("section", "batch"),
            P("batch", None, "section"),
            P("batch", None, "section"),
            P("batch", None),
            P("batch", None),
        ),
        check_vma=False,
    )
```

```python
import jax
import jax.numpy as jnp
from jax import lax
from jax.sharding import PartitionSpec as P

HEAD_DIM = 64
CAP = 2
CODE_LANES = 128


EPSILON = 1e-05
MAX_PERIOD = 10000.0


def layer_norm(hidden, weight_gain):
    average = jnp.mean(hidden, axis=-1, keepdims=True)
    centred = hidden - average
    variance = jnp.mean(centred * centred, axis=-1, keepdims=True)
    return centred * lax.rsqrt(variance + EPSILON) * weight_gain


def rotate(features, times, head_width):
    streams = features.shape[0]
    half = head_width // 2
    freqs = MAX_PERIOD ** (-2.0 * jnp.arange(half, dtype=jnp.float32) / head_width)
    angle = times.astype(jnp.float32)[:, :, None] * freqs[None, None, :]
    cosine = jnp.cos(angle)[:, :, None, :]
    sine = jnp.sin(angle)[:, :, None, :]
    paired = features.reshape(streams, 2, -1, half, 2)
    first = paired[..., 0]
    second = paired[..., 1]
    turned = jnp.stack([first * cosine - second * sine, first * sine + second * cosine], axis=-1)
    return turned.reshape(features.shape)


def attend(queries, fresh_keys, fresh_values, old_keys, old_values, starts, local_heads, head_width):
    streams, window, share = old_keys.shape
    head_of = jnp.arange(share, dtype=jnp.int32) // head_width
    head_ids = jnp.arange(local_heads, dtype=jnp.int32)
    in_head = head_of[None, :] == head_ids[:, None]
    lanes = in_head[None, :, None, :]
    masked = jnp.where(lanes, queries[:, None], jnp.zeros((), queries.dtype))
    masked = masked.reshape(streams, local_heads * 2, share)
    score_scale = head_width ** (-0.5)
    cache_scores = (
        jnp.einsum("sxd,swd->sxw", masked, old_keys, preferred_element_type=jnp.float32)
        * score_scale
    )
    fresh_scores = (
        jnp.einsum("sxd,sgd->sxg", masked, fresh_keys, preferred_element_type=jnp.float32)
        * score_scale
    )
    cycle_slots = jnp.arange(window, dtype=jnp.int32)
    held_time = starts[:, None] - window + jnp.mod(cycle_slots[None, :] - starts[:, None], window)
    query_times = starts[:, None] + jnp.arange(2, dtype=jnp.int32)[None, :]
    cache_ok = (held_time[:, None, :] >= 0) & (
        held_time[:, None, :] > query_times[:, :, None] - window
    )
    cache_ok = jnp.broadcast_to(cache_ok[:, None], (streams, local_heads, 2, window)).reshape(
        streams, local_heads * 2, window
    )
    frame_ids = jnp.arange(2, dtype=jnp.int32)
    fresh_ok = jnp.tile(frame_ids[None, :] <= frame_ids[:, None], (local_heads, 1))[None]
    cache_scores = jnp.where(cache_ok, cache_scores, -jnp.inf)
    fresh_scores = jnp.where(fresh_ok, fresh_scores, -jnp.inf)
    score_max = jnp.maximum(
        jnp.max(cache_scores, axis=-1, keepdims=True), jnp.max(fresh_scores, axis=-1, keepdims=True)
    )
    cache_weights = jnp.where(cache_ok, jnp.exp(cache_scores - score_max), 0.0)
    fresh_weights = jnp.where(fresh_ok, jnp.exp(fresh_scores - score_max), 0.0)
    denominator = jnp.sum(cache_weights, axis=-1, keepdims=True) + jnp.sum(
        fresh_weights, axis=-1, keepdims=True
    )
    spread = jnp.einsum(
        "sxw,swd->sxd",
        cache_weights.astype(jnp.bfloat16),
        old_values,
        preferred_element_type=jnp.float32,
    )
    spread = spread + jnp.einsum(
        "sxg,sgd->sxd",
        fresh_weights.astype(jnp.bfloat16),
        fresh_values,
        preferred_element_type=jnp.float32,
    )
    spread = (spread / denominator).reshape(streams, local_heads, 2, share)
    attended = jnp.sum(jnp.where(lanes, spread, 0.0), axis=1)
    return attended.astype(jnp.bfloat16)


def section_sum(partial):
    size = lax.axis_size("section")
    rounded = partial.astype(jnp.bfloat16)
    copies = jnp.broadcast_to(rounded[None], (size,) + rounded.shape)
    every = lax.all_to_all(copies, "section", 0, 0, tiled=False).astype(jnp.float32)
    terms = [every[i] for i in range(size)]
    while len(terms) > 1:
        paired = [terms[i] + terms[i + 1] for i in range(0, len(terms) - 1, 2)]
        terms = paired + ([terms[-1]] if len(terms) % 2 else [])
    return terms[0]


def one_hot(rows, columns):
    return (rows[:, None] == columns[None, :]).astype(jnp.bfloat16)


def local(
    latents,
    token_slot,
    cache_keys,
    cache_values,
    up_state,
    conv_state,
    cache_slot,
    positions,
    up_kernel,
    norm_gain_one,
    qkv_weight,
    out_weight,
    scale_attention,
    norm_gain_two,
    in_weight,
    down_weight,
    scale_feedforward,
    conv_weight,
    conv_bias,
):
    owners = lax.axis_size("batch")
    own_index = lax.axis_index("batch")
    streams = latents.shape[0]
    model_width = latents.shape[1]
    window = cache_keys.shape[1]
    head_share = cache_keys.shape[2]
    capacity = max(CAP, streams // owners)
    slot_ids = jnp.arange(streams, dtype=jnp.int32)

    dest_owner = cache_slot // streams
    dest_local = cache_slot % streams
    right_owner = jnp.mod(own_index + 1, owners)
    left_owner = jnp.mod(own_index + owners - 1, owners)
    state_rows = model_width // head_share

    def pack(direction_owner):
        chosen = dest_owner == direction_owner
        code = jnp.sum(jnp.where(chosen, dest_local + 1, 0))

        def pick(rows):
            shape = (streams,) + (1,) * (rows.ndim - 1)
            return jnp.sum(jnp.where(chosen.reshape(shape), rows, jnp.zeros((), rows.dtype)), axis=0)

        pieces = [
            pick(cache_keys),
            pick(cache_values),
            pick(up_state).reshape(state_rows, head_share),
            pick(conv_state).reshape(state_rows, head_share),
            jnp.full((8, head_share), code, jnp.int32).astype(jnp.bfloat16),
        ]
        return jnp.concatenate(pieces, axis=0)

    def unpack(box):
        keys = box[:window]
        values = box[window : 2 * window]
        up = box[2 * window : 2 * window + state_rows].reshape(model_width)
        conv = box[2 * window + state_rows : 2 * window + 2 * state_rows].reshape(model_width)
        code = box[2 * window + 2 * state_rows, 0].astype(jnp.int32) - 1
        return keys, values, up, conv, code

    from_left = unpack(
        lax.ppermute(pack(right_owner), "batch", [(i, (i + 1) % owners) for i in range(owners)])
    )
    from_right = unpack(
        lax.ppermute(pack(left_owner), "batch", [(i, (i - 1) % owners) for i in range(owners)])
    )

    target = token_slot // streams
    landing = token_slot % streams
    same_before = (target[None, :] == target[:, None]) & (slot_ids[None, :] < slot_ids[:, None])
    arrival_rank = jnp.sum(same_before.astype(jnp.int32), axis=1)
    box_ids = target * capacity + arrival_rank
    placing = one_hot(jnp.arange(owners * capacity, dtype=jnp.int32), box_ids)
    send_rows = jnp.dot(placing, latents, preferred_element_type=jnp.float32).astype(jnp.bfloat16)
    send_codes = jnp.dot(
        placing,
        jnp.broadcast_to((landing + 1).astype(jnp.bfloat16)[:, None], (streams, CODE_LANES)),
        preferred_element_type=jnp.float32,
    ).astype(jnp.bfloat16)
    code_block = send_codes.reshape(owners, capacity, CODE_LANES)[:, :, 0]
    code_block = jnp.pad(code_block, ((0, 0), (0, CODE_LANES - capacity)))
    send = jnp.concatenate(
        [send_rows.reshape(owners, capacity * model_width), code_block], axis=1
    )
    got = lax.all_to_all(send, "batch", split_axis=0, concat_axis=0, tiled=True)
    got_codes = got[:, capacity * model_width : capacity * model_width + capacity]
    got_codes = got_codes.reshape(owners * capacity).astype(jnp.int32) - 1
    got_rows = got[:, : capacity * model_width].reshape(owners * capacity, model_width)
    arrived = jnp.dot(
        one_hot(slot_ids, got_codes), got_rows, preferred_element_type=jnp.float32
    ).astype(jnp.bfloat16)

    staying = dest_owner == own_index
    source_of = (dest_local[None, :] == slot_ids[:, None]) & staying[None, :]
    picking = source_of.astype(jnp.bfloat16)
    from_l = slot_ids == from_left[4]
    from_r = slot_ids == from_right[4]

    def gathered(own_rows, left_row, right_row):
        rows = jnp.tensordot(picking, own_rows, axes=1, preferred_element_type=jnp.float32)
        rows = rows.astype(own_rows.dtype)
        shape = (streams,) + (1,) * (own_rows.ndim - 1)
        rows = jnp.where(from_l.reshape(shape), left_row[None], rows)
        return jnp.where(from_r.reshape(shape), right_row[None], rows)

    keys_old = gathered(cache_keys, from_left[0], from_right[0])
    values_old = gathered(cache_values, from_left[1], from_right[1])
    up_prev = gathered(up_state, from_left[2], from_right[2])
    conv_prev = gathered(conv_state, from_left[3], from_right[3])

    latent_f = arrived.astype(jnp.float32)
    prior_f = up_prev.astype(jnp.float32)
    residual_zero = jnp.stack(
        [
            latent_f * up_kernel[0] + prior_f * up_kernel[2],
            latent_f * up_kernel[1] + prior_f * up_kernel[3],
        ],
        axis=1,
    )
    normed_one = layer_norm(residual_zero, norm_gain_one).astype(jnp.bfloat16)
    projections = jnp.einsum(
        "sfd,kde->ksfe", normed_one, qkv_weight, preferred_element_type=jnp.float32
    )
    times = positions[:, None] + jnp.arange(2, dtype=jnp.int32)[None, :]
    queries = rotate(projections[0], times, HEAD_DIM).astype(jnp.bfloat16)
    fresh_keys = rotate(projections[1], times, HEAD_DIM).astype(jnp.bfloat16)
    fresh_values = projections[2].astype(jnp.bfloat16)
    attended = attend(
        queries,
        fresh_keys,
        fresh_values,
        keys_old,
        values_old,
        positions,
        head_share // HEAD_DIM,
        HEAD_DIM,
    )
    partial_heads = jnp.dot(
        attended.reshape(2 * streams, head_share), out_weight, preferred_element_type=jnp.float32
    )
    mixing = section_sum(partial_heads)
    residual_one = residual_zero + scale_attention * mixing.reshape(streams, 2, model_width)
    normed_two = (
        layer_norm(residual_one, norm_gain_two)
        .astype(jnp.bfloat16)
        .reshape(2 * streams, model_width)
    )
    inner_units = jax.nn.gelu(
        jnp.dot(normed_two, in_weight, preferred_element_type=jnp.float32), approximate=False
    ).astype(jnp.bfloat16)
    partial_units = jnp.dot(inner_units, down_weight, preferred_element_type=jnp.float32)
    feed_forward = section_sum(partial_units)
    residual_two = residual_one + scale_feedforward * feed_forward.reshape(streams, 2, model_width)
    excited = jax.nn.elu(residual_two).astype(jnp.bfloat16)
    earlier = jnp.stack([conv_prev, excited[:, 0]], axis=1)
    stride = conv_weight.shape[0] // 2
    audio_out = jnp.einsum(
        "sfi,rci->csfr", excited, conv_weight[:stride], preferred_element_type=jnp.float32
    )
    audio_out = audio_out + jnp.einsum(
        "sfi,rci->csfr", earlier, conv_weight[stride:], preferred_element_type=jnp.float32
    )
    audio_out = audio_out + conv_bias[:, None, None, None]
    audio_out = audio_out.reshape(conv_bias.shape[0], streams * 2 * stride)
    cycle = jnp.arange(window, dtype=jnp.int32)
    hit_first = (cycle[None, :] == jnp.mod(positions, window)[:, None])[..., None]
    hit_second = (cycle[None, :] == jnp.mod(positions + 1, window)[:, None])[..., None]
    new_keys = jnp.where(
        hit_second,
        fresh_keys[:, 1][:, None, :],
        jnp.where(hit_first, fresh_keys[:, 0][:, None, :], keys_old),
    )
    new_values = jnp.where(
        hit_second,
        fresh_values[:, 1][:, None, :],
        jnp.where(hit_first, fresh_values[:, 0][:, None, :], values_old),
    )
    return (audio_out, new_keys, new_values, arrived, excited[:, 1])
def solution(mesh):
    placed = (
        P("batch", None),
        P("batch"),
        P("batch", None, "section"),
        P("batch", None, "section"),
        P("batch", None),
        P("batch", None),
        P("batch"),
        P("batch"),
        P(),
        P(),
        P(None, None, "section"),
        P("section", None),
        P(),
        P(),
        P(None, "section"),
        P("section", None),
        P(),
        P(None, "section", None),
        P("section"),
    )
    return jax.shard_map(
        local,
        mesh=mesh,
        in_specs=placed,
        out_specs=(
            P("section", "batch"),
            P("batch", None, "section"),
            P("batch", None, "section"),
            P("batch", None),
            P("batch", None),
        ),
        check_vma=False,
    )
```

```python
import jax
import jax.numpy as jnp
from jax import lax
from jax.sharding import PartitionSpec as P
from jax.experimental import pallas as pl
from jax.experimental.pallas import tpu as pltpu

HEAD_DIM = 64
CAP = 2
CODE_LANES = 128


EPSILON = 1e-05
MAX_PERIOD = 10000.0


def layer_norm(hidden, weight_gain):
    average = jnp.mean(hidden, axis=-1, keepdims=True)
    centred = hidden - average
    variance = jnp.mean(centred * centred, axis=-1, keepdims=True)
    return centred * lax.rsqrt(variance + EPSILON) * weight_gain


def rotate(features, times, head_width):
    streams = features.shape[0]
    half = head_width // 2
    freqs = MAX_PERIOD ** (-2.0 * jnp.arange(half, dtype=jnp.float32) / head_width)
    angle = times.astype(jnp.float32)[:, :, None] * freqs[None, None, :]
    cosine = jnp.cos(angle)[:, :, None, :]
    sine = jnp.sin(angle)[:, :, None, :]
    paired = features.reshape(streams, 2, -1, half, 2)
    first = paired[..., 0]
    second = paired[..., 1]
    turned = jnp.stack([first * cosine - second * sine, first * sine + second * cosine], axis=-1)
    return turned.reshape(features.shape)


def attend(queries, fresh_keys, fresh_values, old_keys, old_values, starts, local_heads, head_width):
    streams, window, share = old_keys.shape
    head_of = jnp.arange(share, dtype=jnp.int32) // head_width
    head_ids = jnp.arange(local_heads, dtype=jnp.int32)
    in_head = head_of[None, :] == head_ids[:, None]
    lanes = in_head[None, :, None, :]
    masked = jnp.where(lanes, queries[:, None], jnp.zeros((), queries.dtype))
    masked = masked.reshape(streams, local_heads * 2, share)
    score_scale = head_width ** (-0.5)
    cache_scores = (
        jnp.einsum("sxd,swd->sxw", masked, old_keys, preferred_element_type=jnp.float32)
        * score_scale
    )
    fresh_scores = (
        jnp.einsum("sxd,sgd->sxg", masked, fresh_keys, preferred_element_type=jnp.float32)
        * score_scale
    )
    cycle_slots = jnp.arange(window, dtype=jnp.int32)
    held_time = starts[:, None] - window + jnp.mod(cycle_slots[None, :] - starts[:, None], window)
    query_times = starts[:, None] + jnp.arange(2, dtype=jnp.int32)[None, :]
    cache_ok = (held_time[:, None, :] >= 0) & (
        held_time[:, None, :] > query_times[:, :, None] - window
    )
    cache_ok = jnp.broadcast_to(cache_ok[:, None], (streams, local_heads, 2, window)).reshape(
        streams, local_heads * 2, window
    )
    frame_ids = jnp.arange(2, dtype=jnp.int32)
    fresh_ok = jnp.tile(frame_ids[None, :] <= frame_ids[:, None], (local_heads, 1))[None]
    cache_scores = jnp.where(cache_ok, cache_scores, -jnp.inf)
    fresh_scores = jnp.where(fresh_ok, fresh_scores, -jnp.inf)
    score_max = jnp.maximum(
        jnp.max(cache_scores, axis=-1, keepdims=True), jnp.max(fresh_scores, axis=-1, keepdims=True)
    )
    cache_weights = jnp.where(cache_ok, jnp.exp(cache_scores - score_max), 0.0)
    fresh_weights = jnp.where(fresh_ok, jnp.exp(fresh_scores - score_max), 0.0)
    denominator = jnp.sum(cache_weights, axis=-1, keepdims=True) + jnp.sum(
        fresh_weights, axis=-1, keepdims=True
    )
    spread = jnp.einsum(
        "sxw,swd->sxd",
        cache_weights.astype(jnp.bfloat16),
        old_values,
        preferred_element_type=jnp.float32,
    )
    spread = spread + jnp.einsum(
        "sxg,sgd->sxd",
        fresh_weights.astype(jnp.bfloat16),
        fresh_values,
        preferred_element_type=jnp.float32,
    )
    spread = (spread / denominator).reshape(streams, local_heads, 2, share)
    attended = jnp.sum(jnp.where(lanes, spread, 0.0), axis=1)
    return attended.astype(jnp.bfloat16)


def section_sum(partial):
    size = lax.axis_size("section")
    if size & (size - 1):
        return lax.psum(partial.astype(jnp.bfloat16), "section").astype(jnp.float32)
    total = partial.astype(jnp.bfloat16)
    bit = size // 2
    while bit >= 1:
        route = [(i, i ^ bit) for i in range(size)]
        other = lax.ppermute(total, "section", route)
        total = total.astype(jnp.float32) + other.astype(jnp.float32)
        bit //= 2
    return total


def cache_kernel(src_ref, take_ref, keys_ref, values_ref, lbox_ref, rbox_ref, ok_ref, ov_ref):
    streams, window, _ = keys_ref.shape

    def body(n, carry):
        src = src_ref[n]
        take = take_ref[n]
        ok_ref[n] = keys_ref[src]
        ov_ref[n] = values_ref[src]

        @pl.when(take == 1)
        def _():
            ok_ref[n] = lbox_ref[0:window]
            ov_ref[n] = lbox_ref[window : 2 * window]

        @pl.when(take == 2)
        def _():
            ok_ref[n] = rbox_ref[0:window]
            ov_ref[n] = rbox_ref[window : 2 * window]

        return carry

    lax.fori_loop(0, streams, body, 0)


def route_caches(src, take, keys, values, lbox, rbox):
    smem = pl.BlockSpec(memory_space=pltpu.SMEM)
    vmem = pl.BlockSpec(memory_space=pltpu.VMEM)
    shape = jax.ShapeDtypeStruct(keys.shape, keys.dtype)
    moved = 4 * keys.size * keys.dtype.itemsize
    return pl.pallas_call(
        cache_kernel,
        out_shape=(shape, shape),
        in_specs=[smem] * 2 + [vmem] * 4,
        out_specs=(vmem, vmem),
        cost_estimate=pl.CostEstimate(flops=0, transcendentals=0, bytes_accessed=moved),
    )(src, take, keys, values, lbox, rbox)


def one_hot(rows, columns):
    return (rows[:, None] == columns[None, :]).astype(jnp.bfloat16)


def local(
    latents,
    token_slot,
    cache_keys,
    cache_values,
    up_state,
    conv_state,
    cache_slot,
    positions,
    up_kernel,
    norm_gain_one,
    qkv_weight,
    out_weight,
    scale_attention,
    norm_gain_two,
    in_weight,
    down_weight,
    scale_feedforward,
    conv_weight,
    conv_bias,
):
    owners = lax.axis_size("batch")
    own_index = lax.axis_index("batch")
    streams = latents.shape[0]
    model_width = latents.shape[1]
    window = cache_keys.shape[1]
    head_share = cache_keys.shape[2]
    capacity = max(CAP, streams // owners)
    slot_ids = jnp.arange(streams, dtype=jnp.int32)

    dest_owner = cache_slot // streams
    dest_local = cache_slot % streams
    right_owner = jnp.mod(own_index + 1, owners)
    left_owner = jnp.mod(own_index + owners - 1, owners)
    state_rows = model_width // head_share

    def pack(direction_owner):
        chosen = dest_owner == direction_owner
        code = jnp.sum(jnp.where(chosen, dest_local + 1, 0))

        def pick(rows):
            shape = (streams,) + (1,) * (rows.ndim - 1)
            return jnp.sum(jnp.where(chosen.reshape(shape), rows, jnp.zeros((), rows.dtype)), axis=0)

        pieces = [
            pick(cache_keys),
            pick(cache_values),
            pick(up_state).reshape(state_rows, head_share),
            pick(conv_state).reshape(state_rows, head_share),
            jnp.full((8, head_share), code, jnp.int32).astype(jnp.bfloat16),
        ]
        return jnp.concatenate(pieces, axis=0)

    def unpack(box):
        keys = box[:window]
        values = box[window : 2 * window]
        up = box[2 * window : 2 * window + state_rows].reshape(model_width)
        conv = box[2 * window + state_rows : 2 * window + 2 * state_rows].reshape(model_width)
        code = box[2 * window + 2 * state_rows, 0].astype(jnp.int32) - 1
        return keys, values, up, conv, code

    left_box = lax.ppermute(
        pack(right_owner), "batch", [(i, (i + 1) % owners) for i in range(owners)]
    )
    right_box = lax.ppermute(
        pack(left_owner), "batch", [(i, (i - 1) % owners) for i in range(owners)]
    )
    from_left = unpack(left_box)
    from_right = unpack(right_box)

    target = token_slot // streams
    landing = token_slot % streams
    same_before = (target[None, :] == target[:, None]) & (slot_ids[None, :] < slot_ids[:, None])
    arrival_rank = jnp.sum(same_before.astype(jnp.int32), axis=1)
    box_ids = target * capacity + arrival_rank
    placing = one_hot(jnp.arange(owners * capacity, dtype=jnp.int32), box_ids)
    send_rows = jnp.dot(placing, latents, preferred_element_type=jnp.float32).astype(jnp.bfloat16)
    send_codes = jnp.dot(
        placing,
        jnp.broadcast_to((landing + 1).astype(jnp.bfloat16)[:, None], (streams, CODE_LANES)),
        preferred_element_type=jnp.float32,
    ).astype(jnp.bfloat16)
    code_block = send_codes.reshape(owners, capacity, CODE_LANES)[:, :, 0]
    code_block = jnp.pad(code_block, ((0, 0), (0, CODE_LANES - capacity)))
    send = jnp.concatenate(
        [send_rows.reshape(owners, capacity * model_width), code_block], axis=1
    )
    got = lax.all_to_all(send, "batch", split_axis=0, concat_axis=0, tiled=True)
    got_codes = got[:, capacity * model_width : capacity * model_width + capacity]
    got_codes = got_codes.reshape(owners * capacity).astype(jnp.int32) - 1
    got_rows = got[:, : capacity * model_width].reshape(owners * capacity, model_width)
    arrived = jnp.dot(
        one_hot(slot_ids, got_codes), got_rows, preferred_element_type=jnp.float32
    ).astype(jnp.bfloat16)

    staying = dest_owner == own_index
    source_of = (dest_local[None, :] == slot_ids[:, None]) & staying[None, :]
    source = jnp.sum(jnp.where(source_of, slot_ids[None, :], 0), axis=1)
    from_l = slot_ids == from_left[4]
    from_r = slot_ids == from_right[4]
    take = jnp.where(from_l, 1, jnp.where(from_r, 2, 0)).astype(jnp.int32)
    keys_old, values_old = route_caches(
        source, take, cache_keys, cache_values, left_box, right_box
    )
    picking = source_of.astype(jnp.bfloat16)

    def gathered(own_rows, left_row, right_row):
        rows = jnp.dot(picking, own_rows, preferred_element_type=jnp.float32)
        rows = rows.astype(own_rows.dtype)
        rows = jnp.where(from_l[:, None], left_row[None], rows)
        return jnp.where(from_r[:, None], right_row[None], rows)

    up_prev = gathered(up_state, from_left[2], from_right[2])
    conv_prev = gathered(conv_state, from_left[3], from_right[3])

    latent_f = arrived.astype(jnp.float32)
    prior_f = up_prev.astype(jnp.float32)
    residual_zero = jnp.stack(
        [
            latent_f * up_kernel[0] + prior_f * up_kernel[2],
            latent_f * up_kernel[1] + prior_f * up_kernel[3],
        ],
        axis=1,
    )
    normed_one = layer_norm(residual_zero, norm_gain_one).astype(jnp.bfloat16)
    projections = jnp.einsum(
        "sfd,kde->ksfe", normed_one, qkv_weight, preferred_element_type=jnp.float32
    )
    times = positions[:, None] + jnp.arange(2, dtype=jnp.int32)[None, :]
    queries = rotate(projections[0], times, HEAD_DIM).astype(jnp.bfloat16)
    fresh_keys = rotate(projections[1], times, HEAD_DIM).astype(jnp.bfloat16)
    fresh_values = projections[2].astype(jnp.bfloat16)
    attended = attend(
        queries,
        fresh_keys,
        fresh_values,
        keys_old,
        values_old,
        positions,
        head_share // HEAD_DIM,
        HEAD_DIM,
    )
    partial_heads = jnp.dot(
        attended.reshape(2 * streams, head_share), out_weight, preferred_element_type=jnp.float32
    )
    mixing = section_sum(partial_heads)
    residual_one = residual_zero + scale_attention * mixing.reshape(streams, 2, model_width)
    normed_two = (
        layer_norm(residual_one, norm_gain_two)
        .astype(jnp.bfloat16)
        .reshape(2 * streams, model_width)
    )
    inner_units = jax.nn.gelu(
        jnp.dot(normed_two, in_weight, preferred_element_type=jnp.float32), approximate=False
    ).astype(jnp.bfloat16)
    partial_units = jnp.dot(inner_units, down_weight, preferred_element_type=jnp.float32)
    feed_forward = section_sum(partial_units)
    residual_two = residual_one + scale_feedforward * feed_forward.reshape(streams, 2, model_width)
    excited = jax.nn.elu(residual_two).astype(jnp.bfloat16)
    earlier = jnp.stack([conv_prev, excited[:, 0]], axis=1)
    stride = conv_weight.shape[0] // 2
    audio_out = jnp.einsum(
        "sfi,rci->csfr", excited, conv_weight[:stride], preferred_element_type=jnp.float32
    )
    audio_out = audio_out + jnp.einsum(
        "sfi,rci->csfr", earlier, conv_weight[stride:], preferred_element_type=jnp.float32
    )
    audio_out = audio_out + conv_bias[:, None, None, None]
    audio_out = audio_out.reshape(conv_bias.shape[0], streams * 2 * stride)
    cycle = jnp.arange(window, dtype=jnp.int32)
    hit_first = (cycle[None, :] == jnp.mod(positions, window)[:, None])[..., None]
    hit_second = (cycle[None, :] == jnp.mod(positions + 1, window)[:, None])[..., None]
    new_keys = jnp.where(
        hit_second,
        fresh_keys[:, 1][:, None, :],
        jnp.where(hit_first, fresh_keys[:, 0][:, None, :], keys_old),
    )
    new_values = jnp.where(
        hit_second,
        fresh_values[:, 1][:, None, :],
        jnp.where(hit_first, fresh_values[:, 0][:, None, :], values_old),
    )
    return (audio_out, new_keys, new_values, arrived, excited[:, 1])
def solution(mesh):
    placed = (
        P("batch", None),
        P("batch"),
        P("batch", None, "section"),
        P("batch", None, "section"),
        P("batch", None),
        P("batch", None),
        P("batch"),
        P("batch"),
        P(),
        P(),
        P(None, None, "section"),
        P("section", None),
        P(),
        P(),
        P(None, "section"),
        P("section", None),
        P(),
        P(None, "section", None),
        P("section"),
    )
    return jax.shard_map(
        local,
        mesh=mesh,
        in_specs=placed,
        out_specs=(
            P("section", "batch"),
            P("batch", None, "section"),
            P("batch", None, "section"),
            P("batch", None),
            P("batch", None),
        ),
        check_vma=False,
    )
```

```python
import jax
import jax.numpy as jnp
from jax import lax
from jax.sharding import PartitionSpec as P
from jax.experimental import pallas as pl
from jax.experimental.pallas import tpu as pltpu

HEAD_DIM = 64
CAP = 2
CODE_LANES = 128


EPSILON = 1e-05
MAX_PERIOD = 10000.0


def layer_norm(hidden, weight_gain):
    average = jnp.mean(hidden, axis=-1, keepdims=True)
    centred = hidden - average
    variance = jnp.mean(centred * centred, axis=-1, keepdims=True)
    return centred * lax.rsqrt(variance + EPSILON) * weight_gain


def rotate(features, times, head_width):
    streams = features.shape[0]
    half = head_width // 2
    freqs = MAX_PERIOD ** (-2.0 * jnp.arange(half, dtype=jnp.float32) / head_width)
    angle = times.astype(jnp.float32)[:, :, None] * freqs[None, None, :]
    cosine = jnp.cos(angle)[:, :, None, :]
    sine = jnp.sin(angle)[:, :, None, :]
    paired = features.reshape(streams, 2, -1, half, 2)
    first = paired[..., 0]
    second = paired[..., 1]
    turned = jnp.stack([first * cosine - second * sine, first * sine + second * cosine], axis=-1)
    return turned.reshape(features.shape)


def attend(queries, fresh_keys, fresh_values, old_keys, old_values, starts, local_heads, head_width):
    streams, window, share = old_keys.shape
    head_of = jnp.arange(share, dtype=jnp.int32) // head_width
    head_ids = jnp.arange(local_heads, dtype=jnp.int32)
    in_head = head_of[None, :] == head_ids[:, None]
    lanes = in_head[None, :, None, :]
    masked = jnp.where(lanes, queries[:, None], jnp.zeros((), queries.dtype))
    masked = masked.reshape(streams, local_heads * 2, share)
    score_scale = head_width ** (-0.5)
    cache_scores = (
        jnp.einsum("sxd,swd->sxw", masked, old_keys, preferred_element_type=jnp.float32)
        * score_scale
    )
    fresh_scores = (
        jnp.einsum("sxd,sgd->sxg", masked, fresh_keys, preferred_element_type=jnp.float32)
        * score_scale
    )
    cycle_slots = jnp.arange(window, dtype=jnp.int32)
    held_time = starts[:, None] - window + jnp.mod(cycle_slots[None, :] - starts[:, None], window)
    query_times = starts[:, None] + jnp.arange(2, dtype=jnp.int32)[None, :]
    cache_ok = (held_time[:, None, :] >= 0) & (
        held_time[:, None, :] > query_times[:, :, None] - window
    )
    cache_ok = jnp.broadcast_to(cache_ok[:, None], (streams, local_heads, 2, window)).reshape(
        streams, local_heads * 2, window
    )
    frame_ids = jnp.arange(2, dtype=jnp.int32)
    fresh_ok = jnp.tile(frame_ids[None, :] <= frame_ids[:, None], (local_heads, 1))[None]
    cache_scores = jnp.where(cache_ok, cache_scores, -jnp.inf)
    fresh_scores = jnp.where(fresh_ok, fresh_scores, -jnp.inf)
    score_max = jnp.maximum(
        jnp.max(cache_scores, axis=-1, keepdims=True), jnp.max(fresh_scores, axis=-1, keepdims=True)
    )
    cache_weights = jnp.where(cache_ok, jnp.exp(cache_scores - score_max), 0.0)
    fresh_weights = jnp.where(fresh_ok, jnp.exp(fresh_scores - score_max), 0.0)
    denominator = jnp.sum(cache_weights, axis=-1, keepdims=True) + jnp.sum(
        fresh_weights, axis=-1, keepdims=True
    )
    spread = jnp.einsum(
        "sxw,swd->sxd",
        cache_weights.astype(jnp.bfloat16),
        old_values,
        preferred_element_type=jnp.float32,
    )
    spread = spread + jnp.einsum(
        "sxg,sgd->sxd",
        fresh_weights.astype(jnp.bfloat16),
        fresh_values,
        preferred_element_type=jnp.float32,
    )
    spread = (spread / denominator).reshape(streams, local_heads, 2, share)
    attended = jnp.sum(jnp.where(lanes, spread, 0.0), axis=1)
    return attended.astype(jnp.bfloat16)


def section_sum(partial):
    size = lax.axis_size("section")
    if size & (size - 1):
        return lax.psum(partial.astype(jnp.bfloat16), "section").astype(jnp.float32)
    total = partial.astype(jnp.bfloat16)
    bit = size // 2
    while bit >= 1:
        route = [(i, i ^ bit) for i in range(size)]
        other = lax.ppermute(total, "section", route)
        total = total.astype(jnp.float32) + other.astype(jnp.float32)
        bit //= 2
    return total


def cache_kernel(src_ref, take_ref, keys_ref, values_ref, lbox_ref, rbox_ref, ok_ref, ov_ref):
    streams, window, _ = keys_ref.shape

    def body(n, carry):
        src = src_ref[n]
        take = take_ref[n]
        ok_ref[n] = keys_ref[src]
        ov_ref[n] = values_ref[src]

        @pl.when(take == 1)
        def _():
            ok_ref[n] = lbox_ref[0:window]
            ov_ref[n] = lbox_ref[window : 2 * window]

        @pl.when(take == 2)
        def _():
            ok_ref[n] = rbox_ref[0:window]
            ov_ref[n] = rbox_ref[window : 2 * window]

        return carry

    lax.fori_loop(0, streams, body, 0)


def route_caches(src, take, keys, values, lbox, rbox):
    smem = pl.BlockSpec(memory_space=pltpu.SMEM)
    vmem = pl.BlockSpec(memory_space=pltpu.VMEM)
    shape = jax.ShapeDtypeStruct(keys.shape, keys.dtype)
    moved = 4 * keys.size * keys.dtype.itemsize
    return pl.pallas_call(
        cache_kernel,
        out_shape=(shape, shape),
        in_specs=[smem] * 2 + [vmem] * 4,
        out_specs=(vmem, vmem),
        cost_estimate=pl.CostEstimate(flops=0, transcendentals=0, bytes_accessed=moved),
    )(src, take, keys, values, lbox, rbox)


def one_hot(rows, columns):
    return (rows[:, None] == columns[None, :]).astype(jnp.bfloat16)


def local(
    latents,
    token_slot,
    cache_keys,
    cache_values,
    up_state,
    conv_state,
    cache_slot,
    positions,
    up_kernel,
    norm_gain_one,
    qkv_weight,
    out_weight,
    scale_attention,
    norm_gain_two,
    in_weight,
    down_weight,
    scale_feedforward,
    conv_weight,
    conv_bias,
):
    owners = lax.axis_size("batch")
    own_index = lax.axis_index("batch")
    streams = latents.shape[0]
    model_width = latents.shape[1]
    window = cache_keys.shape[1]
    head_share = cache_keys.shape[2]
    capacity = max(CAP, streams // owners)
    slot_ids = jnp.arange(streams, dtype=jnp.int32)

    dest_owner = cache_slot // streams
    dest_local = cache_slot % streams
    right_owner = jnp.mod(own_index + 1, owners)
    left_owner = jnp.mod(own_index + owners - 1, owners)
    state_rows = model_width // head_share

    def pack(direction_owner):
        chosen = dest_owner == direction_owner
        code = jnp.sum(jnp.where(chosen, dest_local + 1, 0))

        def pick(rows):
            shape = (streams,) + (1,) * (rows.ndim - 1)
            return jnp.sum(jnp.where(chosen.reshape(shape), rows, jnp.zeros((), rows.dtype)), axis=0)

        pieces = [
            pick(cache_keys),
            pick(cache_values),
            pick(up_state).reshape(state_rows, head_share),
            pick(conv_state).reshape(state_rows, head_share),
            jnp.full((8, head_share), code, jnp.int32).astype(jnp.bfloat16),
        ]
        return jnp.concatenate(pieces, axis=0)

    def unpack(box):
        keys = box[:window]
        values = box[window : 2 * window]
        up = box[2 * window : 2 * window + state_rows].reshape(model_width)
        conv = box[2 * window + state_rows : 2 * window + 2 * state_rows].reshape(model_width)
        code = box[2 * window + 2 * state_rows, 0].astype(jnp.int32) - 1
        return keys, values, up, conv, code

    left_box = lax.ppermute(
        pack(right_owner), "batch", [(i, (i + 1) % owners) for i in range(owners)]
    )
    right_box = lax.ppermute(
        pack(left_owner), "batch", [(i, (i - 1) % owners) for i in range(owners)]
    )
    from_left = unpack(left_box)
    from_right = unpack(right_box)

    target = token_slot // streams
    landing = token_slot % streams
    same_before = (target[None, :] == target[:, None]) & (slot_ids[None, :] < slot_ids[:, None])
    arrival_rank = jnp.sum(same_before.astype(jnp.int32), axis=1)
    owner_ids = jnp.arange(owners, dtype=jnp.int32)
    lane_ids = jnp.arange(CODE_LANES, dtype=jnp.int32)
    blocks = []
    code_block = jnp.zeros((owners, CODE_LANES), jnp.int32)
    for rank in range(capacity):
        chosen = (owner_ids[:, None] == target[None, :]) & (arrival_rank == rank)[None, :]
        blocks.append(
            jnp.dot(chosen.astype(jnp.bfloat16), latents, preferred_element_type=jnp.float32)
        )
        code = jnp.sum(jnp.where(chosen, landing[None, :] + 1, 0), axis=1)
        code_block = jnp.where(lane_ids[None, :] == rank, code[:, None], code_block)
    blocks.append(code_block.astype(jnp.float32))
    send = jnp.concatenate(blocks, axis=1).astype(jnp.bfloat16)
    got = lax.all_to_all(send, "batch", split_axis=0, concat_axis=0, tiled=True)
    arrived = jnp.zeros((streams, model_width), jnp.float32)
    for rank in range(capacity):
        got_code = got[:, capacity * model_width + rank].astype(jnp.int32) - 1
        arrived = arrived + jnp.dot(
            one_hot(slot_ids, got_code),
            got[:, rank * model_width : (rank + 1) * model_width],
            preferred_element_type=jnp.float32,
        )
    arrived = arrived.astype(jnp.bfloat16)

    staying = dest_owner == own_index
    source_of = (dest_local[None, :] == slot_ids[:, None]) & staying[None, :]
    source = jnp.sum(jnp.where(source_of, slot_ids[None, :], 0), axis=1)
    from_l = slot_ids == from_left[4]
    from_r = slot_ids == from_right[4]
    take = jnp.where(from_l, 1, jnp.where(from_r, 2, 0)).astype(jnp.int32)
    keys_old, values_old = route_caches(
        source, take, cache_keys, cache_values, left_box, right_box
    )
    picking = source_of.astype(jnp.bfloat16)

    def gathered(own_rows, left_row, right_row):
        rows = jnp.dot(picking, own_rows, preferred_element_type=jnp.float32)
        rows = rows.astype(own_rows.dtype)
        rows = jnp.where(from_l[:, None], left_row[None], rows)
        return jnp.where(from_r[:, None], right_row[None], rows)

    up_prev = gathered(up_state, from_left[2], from_right[2])
    conv_prev = gathered(conv_state, from_left[3], from_right[3])

    latent_f = arrived.astype(jnp.float32)
    prior_f = up_prev.astype(jnp.float32)
    residual_zero = jnp.stack(
        [
            latent_f * up_kernel[0] + prior_f * up_kernel[2],
            latent_f * up_kernel[1] + prior_f * up_kernel[3],
        ],
        axis=1,
    )
    normed_one = layer_norm(residual_zero, norm_gain_one).astype(jnp.bfloat16)
    projections = jnp.einsum(
        "sfd,kde->ksfe", normed_one, qkv_weight, preferred_element_type=jnp.float32
    )
    times = positions[:, None] + jnp.arange(2, dtype=jnp.int32)[None, :]
    queries = rotate(projections[0], times, HEAD_DIM).astype(jnp.bfloat16)
    fresh_keys = rotate(projections[1], times, HEAD_DIM).astype(jnp.bfloat16)
    fresh_values = projections[2].astype(jnp.bfloat16)
    attended = attend(
        queries,
        fresh_keys,
        fresh_values,
        keys_old,
        values_old,
        positions,
        head_share // HEAD_DIM,
        HEAD_DIM,
    )
    partial_heads = jnp.dot(
        attended.reshape(2 * streams, head_share), out_weight, preferred_element_type=jnp.float32
    )
    mixing = section_sum(partial_heads)
    residual_one = residual_zero + scale_attention * mixing.reshape(streams, 2, model_width)
    normed_two = (
        layer_norm(residual_one, norm_gain_two)
        .astype(jnp.bfloat16)
        .reshape(2 * streams, model_width)
    )
    inner_units = jax.nn.gelu(
        jnp.dot(normed_two, in_weight, preferred_element_type=jnp.float32), approximate=False
    ).astype(jnp.bfloat16)
    partial_units = jnp.dot(inner_units, down_weight, preferred_element_type=jnp.float32)
    feed_forward = section_sum(partial_units)
    residual_two = residual_one + scale_feedforward * feed_forward.reshape(streams, 2, model_width)
    excited = jax.nn.elu(residual_two).astype(jnp.bfloat16)
    earlier = jnp.stack([conv_prev, excited[:, 0]], axis=1)
    stride = conv_weight.shape[0] // 2
    audio_out = jnp.einsum(
        "sfi,rci->csfr", excited, conv_weight[:stride], preferred_element_type=jnp.float32
    )
    audio_out = audio_out + jnp.einsum(
        "sfi,rci->csfr", earlier, conv_weight[stride:], preferred_element_type=jnp.float32
    )
    audio_out = audio_out + conv_bias[:, None, None, None]
    audio_out = audio_out.reshape(conv_bias.shape[0], streams * 2 * stride)
    cycle = jnp.arange(window, dtype=jnp.int32)
    hit_first = (cycle[None, :] == jnp.mod(positions, window)[:, None])[..., None]
    hit_second = (cycle[None, :] == jnp.mod(positions + 1, window)[:, None])[..., None]
    new_keys = jnp.where(
        hit_second,
        fresh_keys[:, 1][:, None, :],
        jnp.where(hit_first, fresh_keys[:, 0][:, None, :], keys_old),
    )
    new_values = jnp.where(
        hit_second,
        fresh_values[:, 1][:, None, :],
        jnp.where(hit_first, fresh_values[:, 0][:, None, :], values_old),
    )
    return (audio_out, new_keys, new_values, arrived, excited[:, 1])
def solution(mesh):
    placed = (
        P("batch", None),
        P("batch"),
        P("batch", None, "section"),
        P("batch", None, "section"),
        P("batch", None),
        P("batch", None),
        P("batch"),
        P("batch"),
        P(),
        P(),
        P(None, None, "section"),
        P("section", None),
        P(),
        P(),
        P(None, "section"),
        P("section", None),
        P(),
        P(None, "section", None),
        P("section"),
    )
    return jax.shard_map(
        local,
        mesh=mesh,
        in_specs=placed,
        out_specs=(
            P("section", "batch"),
            P("batch", None, "section"),
            P("batch", None, "section"),
            P("batch", None),
            P("batch", None),
        ),
        check_vma=False,
    )
```

```python
import jax
import jax.numpy as jnp
from jax import lax
from jax.sharding import PartitionSpec as P
from jax.experimental import pallas as pl
from jax.experimental.pallas import tpu as pltpu

HEAD_DIM = 64
CAP = 2
CODE_LANES = 128


EPSILON = 1e-05
MAX_PERIOD = 10000.0


def layer_norm(hidden, weight_gain):
    average = jnp.mean(hidden, axis=-1, keepdims=True)
    centred = hidden - average
    variance = jnp.mean(centred * centred, axis=-1, keepdims=True)
    return centred * lax.rsqrt(variance + EPSILON) * weight_gain


def rotate(features, times, head_width):
    streams = features.shape[0]
    half = head_width // 2
    freqs = MAX_PERIOD ** (-2.0 * jnp.arange(half, dtype=jnp.float32) / head_width)
    angle = times.astype(jnp.float32)[:, :, None] * freqs[None, None, :]
    cosine = jnp.cos(angle)[:, :, None, :]
    sine = jnp.sin(angle)[:, :, None, :]
    paired = features.reshape(streams, 2, -1, half, 2)
    first = paired[..., 0]
    second = paired[..., 1]
    turned = jnp.stack([first * cosine - second * sine, first * sine + second * cosine], axis=-1)
    return turned.reshape(features.shape)


def attend(queries, fresh_keys, fresh_values, old_keys, old_values, starts, local_heads, head_width):
    streams, window, share = old_keys.shape
    head_of = jnp.arange(share, dtype=jnp.int32) // head_width
    head_ids = jnp.arange(local_heads, dtype=jnp.int32)
    in_head = head_of[None, :] == head_ids[:, None]
    lanes = in_head[None, :, None, :]
    masked = jnp.where(lanes, queries[:, None], jnp.zeros((), queries.dtype))
    masked = masked.reshape(streams, local_heads * 2, share)
    score_scale = head_width ** (-0.5)
    cache_scores = (
        jnp.einsum("sxd,swd->sxw", masked, old_keys, preferred_element_type=jnp.float32)
        * score_scale
    )
    fresh_scores = (
        jnp.einsum("sxd,sgd->sxg", masked, fresh_keys, preferred_element_type=jnp.float32)
        * score_scale
    )
    cycle_slots = jnp.arange(window, dtype=jnp.int32)
    held_time = starts[:, None] - window + jnp.mod(cycle_slots[None, :] - starts[:, None], window)
    query_times = starts[:, None] + jnp.arange(2, dtype=jnp.int32)[None, :]
    cache_ok = (held_time[:, None, :] >= 0) & (
        held_time[:, None, :] > query_times[:, :, None] - window
    )
    cache_ok = jnp.broadcast_to(cache_ok[:, None], (streams, local_heads, 2, window)).reshape(
        streams, local_heads * 2, window
    )
    frame_ids = jnp.arange(2, dtype=jnp.int32)
    fresh_ok = jnp.tile(frame_ids[None, :] <= frame_ids[:, None], (local_heads, 1))[None]
    cache_scores = jnp.where(cache_ok, cache_scores, -jnp.inf)
    fresh_scores = jnp.where(fresh_ok, fresh_scores, -jnp.inf)
    score_max = jnp.maximum(
        jnp.max(cache_scores, axis=-1, keepdims=True), jnp.max(fresh_scores, axis=-1, keepdims=True)
    )
    cache_weights = jnp.where(cache_ok, jnp.exp(cache_scores - score_max), 0.0)
    fresh_weights = jnp.where(fresh_ok, jnp.exp(fresh_scores - score_max), 0.0)
    denominator = jnp.sum(cache_weights, axis=-1, keepdims=True) + jnp.sum(
        fresh_weights, axis=-1, keepdims=True
    )
    spread = jnp.einsum(
        "sxw,swd->sxd",
        cache_weights.astype(jnp.bfloat16),
        old_values,
        preferred_element_type=jnp.float32,
    )
    spread = spread + jnp.einsum(
        "sxg,sgd->sxd",
        fresh_weights.astype(jnp.bfloat16),
        fresh_values,
        preferred_element_type=jnp.float32,
    )
    spread = (spread / denominator).reshape(streams, local_heads, 2, share)
    attended = jnp.sum(jnp.where(lanes, spread, 0.0), axis=1)
    return attended.astype(jnp.bfloat16)


def section_sum(partial):
    size = lax.axis_size("section")
    if size != 4:
        return lax.psum(partial.astype(jnp.bfloat16), "section").astype(jnp.float32)
    rounded = partial.astype(jnp.bfloat16)
    got = [
        lax.ppermute(rounded, "section", [(i, i ^ mask) for i in range(size)]).astype(jnp.float32)
        for mask in (1, 2, 3)
    ]
    return (rounded.astype(jnp.float32) + got[0]) + (got[1] + got[2])


def cache_kernel(src_ref, take_ref, keys_ref, values_ref, lbox_ref, rbox_ref, ok_ref, ov_ref):
    streams, window, _ = keys_ref.shape

    def body(n, carry):
        src = src_ref[n]
        take = take_ref[n]
        ok_ref[n] = keys_ref[src]
        ov_ref[n] = values_ref[src]

        @pl.when(take == 1)
        def _():
            ok_ref[n] = lbox_ref[0:window]
            ov_ref[n] = lbox_ref[window : 2 * window]

        @pl.when(take == 2)
        def _():
            ok_ref[n] = rbox_ref[0:window]
            ov_ref[n] = rbox_ref[window : 2 * window]

        return carry

    lax.fori_loop(0, streams, body, 0)


def route_caches(src, take, keys, values, lbox, rbox):
    smem = pl.BlockSpec(memory_space=pltpu.SMEM)
    vmem = pl.BlockSpec(memory_space=pltpu.VMEM)
    shape = jax.ShapeDtypeStruct(keys.shape, keys.dtype)
    moved = 4 * keys.size * keys.dtype.itemsize
    return pl.pallas_call(
        cache_kernel,
        out_shape=(shape, shape),
        in_specs=[smem] * 2 + [vmem] * 4,
        out_specs=(vmem, vmem),
        cost_estimate=pl.CostEstimate(flops=0, transcendentals=0, bytes_accessed=moved),
    )(src, take, keys, values, lbox, rbox)


def one_hot(rows, columns):
    return (rows[:, None] == columns[None, :]).astype(jnp.bfloat16)


def local(
    latents,
    token_slot,
    cache_keys,
    cache_values,
    up_state,
    conv_state,
    cache_slot,
    positions,
    up_kernel,
    norm_gain_one,
    qkv_weight,
    out_weight,
    scale_attention,
    norm_gain_two,
    in_weight,
    down_weight,
    scale_feedforward,
    conv_weight,
    conv_bias,
):
    owners = lax.axis_size("batch")
    own_index = lax.axis_index("batch")
    streams = latents.shape[0]
    model_width = latents.shape[1]
    window = cache_keys.shape[1]
    head_share = cache_keys.shape[2]
    capacity = max(CAP, streams // owners)
    slot_ids = jnp.arange(streams, dtype=jnp.int32)

    dest_owner = cache_slot // streams
    dest_local = cache_slot % streams
    right_owner = jnp.mod(own_index + 1, owners)
    left_owner = jnp.mod(own_index + owners - 1, owners)
    state_rows = model_width // head_share

    def pack(direction_owner):
        chosen = dest_owner == direction_owner
        code = jnp.sum(jnp.where(chosen, dest_local + 1, 0))

        def pick(rows):
            shape = (streams,) + (1,) * (rows.ndim - 1)
            return jnp.sum(jnp.where(chosen.reshape(shape), rows, jnp.zeros((), rows.dtype)), axis=0)

        pieces = [
            pick(cache_keys),
            pick(cache_values),
            pick(up_state).reshape(state_rows, head_share),
            pick(conv_state).reshape(state_rows, head_share),
            jnp.full((8, head_share), code, jnp.int32).astype(jnp.bfloat16),
        ]
        return jnp.concatenate(pieces, axis=0)

    def unpack(box):
        keys = box[:window]
        values = box[window : 2 * window]
        up = box[2 * window : 2 * window + state_rows].reshape(model_width)
        conv = box[2 * window + state_rows : 2 * window + 2 * state_rows].reshape(model_width)
        code = box[2 * window + 2 * state_rows, 0].astype(jnp.int32) - 1
        return keys, values, up, conv, code

    left_box = lax.ppermute(
        pack(right_owner), "batch", [(i, (i + 1) % owners) for i in range(owners)]
    )
    right_box = lax.ppermute(
        pack(left_owner), "batch", [(i, (i - 1) % owners) for i in range(owners)]
    )
    from_left = unpack(left_box)
    from_right = unpack(right_box)

    target = token_slot // streams
    landing = token_slot % streams
    same_before = (target[None, :] == target[:, None]) & (slot_ids[None, :] < slot_ids[:, None])
    arrival_rank = jnp.sum(same_before.astype(jnp.int32), axis=1)
    owner_ids = jnp.arange(owners, dtype=jnp.int32)
    lane_ids = jnp.arange(CODE_LANES, dtype=jnp.int32)
    blocks = []
    code_block = jnp.zeros((owners, CODE_LANES), jnp.int32)
    for rank in range(capacity):
        chosen = (owner_ids[:, None] == target[None, :]) & (arrival_rank == rank)[None, :]
        blocks.append(
            jnp.dot(chosen.astype(jnp.bfloat16), latents, preferred_element_type=jnp.float32)
        )
        code = jnp.sum(jnp.where(chosen, landing[None, :] + 1, 0), axis=1)
        code_block = jnp.where(lane_ids[None, :] == rank, code[:, None], code_block)
    blocks.append(code_block.astype(jnp.float32))
    send = jnp.concatenate(blocks, axis=1).astype(jnp.bfloat16)
    got = lax.all_to_all(send, "batch", split_axis=0, concat_axis=0, tiled=True)
    arrived = jnp.zeros((streams, model_width), jnp.float32)
    for rank in range(capacity):
        got_code = got[:, capacity * model_width + rank].astype(jnp.int32) - 1
        arrived = arrived + jnp.dot(
            one_hot(slot_ids, got_code),
            got[:, rank * model_width : (rank + 1) * model_width],
            preferred_element_type=jnp.float32,
        )
    arrived = arrived.astype(jnp.bfloat16)

    staying = dest_owner == own_index
    source_of = (dest_local[None, :] == slot_ids[:, None]) & staying[None, :]
    source = jnp.sum(jnp.where(source_of, slot_ids[None, :], 0), axis=1)
    from_l = slot_ids == from_left[4]
    from_r = slot_ids == from_right[4]
    take = jnp.where(from_l, 1, jnp.where(from_r, 2, 0)).astype(jnp.int32)
    keys_old, values_old = route_caches(
        source, take, cache_keys, cache_values, left_box, right_box
    )
    picking = source_of.astype(jnp.bfloat16)

    def gathered(own_rows, left_row, right_row):
        rows = jnp.dot(picking, own_rows, preferred_element_type=jnp.float32)
        rows = rows.astype(own_rows.dtype)
        rows = jnp.where(from_l[:, None], left_row[None], rows)
        return jnp.where(from_r[:, None], right_row[None], rows)

    up_prev = gathered(up_state, from_left[2], from_right[2])
    conv_prev = gathered(conv_state, from_left[3], from_right[3])

    latent_f = arrived.astype(jnp.float32)
    prior_f = up_prev.astype(jnp.float32)
    residual_zero = jnp.stack(
        [
            latent_f * up_kernel[0] + prior_f * up_kernel[2],
            latent_f * up_kernel[1] + prior_f * up_kernel[3],
        ],
        axis=1,
    )
    normed_one = layer_norm(residual_zero, norm_gain_one).astype(jnp.bfloat16)
    projections = jnp.einsum(
        "sfd,kde->ksfe", normed_one, qkv_weight, preferred_element_type=jnp.float32
    )
    times = positions[:, None] + jnp.arange(2, dtype=jnp.int32)[None, :]
    queries = rotate(projections[0], times, HEAD_DIM).astype(jnp.bfloat16)
    fresh_keys = rotate(projections[1], times, HEAD_DIM).astype(jnp.bfloat16)
    fresh_values = projections[2].astype(jnp.bfloat16)
    attended = attend(
        queries,
        fresh_keys,
        fresh_values,
        keys_old,
        values_old,
        positions,
        head_share // HEAD_DIM,
        HEAD_DIM,
    )
    partial_heads = jnp.dot(
        attended.reshape(2 * streams, head_share), out_weight, preferred_element_type=jnp.float32
    )
    mixing = section_sum(partial_heads)
    residual_one = residual_zero + scale_attention * mixing.reshape(streams, 2, model_width)
    normed_two = (
        layer_norm(residual_one, norm_gain_two)
        .astype(jnp.bfloat16)
        .reshape(2 * streams, model_width)
    )
    inner_units = jax.nn.gelu(
        jnp.dot(normed_two, in_weight, preferred_element_type=jnp.float32), approximate=False
    ).astype(jnp.bfloat16)
    partial_units = jnp.dot(inner_units, down_weight, preferred_element_type=jnp.float32)
    feed_forward = section_sum(partial_units)
    residual_two = residual_one + scale_feedforward * feed_forward.reshape(streams, 2, model_width)
    excited = jax.nn.elu(residual_two).astype(jnp.bfloat16)
    earlier = jnp.stack([conv_prev, excited[:, 0]], axis=1)
    stride = conv_weight.shape[0] // 2
    audio_out = jnp.einsum(
        "sfi,rci->csfr", excited, conv_weight[:stride], preferred_element_type=jnp.float32
    )
    audio_out = audio_out + jnp.einsum(
        "sfi,rci->csfr", earlier, conv_weight[stride:], preferred_element_type=jnp.float32
    )
    audio_out = audio_out + conv_bias[:, None, None, None]
    audio_out = audio_out.reshape(conv_bias.shape[0], streams * 2 * stride)
    cycle = jnp.arange(window, dtype=jnp.int32)
    hit_first = (cycle[None, :] == jnp.mod(positions, window)[:, None])[..., None]
    hit_second = (cycle[None, :] == jnp.mod(positions + 1, window)[:, None])[..., None]
    new_keys = jnp.where(
        hit_second,
        fresh_keys[:, 1][:, None, :],
        jnp.where(hit_first, fresh_keys[:, 0][:, None, :], keys_old),
    )
    new_values = jnp.where(
        hit_second,
        fresh_values[:, 1][:, None, :],
        jnp.where(hit_first, fresh_values[:, 0][:, None, :], values_old),
    )
    return (audio_out, new_keys, new_values, arrived, excited[:, 1])
def solution(mesh):
    placed = (
        P("batch", None),
        P("batch"),
        P("batch", None, "section"),
        P("batch", None, "section"),
        P("batch", None),
        P("batch", None),
        P("batch"),
        P("batch"),
        P(),
        P(),
        P(None, None, "section"),
        P("section", None),
        P(),
        P(),
        P(None, "section"),
        P("section", None),
        P(),
        P(None, "section", None),
        P("section"),
    )
    return jax.shard_map(
        local,
        mesh=mesh,
        in_specs=placed,
        out_specs=(
            P("section", "batch"),
            P("batch", None, "section"),
            P("batch", None, "section"),
            P("batch", None),
            P("batch", None),
        ),
        check_vma=False,
    )
```

```python
import jax
import jax.numpy as jnp
from jax import lax
from jax.sharding import PartitionSpec as P
from jax.experimental import pallas as pl
from jax.experimental.pallas import tpu as pltpu

HEAD_DIM = 64
CAP = 2
CODE_LANES = 128


EPSILON = 1e-05
MAX_PERIOD = 10000.0


def layer_norm(hidden, weight_gain):
    average = jnp.mean(hidden, axis=-1, keepdims=True)
    centred = hidden - average
    variance = jnp.mean(centred * centred, axis=-1, keepdims=True)
    return centred * lax.rsqrt(variance + EPSILON) * weight_gain


def rotate(features, times, head_width):
    streams = features.shape[0]
    half = head_width // 2
    freqs = MAX_PERIOD ** (-2.0 * jnp.arange(half, dtype=jnp.float32) / head_width)
    angle = times.astype(jnp.float32)[:, :, None] * freqs[None, None, :]
    cosine = jnp.cos(angle)[:, :, None, :]
    sine = jnp.sin(angle)[:, :, None, :]
    paired = features.reshape(streams, 2, -1, half, 2)
    first = paired[..., 0]
    second = paired[..., 1]
    turned = jnp.stack([first * cosine - second * sine, first * sine + second * cosine], axis=-1)
    return turned.reshape(features.shape)


def attend(queries, fresh_keys, fresh_values, old_keys, old_values, starts, local_heads, head_width):
    streams, window, share = old_keys.shape
    head_of = jnp.arange(share, dtype=jnp.int32) // head_width
    head_ids = jnp.arange(local_heads, dtype=jnp.int32)
    in_head = head_of[None, :] == head_ids[:, None]
    lanes = in_head[None, :, None, :]
    masked = jnp.where(lanes, queries[:, None], jnp.zeros((), queries.dtype))
    masked = masked.reshape(streams, local_heads * 2, share)
    score_scale = head_width ** (-0.5)
    cache_scores = (
        jnp.einsum("sxd,swd->sxw", masked, old_keys, preferred_element_type=jnp.float32)
        * score_scale
    )
    fresh_scores = (
        jnp.einsum("sxd,sgd->sxg", masked, fresh_keys, preferred_element_type=jnp.float32)
        * score_scale
    )
    cycle_slots = jnp.arange(window, dtype=jnp.int32)
    held_time = starts[:, None] - window + jnp.mod(cycle_slots[None, :] - starts[:, None], window)
    query_times = starts[:, None] + jnp.arange(2, dtype=jnp.int32)[None, :]
    cache_ok = (held_time[:, None, :] >= 0) & (
        held_time[:, None, :] > query_times[:, :, None] - window
    )
    cache_ok = jnp.broadcast_to(cache_ok[:, None], (streams, local_heads, 2, window)).reshape(
        streams, local_heads * 2, window
    )
    frame_ids = jnp.arange(2, dtype=jnp.int32)
    fresh_ok = jnp.tile(frame_ids[None, :] <= frame_ids[:, None], (local_heads, 1))[None]
    cache_scores = jnp.where(cache_ok, cache_scores, -jnp.inf)
    fresh_scores = jnp.where(fresh_ok, fresh_scores, -jnp.inf)
    score_max = jnp.maximum(
        jnp.max(cache_scores, axis=-1, keepdims=True), jnp.max(fresh_scores, axis=-1, keepdims=True)
    )
    cache_weights = jnp.where(cache_ok, jnp.exp(cache_scores - score_max), 0.0)
    fresh_weights = jnp.where(fresh_ok, jnp.exp(fresh_scores - score_max), 0.0)
    denominator = jnp.sum(cache_weights, axis=-1, keepdims=True) + jnp.sum(
        fresh_weights, axis=-1, keepdims=True
    )
    spread = jnp.einsum(
        "sxw,swd->sxd",
        cache_weights.astype(jnp.bfloat16),
        old_values,
        preferred_element_type=jnp.float32,
    )
    spread = spread + jnp.einsum(
        "sxg,sgd->sxd",
        fresh_weights.astype(jnp.bfloat16),
        fresh_values,
        preferred_element_type=jnp.float32,
    )
    spread = (spread / denominator).reshape(streams, local_heads, 2, share)
    attended = jnp.sum(jnp.where(lanes, spread, 0.0), axis=1)
    return attended.astype(jnp.bfloat16)


def section_sum(partial):
    size = lax.axis_size("section")
    if size & (size - 1):
        return lax.psum(partial.astype(jnp.bfloat16), "section").astype(jnp.float32)
    total = partial.astype(jnp.bfloat16)
    bit = size // 2
    while bit >= 1:
        route = [(i, i ^ bit) for i in range(size)]
        other = lax.ppermute(total, "section", route)
        total = total.astype(jnp.float32) + other.astype(jnp.float32)
        bit //= 2
    return total


def cache_kernel(src_ref, take_ref, keys_ref, values_ref, lbox_ref, rbox_ref, ok_ref, ov_ref):
    streams, window, _ = keys_ref.shape

    def body(n, carry):
        src = src_ref[n]
        take = take_ref[n]
        ok_ref[n] = keys_ref[src]
        ov_ref[n] = values_ref[src]

        @pl.when(take == 1)
        def _():
            ok_ref[n] = lbox_ref[0:window]
            ov_ref[n] = lbox_ref[window : 2 * window]

        @pl.when(take == 2)
        def _():
            ok_ref[n] = rbox_ref[0:window]
            ov_ref[n] = rbox_ref[window : 2 * window]

        return carry

    lax.fori_loop(0, streams, body, 0)


def route_caches(src, take, keys, values, lbox, rbox):
    smem = pl.BlockSpec(memory_space=pltpu.SMEM)
    vmem = pl.BlockSpec(memory_space=pltpu.VMEM)
    shape = jax.ShapeDtypeStruct(keys.shape, keys.dtype)
    moved = 4 * keys.size * keys.dtype.itemsize
    return pl.pallas_call(
        cache_kernel,
        out_shape=(shape, shape),
        in_specs=[smem] * 2 + [vmem] * 4,
        out_specs=(vmem, vmem),
        cost_estimate=pl.CostEstimate(flops=0, transcendentals=0, bytes_accessed=moved),
    )(src, take, keys, values, lbox, rbox)


def one_hot(rows, columns):
    return (rows[:, None] == columns[None, :]).astype(jnp.bfloat16)


def local(
    latents,
    token_slot,
    cache_keys,
    cache_values,
    up_state,
    conv_state,
    cache_slot,
    positions,
    up_kernel,
    norm_gain_one,
    qkv_weight,
    out_weight,
    scale_attention,
    norm_gain_two,
    in_weight,
    down_weight,
    scale_feedforward,
    conv_weight,
    conv_bias,
):
    owners = lax.axis_size("batch")
    own_index = lax.axis_index("batch")
    streams = latents.shape[0]
    model_width = latents.shape[1]
    window = cache_keys.shape[1]
    head_share = cache_keys.shape[2]
    capacity = max(CAP, streams // owners)
    slot_ids = jnp.arange(streams, dtype=jnp.int32)

    dest_owner = cache_slot // streams
    dest_local = cache_slot % streams
    right_owner = jnp.mod(own_index + 1, owners)
    left_owner = jnp.mod(own_index + owners - 1, owners)
    state_rows = model_width // head_share

    def pack(direction_owner):
        chosen = dest_owner == direction_owner
        code = jnp.sum(jnp.where(chosen, dest_local + 1, 0))

        def pick(rows):
            shape = (streams,) + (1,) * (rows.ndim - 1)
            return jnp.sum(jnp.where(chosen.reshape(shape), rows, jnp.zeros((), rows.dtype)), axis=0)

        pieces = [
            pick(cache_keys),
            pick(cache_values),
            pick(up_state).reshape(state_rows, head_share),
            pick(conv_state).reshape(state_rows, head_share),
            jnp.full((8, head_share), code, jnp.int32).astype(jnp.bfloat16),
        ]
        return jnp.concatenate(pieces, axis=0)

    def unpack(box):
        keys = box[:window]
        values = box[window : 2 * window]
        up = box[2 * window : 2 * window + state_rows].reshape(model_width)
        conv = box[2 * window + state_rows : 2 * window + 2 * state_rows].reshape(model_width)
        code = box[2 * window + 2 * state_rows, 0].astype(jnp.int32) - 1
        return keys, values, up, conv, code

    left_box = lax.ppermute(
        pack(right_owner), "batch", [(i, (i + 1) % owners) for i in range(owners)]
    )
    right_box = lax.ppermute(
        pack(left_owner), "batch", [(i, (i - 1) % owners) for i in range(owners)]
    )
    from_left = unpack(left_box)
    from_right = unpack(right_box)

    target = token_slot // streams
    landing = token_slot % streams
    same_before = (target[None, :] == target[:, None]) & (slot_ids[None, :] < slot_ids[:, None])
    arrival_rank = jnp.sum(same_before.astype(jnp.int32), axis=1)
    box_ids = target * capacity + arrival_rank
    payload = jnp.concatenate(
        [
            latents,
            jnp.broadcast_to((landing + 1).astype(jnp.bfloat16)[:, None], (streams, CODE_LANES)),
        ],
        axis=1,
    )
    placing = one_hot(jnp.arange(owners * capacity, dtype=jnp.int32), box_ids)
    send_rows = jnp.dot(placing, payload, preferred_element_type=jnp.float32).astype(jnp.bfloat16)
    got = lax.all_to_all(
        send_rows.reshape(owners, capacity, model_width + CODE_LANES),
        "batch",
        split_axis=0,
        concat_axis=0,
        tiled=True,
    ).reshape(owners * capacity, model_width + CODE_LANES)
    got_codes = got[:, model_width].astype(jnp.int32) - 1
    arrived = jnp.dot(
        one_hot(slot_ids, got_codes), got[:, :model_width], preferred_element_type=jnp.float32
    ).astype(jnp.bfloat16)

    staying = dest_owner == own_index
    source_of = (dest_local[None, :] == slot_ids[:, None]) & staying[None, :]
    source = jnp.sum(jnp.where(source_of, slot_ids[None, :], 0), axis=1)
    from_l = slot_ids == from_left[4]
    from_r = slot_ids == from_right[4]
    take = jnp.where(from_l, 1, jnp.where(from_r, 2, 0)).astype(jnp.int32)
    keys_old, values_old = route_caches(
        source, take, cache_keys, cache_values, left_box, right_box
    )
    picking = source_of.astype(jnp.bfloat16)

    def gathered(own_rows, left_row, right_row):
        rows = jnp.dot(picking, own_rows, preferred_element_type=jnp.float32)
        rows = rows.astype(own_rows.dtype)
        rows = jnp.where(from_l[:, None], left_row[None], rows)
        return jnp.where(from_r[:, None], right_row[None], rows)

    up_prev = gathered(up_state, from_left[2], from_right[2])
    conv_prev = gathered(conv_state, from_left[3], from_right[3])

    latent_f = arrived.astype(jnp.float32)
    prior_f = up_prev.astype(jnp.float32)
    residual_zero = jnp.stack(
        [
            latent_f * up_kernel[0] + prior_f * up_kernel[2],
            latent_f * up_kernel[1] + prior_f * up_kernel[3],
        ],
        axis=1,
    )
    normed_one = layer_norm(residual_zero, norm_gain_one).astype(jnp.bfloat16)
    projections = jnp.einsum(
        "sfd,kde->ksfe", normed_one, qkv_weight, preferred_element_type=jnp.float32
    )
    times = positions[:, None] + jnp.arange(2, dtype=jnp.int32)[None, :]
    queries = rotate(projections[0], times, HEAD_DIM).astype(jnp.bfloat16)
    fresh_keys = rotate(projections[1], times, HEAD_DIM).astype(jnp.bfloat16)
    fresh_values = projections[2].astype(jnp.bfloat16)
    to_source = jnp.transpose(picking)
    arrivals = jnp.stack([from_l, from_r]).astype(jnp.bfloat16)

    def reorder(order, rows):
        return jnp.einsum(
            "gn,nfd->gfd", order, rows, preferred_element_type=jnp.float32
        ).astype(rows.dtype)

    def reorder_positions(order):
        return jnp.sum(jnp.where(order > 0, positions[None, :], 0), axis=1)

    local_heads = head_share // HEAD_DIM
    staying_attended = attend(
        reorder(to_source, queries),
        reorder(to_source, fresh_keys),
        reorder(to_source, fresh_values),
        cache_keys,
        cache_values,
        reorder_positions(to_source),
        local_heads,
        HEAD_DIM,
    )
    arriving_attended = attend(
        reorder(arrivals, queries),
        reorder(arrivals, fresh_keys),
        reorder(arrivals, fresh_values),
        jnp.stack([from_left[0], from_right[0]]),
        jnp.stack([from_left[1], from_right[1]]),
        reorder_positions(arrivals),
        local_heads,
        HEAD_DIM,
    )
    attended = reorder(picking, staying_attended) + reorder(
        jnp.transpose(arrivals), arriving_attended
    )
    partial_heads = jnp.dot(
        attended.reshape(2 * streams, head_share), out_weight, preferred_element_type=jnp.float32
    )
    mixing = section_sum(partial_heads)
    residual_one = residual_zero + scale_attention * mixing.reshape(streams, 2, model_width)
    normed_two = (
        layer_norm(residual_one, norm_gain_two)
        .astype(jnp.bfloat16)
        .reshape(2 * streams, model_width)
    )
    inner_units = jax.nn.gelu(
        jnp.dot(normed_two, in_weight, preferred_element_type=jnp.float32), approximate=False
    ).astype(jnp.bfloat16)
    partial_units = jnp.dot(inner_units, down_weight, preferred_element_type=jnp.float32)
    feed_forward = section_sum(partial_units)
    residual_two = residual_one + scale_feedforward * feed_forward.reshape(streams, 2, model_width)
    excited = jax.nn.elu(residual_two).astype(jnp.bfloat16)
    earlier = jnp.stack([conv_prev, excited[:, 0]], axis=1)
    stride = conv_weight.shape[0] // 2
    audio_out = jnp.einsum(
        "sfi,rci->csfr", excited, conv_weight[:stride], preferred_element_type=jnp.float32
    )
    audio_out = audio_out + jnp.einsum(
        "sfi,rci->csfr", earlier, conv_weight[stride:], preferred_element_type=jnp.float32
    )
    audio_out = audio_out + conv_bias[:, None, None, None]
    audio_out = audio_out.reshape(conv_bias.shape[0], streams * 2 * stride)
    cycle = jnp.arange(window, dtype=jnp.int32)
    hit_first = (cycle[None, :] == jnp.mod(positions, window)[:, None])[..., None]
    hit_second = (cycle[None, :] == jnp.mod(positions + 1, window)[:, None])[..., None]
    new_keys = jnp.where(
        hit_second,
        fresh_keys[:, 1][:, None, :],
        jnp.where(hit_first, fresh_keys[:, 0][:, None, :], keys_old),
    )
    new_values = jnp.where(
        hit_second,
        fresh_values[:, 1][:, None, :],
        jnp.where(hit_first, fresh_values[:, 0][:, None, :], values_old),
    )
    return (audio_out, new_keys, new_values, arrived, excited[:, 1])
def solution(mesh):
    placed = (
        P("batch", None),
        P("batch"),
        P("batch", None, "section"),
        P("batch", None, "section"),
        P("batch", None),
        P("batch", None),
        P("batch"),
        P("batch"),
        P(),
        P(),
        P(None, None, "section"),
        P("section", None),
        P(),
        P(),
        P(None, "section"),
        P("section", None),
        P(),
        P(None, "section", None),
        P("section"),
    )
    return jax.shard_map(
        local,
        mesh=mesh,
        in_specs=placed,
        out_specs=(
            P("section", "batch"),
            P("batch", None, "section"),
            P("batch", None, "section"),
            P("batch", None),
            P("batch", None),
        ),
        check_vma=False,
    )
```

```python
import jax
import jax.numpy as jnp
from jax import lax
from jax.sharding import PartitionSpec as P
from jax.experimental import pallas as pl
from jax.experimental.pallas import tpu as pltpu

HEAD_DIM = 64
CAP = 2
CODE_LANES = 128


EPSILON = 1e-05
MAX_PERIOD = 10000.0


def layer_norm(hidden, weight_gain):
    average = jnp.mean(hidden, axis=-1, keepdims=True)
    centred = hidden - average
    variance = jnp.mean(centred * centred, axis=-1, keepdims=True)
    return centred * lax.rsqrt(variance + EPSILON) * weight_gain


def rotate(features, times, head_width):
    streams = features.shape[0]
    half = head_width // 2
    freqs = MAX_PERIOD ** (-2.0 * jnp.arange(half, dtype=jnp.float32) / head_width)
    angle = times.astype(jnp.float32)[:, :, None] * freqs[None, None, :]
    cosine = jnp.cos(angle)[:, :, None, :]
    sine = jnp.sin(angle)[:, :, None, :]
    paired = features.reshape(streams, 2, -1, half, 2)
    first = paired[..., 0]
    second = paired[..., 1]
    turned = jnp.stack([first * cosine - second * sine, first * sine + second * cosine], axis=-1)
    return turned.reshape(features.shape)


def attend(queries, fresh_keys, fresh_values, old_keys, old_values, starts, local_heads, head_width):
    streams, window, share = old_keys.shape
    head_of = jnp.arange(share, dtype=jnp.int32) // head_width
    head_ids = jnp.arange(local_heads, dtype=jnp.int32)
    in_head = head_of[None, :] == head_ids[:, None]
    lanes = in_head[None, :, None, :]
    masked = jnp.where(lanes, queries[:, None], jnp.zeros((), queries.dtype))
    masked = masked.reshape(streams, local_heads * 2, share)
    score_scale = head_width ** (-0.5)
    cache_scores = (
        jnp.einsum("sxd,swd->sxw", masked, old_keys, preferred_element_type=jnp.float32)
        * score_scale
    )
    fresh_scores = (
        jnp.einsum("sxd,sgd->sxg", masked, fresh_keys, preferred_element_type=jnp.float32)
        * score_scale
    )
    cycle_slots = jnp.arange(window, dtype=jnp.int32)
    held_time = starts[:, None] - window + jnp.mod(cycle_slots[None, :] - starts[:, None], window)
    query_times = starts[:, None] + jnp.arange(2, dtype=jnp.int32)[None, :]
    cache_ok = (held_time[:, None, :] >= 0) & (
        held_time[:, None, :] > query_times[:, :, None] - window
    )
    cache_ok = jnp.broadcast_to(cache_ok[:, None], (streams, local_heads, 2, window)).reshape(
        streams, local_heads * 2, window
    )
    frame_ids = jnp.arange(2, dtype=jnp.int32)
    fresh_ok = jnp.tile(frame_ids[None, :] <= frame_ids[:, None], (local_heads, 1))[None]
    cache_scores = jnp.where(cache_ok, cache_scores, -jnp.inf)
    fresh_scores = jnp.where(fresh_ok, fresh_scores, -jnp.inf)
    score_max = jnp.maximum(
        jnp.max(cache_scores, axis=-1, keepdims=True), jnp.max(fresh_scores, axis=-1, keepdims=True)
    )
    cache_weights = jnp.where(cache_ok, jnp.exp(cache_scores - score_max), 0.0)
    fresh_weights = jnp.where(fresh_ok, jnp.exp(fresh_scores - score_max), 0.0)
    denominator = jnp.sum(cache_weights, axis=-1, keepdims=True) + jnp.sum(
        fresh_weights, axis=-1, keepdims=True
    )
    spread = jnp.einsum(
        "sxw,swd->sxd",
        cache_weights.astype(jnp.bfloat16),
        old_values,
        preferred_element_type=jnp.float32,
    )
    spread = spread + jnp.einsum(
        "sxg,sgd->sxd",
        fresh_weights.astype(jnp.bfloat16),
        fresh_values,
        preferred_element_type=jnp.float32,
    )
    spread = (spread / denominator).reshape(streams, local_heads, 2, share)
    attended = jnp.sum(jnp.where(lanes, spread, 0.0), axis=1)
    return attended.astype(jnp.bfloat16)


def section_sum(partial):
    size = lax.axis_size("section")
    if size & (size - 1):
        return lax.psum(partial.astype(jnp.bfloat16), "section").astype(jnp.float32)
    total = partial.astype(jnp.bfloat16)
    bit = size // 2
    while bit >= 1:
        route = [(i, i ^ bit) for i in range(size)]
        other = lax.ppermute(total, "section", route)
        total = total.astype(jnp.float32) + other.astype(jnp.float32)
        bit //= 2
    return total


def cache_kernel(src_ref, take_ref, keys_ref, values_ref, lbox_ref, rbox_ref, ok_ref, ov_ref):
    streams, window, _ = keys_ref.shape

    def body(n, carry):
        src = src_ref[n]
        take = take_ref[n]
        ok_ref[n] = keys_ref[src]
        ov_ref[n] = values_ref[src]

        @pl.when(take == 1)
        def _():
            ok_ref[n] = lbox_ref[0:window]
            ov_ref[n] = lbox_ref[window : 2 * window]

        @pl.when(take == 2)
        def _():
            ok_ref[n] = rbox_ref[0:window]
            ov_ref[n] = rbox_ref[window : 2 * window]

        return carry

    lax.fori_loop(0, streams, body, 0)


def route_caches(src, take, keys, values, lbox, rbox):
    smem = pl.BlockSpec(memory_space=pltpu.SMEM)
    vmem = pl.BlockSpec(memory_space=pltpu.VMEM)
    shape = jax.ShapeDtypeStruct(keys.shape, keys.dtype)
    moved = 4 * keys.size * keys.dtype.itemsize
    return pl.pallas_call(
        cache_kernel,
        out_shape=(shape, shape),
        in_specs=[smem] * 2 + [vmem] * 4,
        out_specs=(vmem, vmem),
        cost_estimate=pl.CostEstimate(flops=0, transcendentals=0, bytes_accessed=moved),
    )(src, take, keys, values, lbox, rbox)


def one_hot(rows, columns):
    return (rows[:, None] == columns[None, :]).astype(jnp.bfloat16)


def local(
    latents,
    token_slot,
    cache_keys,
    cache_values,
    up_state,
    conv_state,
    cache_slot,
    positions,
    up_kernel,
    norm_gain_one,
    qkv_weight,
    out_weight,
    scale_attention,
    norm_gain_two,
    in_weight,
    down_weight,
    scale_feedforward,
    conv_weight,
    conv_bias,
):
    owners = lax.axis_size("batch")
    own_index = lax.axis_index("batch")
    streams = latents.shape[0]
    model_width = latents.shape[1]
    window = cache_keys.shape[1]
    head_share = cache_keys.shape[2]
    capacity = max(CAP, streams // owners)
    slot_ids = jnp.arange(streams, dtype=jnp.int32)

    target = token_slot // streams
    landing = token_slot % streams
    same_before = (target[None, :] == target[:, None]) & (slot_ids[None, :] < slot_ids[:, None])
    arrival_rank = jnp.sum(same_before.astype(jnp.int32), axis=1)
    box_ids = target * capacity + arrival_rank
    payload = jnp.concatenate(
        [
            latents,
            jnp.broadcast_to((landing + 1).astype(jnp.bfloat16)[:, None], (streams, CODE_LANES)),
        ],
        axis=1,
    )
    placing = one_hot(jnp.arange(owners * capacity, dtype=jnp.int32), box_ids)
    send_rows = jnp.dot(placing, payload, preferred_element_type=jnp.float32).astype(jnp.bfloat16)
    got = lax.all_to_all(
        send_rows.reshape(owners, capacity, model_width + CODE_LANES),
        "batch",
        split_axis=0,
        concat_axis=0,
        tiled=True,
    ).reshape(owners * capacity, model_width + CODE_LANES)

    got, cache_keys, cache_values, up_state, conv_state, cache_slot = lax.optimization_barrier(
        (got, cache_keys, cache_values, up_state, conv_state, cache_slot)
    )

    got_codes = got[:, model_width].astype(jnp.int32) - 1
    arrived = jnp.dot(
        one_hot(slot_ids, got_codes), got[:, :model_width], preferred_element_type=jnp.float32
    ).astype(jnp.bfloat16)

    dest_owner = cache_slot // streams
    dest_local = cache_slot % streams
    right_owner = jnp.mod(own_index + 1, owners)
    left_owner = jnp.mod(own_index + owners - 1, owners)
    state_rows = model_width // head_share

    def pack(direction_owner):
        chosen = dest_owner == direction_owner
        code = jnp.sum(jnp.where(chosen, dest_local + 1, 0))

        def pick(rows):
            shape = (streams,) + (1,) * (rows.ndim - 1)
            return jnp.sum(jnp.where(chosen.reshape(shape), rows, jnp.zeros((), rows.dtype)), axis=0)

        pieces = [
            pick(cache_keys),
            pick(cache_values),
            pick(up_state).reshape(state_rows, head_share),
            pick(conv_state).reshape(state_rows, head_share),
            jnp.full((8, head_share), code, jnp.int32).astype(jnp.bfloat16),
        ]
        return jnp.concatenate(pieces, axis=0)

    def unpack(box):
        keys = box[:window]
        values = box[window : 2 * window]
        up = box[2 * window : 2 * window + state_rows].reshape(model_width)
        conv = box[2 * window + state_rows : 2 * window + 2 * state_rows].reshape(model_width)
        code = box[2 * window + 2 * state_rows, 0].astype(jnp.int32) - 1
        return keys, values, up, conv, code

    left_box = lax.ppermute(
        pack(right_owner), "batch", [(i, (i + 1) % owners) for i in range(owners)]
    )
    right_box = lax.ppermute(
        pack(left_owner), "batch", [(i, (i - 1) % owners) for i in range(owners)]
    )
    from_left = unpack(left_box)
    from_right = unpack(right_box)


    staying = dest_owner == own_index
    source_of = (dest_local[None, :] == slot_ids[:, None]) & staying[None, :]
    source = jnp.sum(jnp.where(source_of, slot_ids[None, :], 0), axis=1)
    from_l = slot_ids == from_left[4]
    from_r = slot_ids == from_right[4]
    take = jnp.where(from_l, 1, jnp.where(from_r, 2, 0)).astype(jnp.int32)
    keys_old, values_old = route_caches(
        source, take, cache_keys, cache_values, left_box, right_box
    )
    picking = source_of.astype(jnp.bfloat16)

    def gathered(own_rows, left_row, right_row):
        rows = jnp.dot(picking, own_rows, preferred_element_type=jnp.float32)
        rows = rows.astype(own_rows.dtype)
        rows = jnp.where(from_l[:, None], left_row[None], rows)
        return jnp.where(from_r[:, None], right_row[None], rows)

    up_prev = gathered(up_state, from_left[2], from_right[2])
    conv_prev = gathered(conv_state, from_left[3], from_right[3])

    latent_f = arrived.astype(jnp.float32)
    prior_f = up_prev.astype(jnp.float32)
    residual_zero = jnp.stack(
        [
            latent_f * up_kernel[0] + prior_f * up_kernel[2],
            latent_f * up_kernel[1] + prior_f * up_kernel[3],
        ],
        axis=1,
    )
    normed_one = layer_norm(residual_zero, norm_gain_one).astype(jnp.bfloat16)
    projections = jnp.einsum(
        "sfd,kde->ksfe", normed_one, qkv_weight, preferred_element_type=jnp.float32
    )
    times = positions[:, None] + jnp.arange(2, dtype=jnp.int32)[None, :]
    queries = rotate(projections[0], times, HEAD_DIM).astype(jnp.bfloat16)
    fresh_keys = rotate(projections[1], times, HEAD_DIM).astype(jnp.bfloat16)
    fresh_values = projections[2].astype(jnp.bfloat16)
    to_source = jnp.transpose(picking)
    arrivals = jnp.stack([from_l, from_r]).astype(jnp.bfloat16)

    def reorder(order, rows):
        return jnp.einsum(
            "gn,nfd->gfd", order, rows, preferred_element_type=jnp.float32
        ).astype(rows.dtype)

    def reorder_positions(order):
        return jnp.sum(jnp.where(order > 0, positions[None, :], 0), axis=1)

    local_heads = head_share // HEAD_DIM
    staying_attended = attend(
        reorder(to_source, queries),
        reorder(to_source, fresh_keys),
        reorder(to_source, fresh_values),
        cache_keys,
        cache_values,
        reorder_positions(to_source),
        local_heads,
        HEAD_DIM,
    )
    arriving_attended = attend(
        reorder(arrivals, queries),
        reorder(arrivals, fresh_keys),
        reorder(arrivals, fresh_values),
        jnp.stack([from_left[0], from_right[0]]),
        jnp.stack([from_left[1], from_right[1]]),
        reorder_positions(arrivals),
        local_heads,
        HEAD_DIM,
    )
    attended = reorder(picking, staying_attended) + reorder(
        jnp.transpose(arrivals), arriving_attended
    )
    partial_heads = jnp.dot(
        attended.reshape(2 * streams, head_share), out_weight, preferred_element_type=jnp.float32
    )
    mixing = section_sum(partial_heads)
    residual_one = residual_zero + scale_attention * mixing.reshape(streams, 2, model_width)
    normed_two = (
        layer_norm(residual_one, norm_gain_two)
        .astype(jnp.bfloat16)
        .reshape(2 * streams, model_width)
    )
    inner_units = jax.nn.gelu(
        jnp.dot(normed_two, in_weight, preferred_element_type=jnp.float32), approximate=False
    ).astype(jnp.bfloat16)
    partial_units = jnp.dot(inner_units, down_weight, preferred_element_type=jnp.float32)
    feed_forward = section_sum(partial_units)
    residual_two = residual_one + scale_feedforward * feed_forward.reshape(streams, 2, model_width)
    excited = jax.nn.elu(residual_two).astype(jnp.bfloat16)
    earlier = jnp.stack([conv_prev, excited[:, 0]], axis=1)
    stride = conv_weight.shape[0] // 2
    audio_out = jnp.einsum(
        "sfi,rci->csfr", excited, conv_weight[:stride], preferred_element_type=jnp.float32
    )
    audio_out = audio_out + jnp.einsum(
        "sfi,rci->csfr", earlier, conv_weight[stride:], preferred_element_type=jnp.float32
    )
    audio_out = audio_out + conv_bias[:, None, None, None]
    audio_out = audio_out.reshape(conv_bias.shape[0], streams * 2 * stride)
    cycle = jnp.arange(window, dtype=jnp.int32)
    hit_first = (cycle[None, :] == jnp.mod(positions, window)[:, None])[..., None]
    hit_second = (cycle[None, :] == jnp.mod(positions + 1, window)[:, None])[..., None]
    new_keys = jnp.where(
        hit_second,
        fresh_keys[:, 1][:, None, :],
        jnp.where(hit_first, fresh_keys[:, 0][:, None, :], keys_old),
    )
    new_values = jnp.where(
        hit_second,
        fresh_values[:, 1][:, None, :],
        jnp.where(hit_first, fresh_values[:, 0][:, None, :], values_old),
    )
    return (audio_out, new_keys, new_values, arrived, excited[:, 1])
def solution(mesh):
    placed = (
        P("batch", None),
        P("batch"),
        P("batch", None, "section"),
        P("batch", None, "section"),
        P("batch", None),
        P("batch", None),
        P("batch"),
        P("batch"),
        P(),
        P(),
        P(None, None, "section"),
        P("section", None),
        P(),
        P(),
        P(None, "section"),
        P("section", None),
        P(),
        P(None, "section", None),
        P("section"),
    )
    return jax.shard_map(
        local,
        mesh=mesh,
        in_specs=placed,
        out_specs=(
            P("section", "batch"),
            P("batch", None, "section"),
            P("batch", None, "section"),
            P("batch", None),
            P("batch", None),
        ),
        check_vma=False,
    )
```

```python
import jax
import jax.numpy as jnp
from jax import lax
from jax.sharding import PartitionSpec as P
from jax.experimental import pallas as pl
from jax.experimental.pallas import tpu as pltpu

HEAD_DIM = 64
CAP = 2
CODE_LANES = 128


EPSILON = 1e-05
MAX_PERIOD = 10000.0


def layer_norm(hidden, weight_gain):
    average = jnp.mean(hidden, axis=-1, keepdims=True)
    centred = hidden - average
    variance = jnp.mean(centred * centred, axis=-1, keepdims=True)
    return centred * lax.rsqrt(variance + EPSILON) * weight_gain


def rotate(features, times, head_width):
    streams = features.shape[0]
    half = head_width // 2
    freqs = MAX_PERIOD ** (-2.0 * jnp.arange(half, dtype=jnp.float32) / head_width)
    angle = times.astype(jnp.float32)[:, :, None] * freqs[None, None, :]
    cosine = jnp.cos(angle)[:, :, None, :]
    sine = jnp.sin(angle)[:, :, None, :]
    paired = features.reshape(streams, 2, -1, half, 2)
    first = paired[..., 0]
    second = paired[..., 1]
    turned = jnp.stack([first * cosine - second * sine, first * sine + second * cosine], axis=-1)
    return turned.reshape(features.shape)


def attend(queries, fresh_keys, fresh_values, old_keys, old_values, starts, local_heads, head_width):
    streams, window, share = old_keys.shape
    head_of = jnp.arange(share, dtype=jnp.int32) // head_width
    head_ids = jnp.arange(local_heads, dtype=jnp.int32)
    in_head = head_of[None, :] == head_ids[:, None]
    lanes = in_head[None, :, None, :]
    masked = jnp.where(lanes, queries[:, None], jnp.zeros((), queries.dtype))
    masked = masked.reshape(streams, local_heads * 2, share)
    score_scale = head_width ** (-0.5)
    cache_scores = (
        jnp.einsum("sxd,swd->sxw", masked, old_keys, preferred_element_type=jnp.float32)
        * score_scale
    )
    fresh_scores = (
        jnp.einsum("sxd,sgd->sxg", masked, fresh_keys, preferred_element_type=jnp.float32)
        * score_scale
    )
    cycle_slots = jnp.arange(window, dtype=jnp.int32)
    held_time = starts[:, None] - window + jnp.mod(cycle_slots[None, :] - starts[:, None], window)
    query_times = starts[:, None] + jnp.arange(2, dtype=jnp.int32)[None, :]
    cache_ok = (held_time[:, None, :] >= 0) & (
        held_time[:, None, :] > query_times[:, :, None] - window
    )
    cache_ok = jnp.broadcast_to(cache_ok[:, None], (streams, local_heads, 2, window)).reshape(
        streams, local_heads * 2, window
    )
    frame_ids = jnp.arange(2, dtype=jnp.int32)
    fresh_ok = jnp.tile(frame_ids[None, :] <= frame_ids[:, None], (local_heads, 1))[None]
    cache_scores = jnp.where(cache_ok, cache_scores, -jnp.inf)
    fresh_scores = jnp.where(fresh_ok, fresh_scores, -jnp.inf)
    score_max = jnp.maximum(
        jnp.max(cache_scores, axis=-1, keepdims=True), jnp.max(fresh_scores, axis=-1, keepdims=True)
    )
    cache_weights = jnp.where(cache_ok, jnp.exp(cache_scores - score_max), 0.0)
    fresh_weights = jnp.where(fresh_ok, jnp.exp(fresh_scores - score_max), 0.0)
    denominator = jnp.sum(cache_weights, axis=-1, keepdims=True) + jnp.sum(
        fresh_weights, axis=-1, keepdims=True
    )
    spread = jnp.einsum(
        "sxw,swd->sxd",
        cache_weights.astype(jnp.bfloat16),
        old_values,
        preferred_element_type=jnp.float32,
    )
    spread = spread + jnp.einsum(
        "sxg,sgd->sxd",
        fresh_weights.astype(jnp.bfloat16),
        fresh_values,
        preferred_element_type=jnp.float32,
    )
    spread = (spread / denominator).reshape(streams, local_heads, 2, share)
    attended = jnp.sum(jnp.where(lanes, spread, 0.0), axis=1)
    return attended.astype(jnp.bfloat16)


def section_sum(partial):
    size = lax.axis_size("section")
    if size & (size - 1):
        return lax.psum(partial.astype(jnp.bfloat16), "section").astype(jnp.float32)
    total = partial.astype(jnp.bfloat16)
    bit = size // 2
    while bit >= 1:
        route = [(i, i ^ bit) for i in range(size)]
        other = lax.ppermute(total, "section", route)
        total = total.astype(jnp.float32) + other.astype(jnp.float32)
        bit //= 2
    return total


def cache_kernel(src_ref, take_ref, keys_ref, values_ref, lbox_ref, rbox_ref, ok_ref, ov_ref):
    streams, window, _ = keys_ref.shape

    def body(n, carry):
        src = src_ref[n]
        take = take_ref[n]
        ok_ref[n] = keys_ref[src]
        ov_ref[n] = values_ref[src]

        @pl.when(take == 1)
        def _():
            ok_ref[n] = lbox_ref[0:window]
            ov_ref[n] = lbox_ref[window : 2 * window]

        @pl.when(take == 2)
        def _():
            ok_ref[n] = rbox_ref[0:window]
            ov_ref[n] = rbox_ref[window : 2 * window]

        return carry

    lax.fori_loop(0, streams, body, 0)


def route_caches(src, take, keys, values, lbox, rbox):
    smem = pl.BlockSpec(memory_space=pltpu.SMEM)
    vmem = pl.BlockSpec(memory_space=pltpu.VMEM)
    shape = jax.ShapeDtypeStruct(keys.shape, keys.dtype)
    moved = 4 * keys.size * keys.dtype.itemsize
    return pl.pallas_call(
        cache_kernel,
        out_shape=(shape, shape),
        in_specs=[smem] * 2 + [vmem] * 4,
        out_specs=(vmem, vmem),
        cost_estimate=pl.CostEstimate(flops=0, transcendentals=0, bytes_accessed=moved),
    )(src, take, keys, values, lbox, rbox)


def one_hot(rows, columns):
    return (rows[:, None] == columns[None, :]).astype(jnp.bfloat16)


def local(
    latents,
    token_slot,
    cache_keys,
    cache_values,
    up_state,
    conv_state,
    cache_slot,
    positions,
    up_kernel,
    norm_gain_one,
    qkv_weight,
    out_weight,
    scale_attention,
    norm_gain_two,
    in_weight,
    down_weight,
    scale_feedforward,
    conv_weight,
    conv_bias,
):
    owners = lax.axis_size("batch")
    own_index = lax.axis_index("batch")
    streams = latents.shape[0]
    model_width = latents.shape[1]
    window = cache_keys.shape[1]
    head_share = cache_keys.shape[2]
    capacity = max(CAP, streams // owners)
    slot_ids = jnp.arange(streams, dtype=jnp.int32)

    dest_owner = cache_slot // streams
    dest_local = cache_slot % streams
    right_owner = jnp.mod(own_index + 1, owners)
    left_owner = jnp.mod(own_index + owners - 1, owners)
    state_rows = model_width // head_share

    def pack(direction_owner):
        chosen = dest_owner == direction_owner
        code = jnp.sum(jnp.where(chosen, dest_local + 1, 0))

        def pick(rows):
            shape = (streams,) + (1,) * (rows.ndim - 1)
            return jnp.sum(jnp.where(chosen.reshape(shape), rows, jnp.zeros((), rows.dtype)), axis=0)

        pieces = [
            pick(cache_keys),
            pick(cache_values),
            pick(up_state).reshape(state_rows, head_share),
            pick(conv_state).reshape(state_rows, head_share),
            jnp.full((8, head_share), code, jnp.int32).astype(jnp.bfloat16),
        ]
        return jnp.concatenate(pieces, axis=0)

    def unpack(box):
        keys = box[:window]
        values = box[window : 2 * window]
        up = box[2 * window : 2 * window + state_rows].reshape(model_width)
        conv = box[2 * window + state_rows : 2 * window + 2 * state_rows].reshape(model_width)
        code = box[2 * window + 2 * state_rows, 0].astype(jnp.int32) - 1
        return keys, values, up, conv, code

    left_box = lax.ppermute(
        pack(right_owner), "batch", [(i, (i + 1) % owners) for i in range(owners)]
    )
    right_box = lax.ppermute(
        pack(left_owner), "batch", [(i, (i - 1) % owners) for i in range(owners)]
    )
    from_left = unpack(left_box)
    from_right = unpack(right_box)

    target = token_slot // streams
    landing = token_slot % streams
    same_before = (target[None, :] == target[:, None]) & (slot_ids[None, :] < slot_ids[:, None])
    arrival_rank = jnp.sum(same_before.astype(jnp.int32), axis=1)
    members = lax.axis_size("section")
    member = lax.axis_index("section")
    part = model_width // members
    quarter = jnp.zeros((streams, part), latents.dtype)
    for k in range(members):
        quarter = jnp.where(member == k, latents[:, k * part : (k + 1) * part], quarter)
    owner_ids = jnp.arange(owners, dtype=jnp.int32)
    lane_ids = jnp.arange(CODE_LANES, dtype=jnp.int32)
    blocks = []
    code_block = jnp.zeros((owners, CODE_LANES), jnp.int32)
    for rank in range(capacity):
        chosen = (owner_ids[:, None] == target[None, :]) & (arrival_rank == rank)[None, :]
        blocks.append(
            jnp.dot(chosen.astype(jnp.bfloat16), quarter, preferred_element_type=jnp.float32)
        )
        code = jnp.sum(jnp.where(chosen, landing[None, :] + 1, 0), axis=1)
        code_block = jnp.where(lane_ids[None, :] == rank, code[:, None], code_block)
    blocks.append(code_block.astype(jnp.float32))
    send = jnp.concatenate(blocks, axis=1).astype(jnp.bfloat16)
    got = lax.all_to_all(send, "batch", split_axis=0, concat_axis=0, tiled=True)
    mine = jnp.zeros((streams, part), jnp.float32)
    for rank in range(capacity):
        got_code = got[:, capacity * part + rank].astype(jnp.int32) - 1
        mine = mine + jnp.dot(
            one_hot(slot_ids, got_code),
            got[:, rank * part : (rank + 1) * part],
            preferred_element_type=jnp.float32,
        )
    mine = mine.astype(jnp.bfloat16)
    if members == 4:
        pieces = [mine] + [
            lax.ppermute(mine, "section", [(i, i ^ mask) for i in range(members)])
            for mask in (1, 2, 3)
        ]
        columns = []
        for k in range(members):
            column = jnp.zeros_like(mine)
            for mask in range(members):
                column = jnp.where((member ^ mask) == k, pieces[mask], column)
            columns.append(column)
        arrived = jnp.concatenate(columns, axis=1)
    else:
        arrived = lax.all_gather(mine, "section", axis=1, tiled=True)

    staying = dest_owner == own_index
    source_of = (dest_local[None, :] == slot_ids[:, None]) & staying[None, :]
    source = jnp.sum(jnp.where(source_of, slot_ids[None, :], 0), axis=1)
    from_l = slot_ids == from_left[4]
    from_r = slot_ids == from_right[4]
    take = jnp.where(from_l, 1, jnp.where(from_r, 2, 0)).astype(jnp.int32)
    keys_old, values_old = route_caches(
        source, take, cache_keys, cache_values, left_box, right_box
    )
    picking = source_of.astype(jnp.bfloat16)

    def gathered(own_rows, left_row, right_row):
        rows = jnp.dot(picking, own_rows, preferred_element_type=jnp.float32)
        rows = rows.astype(own_rows.dtype)
        rows = jnp.where(from_l[:, None], left_row[None], rows)
        return jnp.where(from_r[:, None], right_row[None], rows)

    up_prev = gathered(up_state, from_left[2], from_right[2])
    conv_prev = gathered(conv_state, from_left[3], from_right[3])

    latent_f = arrived.astype(jnp.float32)
    prior_f = up_prev.astype(jnp.float32)
    residual_zero = jnp.stack(
        [
            latent_f * up_kernel[0] + prior_f * up_kernel[2],
            latent_f * up_kernel[1] + prior_f * up_kernel[3],
        ],
        axis=1,
    )
    normed_one = layer_norm(residual_zero, norm_gain_one).astype(jnp.bfloat16)
    projections = jnp.einsum(
        "sfd,kde->ksfe", normed_one, qkv_weight, preferred_element_type=jnp.float32
    )
    times = positions[:, None] + jnp.arange(2, dtype=jnp.int32)[None, :]
    queries = rotate(projections[0], times, HEAD_DIM).astype(jnp.bfloat16)
    fresh_keys = rotate(projections[1], times, HEAD_DIM).astype(jnp.bfloat16)
    fresh_values = projections[2].astype(jnp.bfloat16)
    attended = attend(
        queries,
        fresh_keys,
        fresh_values,
        keys_old,
        values_old,
        positions,
        head_share // HEAD_DIM,
        HEAD_DIM,
    )
    partial_heads = jnp.dot(
        attended.reshape(2 * streams, head_share), out_weight, preferred_element_type=jnp.float32
    )
    mixing = section_sum(partial_heads)
    residual_one = residual_zero + scale_attention * mixing.reshape(streams, 2, model_width)
    normed_two = (
        layer_norm(residual_one, norm_gain_two)
        .astype(jnp.bfloat16)
        .reshape(2 * streams, model_width)
    )
    inner_units = jax.nn.gelu(
        jnp.dot(normed_two, in_weight, preferred_element_type=jnp.float32), approximate=False
    ).astype(jnp.bfloat16)
    partial_units = jnp.dot(inner_units, down_weight, preferred_element_type=jnp.float32)
    feed_forward = section_sum(partial_units)
    residual_two = residual_one + scale_feedforward * feed_forward.reshape(streams, 2, model_width)
    excited = jax.nn.elu(residual_two).astype(jnp.bfloat16)
    earlier = jnp.stack([conv_prev, excited[:, 0]], axis=1)
    stride = conv_weight.shape[0] // 2
    audio_out = jnp.einsum(
        "sfi,rci->csfr", excited, conv_weight[:stride], preferred_element_type=jnp.float32
    )
    audio_out = audio_out + jnp.einsum(
        "sfi,rci->csfr", earlier, conv_weight[stride:], preferred_element_type=jnp.float32
    )
    audio_out = audio_out + conv_bias[:, None, None, None]
    audio_out = audio_out.reshape(conv_bias.shape[0], streams * 2 * stride)
    cycle = jnp.arange(window, dtype=jnp.int32)
    hit_first = (cycle[None, :] == jnp.mod(positions, window)[:, None])[..., None]
    hit_second = (cycle[None, :] == jnp.mod(positions + 1, window)[:, None])[..., None]
    new_keys = jnp.where(
        hit_second,
        fresh_keys[:, 1][:, None, :],
        jnp.where(hit_first, fresh_keys[:, 0][:, None, :], keys_old),
    )
    new_values = jnp.where(
        hit_second,
        fresh_values[:, 1][:, None, :],
        jnp.where(hit_first, fresh_values[:, 0][:, None, :], values_old),
    )
    return (audio_out, new_keys, new_values, arrived, excited[:, 1])
def solution(mesh):
    placed = (
        P("batch", None),
        P("batch"),
        P("batch", None, "section"),
        P("batch", None, "section"),
        P("batch", None),
        P("batch", None),
        P("batch"),
        P("batch"),
        P(),
        P(),
        P(None, None, "section"),
        P("section", None),
        P(),
        P(),
        P(None, "section"),
        P("section", None),
        P(),
        P(None, "section", None),
        P("section"),
    )
    return jax.shard_map(
        local,
        mesh=mesh,
        in_specs=placed,
        out_specs=(
            P("section", "batch"),
            P("batch", None, "section"),
            P("batch", None, "section"),
            P("batch", None),
            P("batch", None),
        ),
        check_vma=False,
    )
```

```python
import jax
import jax.numpy as jnp
from jax import lax
from jax.sharding import PartitionSpec as P
from jax.experimental import pallas as pl
from jax.experimental.pallas import tpu as pltpu

HEAD_DIM = 64
CAP = 2
CODE_LANES = 128


EPSILON = 1e-05
MAX_PERIOD = 10000.0


def layer_norm(hidden, weight_gain):
    average = jnp.mean(hidden, axis=-1, keepdims=True)
    centred = hidden - average
    variance = jnp.mean(centred * centred, axis=-1, keepdims=True)
    return centred * lax.rsqrt(variance + EPSILON) * weight_gain


def rotate(features, times, head_width):
    streams = features.shape[0]
    half = head_width // 2
    freqs = MAX_PERIOD ** (-2.0 * jnp.arange(half, dtype=jnp.float32) / head_width)
    angle = times.astype(jnp.float32)[:, :, None] * freqs[None, None, :]
    cosine = jnp.cos(angle)[:, :, None, :]
    sine = jnp.sin(angle)[:, :, None, :]
    paired = features.reshape(streams, 2, -1, half, 2)
    first = paired[..., 0]
    second = paired[..., 1]
    turned = jnp.stack([first * cosine - second * sine, first * sine + second * cosine], axis=-1)
    return turned.reshape(features.shape)


def attend(queries, fresh_keys, fresh_values, old_keys, old_values, starts, local_heads, head_width):
    streams, window, share = old_keys.shape
    head_of = jnp.arange(share, dtype=jnp.int32) // head_width
    head_ids = jnp.arange(local_heads, dtype=jnp.int32)
    in_head = head_of[None, :] == head_ids[:, None]
    lanes = in_head[None, :, None, :]
    masked = jnp.where(lanes, queries[:, None], jnp.zeros((), queries.dtype))
    masked = masked.reshape(streams, local_heads * 2, share)
    score_scale = head_width ** (-0.5)
    cache_scores = (
        jnp.einsum("sxd,swd->sxw", masked, old_keys, preferred_element_type=jnp.float32)
        * score_scale
    )
    fresh_scores = (
        jnp.einsum("sxd,sgd->sxg", masked, fresh_keys, preferred_element_type=jnp.float32)
        * score_scale
    )
    cycle_slots = jnp.arange(window, dtype=jnp.int32)
    held_time = starts[:, None] - window + jnp.mod(cycle_slots[None, :] - starts[:, None], window)
    query_times = starts[:, None] + jnp.arange(2, dtype=jnp.int32)[None, :]
    cache_ok = (held_time[:, None, :] >= 0) & (
        held_time[:, None, :] > query_times[:, :, None] - window
    )
    cache_ok = jnp.broadcast_to(cache_ok[:, None], (streams, local_heads, 2, window)).reshape(
        streams, local_heads * 2, window
    )
    frame_ids = jnp.arange(2, dtype=jnp.int32)
    fresh_ok = jnp.tile(frame_ids[None, :] <= frame_ids[:, None], (local_heads, 1))[None]
    cache_scores = jnp.where(cache_ok, cache_scores, -jnp.inf)
    fresh_scores = jnp.where(fresh_ok, fresh_scores, -jnp.inf)
    score_max = jnp.maximum(
        jnp.max(cache_scores, axis=-1, keepdims=True), jnp.max(fresh_scores, axis=-1, keepdims=True)
    )
    cache_weights = jnp.where(cache_ok, jnp.exp(cache_scores - score_max), 0.0)
    fresh_weights = jnp.where(fresh_ok, jnp.exp(fresh_scores - score_max), 0.0)
    denominator = jnp.sum(cache_weights, axis=-1, keepdims=True) + jnp.sum(
        fresh_weights, axis=-1, keepdims=True
    )
    spread = jnp.einsum(
        "sxw,swd->sxd",
        cache_weights.astype(jnp.bfloat16),
        old_values,
        preferred_element_type=jnp.float32,
    )
    spread = spread + jnp.einsum(
        "sxg,sgd->sxd",
        fresh_weights.astype(jnp.bfloat16),
        fresh_values,
        preferred_element_type=jnp.float32,
    )
    spread = (spread / denominator).reshape(streams, local_heads, 2, share)
    attended = jnp.sum(jnp.where(lanes, spread, 0.0), axis=1)
    return attended.astype(jnp.bfloat16)


def section_sum(partial):
    size = lax.axis_size("section")
    if size & (size - 1):
        return lax.psum(partial.astype(jnp.bfloat16), "section").astype(jnp.float32)
    total = partial.astype(jnp.bfloat16)
    bit = size // 2
    while bit >= 1:
        route = [(i, i ^ bit) for i in range(size)]
        other = lax.ppermute(total, "section", route)
        total = total.astype(jnp.float32) + other.astype(jnp.float32)
        bit //= 2
    return total


def cache_kernel(src_ref, take_ref, keys_ref, values_ref, lbox_ref, rbox_ref, ok_ref, ov_ref):
    streams, window, _ = keys_ref.shape

    def body(n, carry):
        src = src_ref[n]
        take = take_ref[n]
        ok_ref[n] = keys_ref[src]
        ov_ref[n] = values_ref[src]

        @pl.when(take == 1)
        def _():
            ok_ref[n] = lbox_ref[0:window]
            ov_ref[n] = lbox_ref[window : 2 * window]

        @pl.when(take == 2)
        def _():
            ok_ref[n] = rbox_ref[0:window]
            ov_ref[n] = rbox_ref[window : 2 * window]

        return carry

    lax.fori_loop(0, streams, body, 0)


def route_caches(src, take, keys, values, lbox, rbox):
    smem = pl.BlockSpec(memory_space=pltpu.SMEM)
    vmem = pl.BlockSpec(memory_space=pltpu.VMEM)
    shape = jax.ShapeDtypeStruct(keys.shape, keys.dtype)
    moved = 4 * keys.size * keys.dtype.itemsize
    return pl.pallas_call(
        cache_kernel,
        out_shape=(shape, shape),
        in_specs=[smem] * 2 + [vmem] * 4,
        out_specs=(vmem, vmem),
        cost_estimate=pl.CostEstimate(flops=0, transcendentals=0, bytes_accessed=moved),
    )(src, take, keys, values, lbox, rbox)


def one_hot(rows, columns):
    return (rows[:, None] == columns[None, :]).astype(jnp.bfloat16)


def local(
    latents,
    token_slot,
    cache_keys,
    cache_values,
    up_state,
    conv_state,
    cache_slot,
    positions,
    up_kernel,
    norm_gain_one,
    qkv_weight,
    out_weight,
    scale_attention,
    norm_gain_two,
    in_weight,
    down_weight,
    scale_feedforward,
    conv_weight,
    conv_bias,
):
    owners = lax.axis_size("batch")
    own_index = lax.axis_index("batch")
    streams = latents.shape[0]
    model_width = latents.shape[1]
    window = cache_keys.shape[1]
    head_share = cache_keys.shape[2]
    capacity = max(CAP, streams // owners)
    slot_ids = jnp.arange(streams, dtype=jnp.int32)

    dest_owner = cache_slot // streams
    dest_local = cache_slot % streams
    right_owner = jnp.mod(own_index + 1, owners)
    left_owner = jnp.mod(own_index + owners - 1, owners)
    state_rows = model_width // head_share

    def pack(direction_owner):
        chosen = dest_owner == direction_owner
        code = jnp.sum(jnp.where(chosen, dest_local + 1, 0))

        def pick(rows):
            shape = (streams,) + (1,) * (rows.ndim - 1)
            return jnp.sum(jnp.where(chosen.reshape(shape), rows, jnp.zeros((), rows.dtype)), axis=0)

        pieces = [
            pick(cache_keys),
            pick(cache_values),
            pick(up_state).reshape(state_rows, head_share),
            pick(conv_state).reshape(state_rows, head_share),
            jnp.full((8, head_share), code, jnp.int32).astype(jnp.bfloat16),
        ]
        return jnp.concatenate(pieces, axis=0)

    def unpack(box):
        keys = box[:window]
        values = box[window : 2 * window]
        up = box[2 * window : 2 * window + state_rows].reshape(model_width)
        conv = box[2 * window + state_rows : 2 * window + 2 * state_rows].reshape(model_width)
        code = box[2 * window + 2 * state_rows, 0].astype(jnp.int32) - 1
        return keys, values, up, conv, code

    left_box = lax.ppermute(
        pack(right_owner), "batch", [(i, (i + 1) % owners) for i in range(owners)]
    )
    right_box = lax.ppermute(
        pack(left_owner), "batch", [(i, (i - 1) % owners) for i in range(owners)]
    )
    from_left = unpack(left_box)
    from_right = unpack(right_box)

    target = token_slot // streams
    landing = token_slot % streams
    same_before = (target[None, :] == target[:, None]) & (slot_ids[None, :] < slot_ids[:, None])
    arrival_rank = jnp.sum(same_before.astype(jnp.int32), axis=1)
    members = lax.axis_size("section")
    halves = 2 if members % 2 == 0 else 1
    half = lax.axis_index("section") % halves
    part = model_width // halves
    share_rows = latents[:, :part]
    for k in range(1, halves):
        share_rows = jnp.where(half == k, latents[:, k * part : (k + 1) * part], share_rows)
    owner_ids = jnp.arange(owners, dtype=jnp.int32)
    lane_ids = jnp.arange(CODE_LANES, dtype=jnp.int32)
    blocks = []
    code_block = jnp.zeros((owners, CODE_LANES), jnp.int32)
    for rank in range(capacity):
        chosen = (owner_ids[:, None] == target[None, :]) & (arrival_rank == rank)[None, :]
        blocks.append(
            jnp.dot(chosen.astype(jnp.bfloat16), share_rows, preferred_element_type=jnp.float32)
        )
        code = jnp.sum(jnp.where(chosen, landing[None, :] + 1, 0), axis=1)
        code_block = jnp.where(lane_ids[None, :] == rank, code[:, None], code_block)
    blocks.append(code_block.astype(jnp.float32))
    send = jnp.concatenate(blocks, axis=1).astype(jnp.bfloat16)
    got = lax.all_to_all(send, "batch", split_axis=0, concat_axis=0, tiled=True)
    mine = jnp.zeros((streams, part), jnp.float32)
    for rank in range(capacity):
        got_code = got[:, capacity * part + rank].astype(jnp.int32) - 1
        mine = mine + jnp.dot(
            one_hot(slot_ids, got_code),
            got[:, rank * part : (rank + 1) * part],
            preferred_element_type=jnp.float32,
        )
    mine = mine.astype(jnp.bfloat16)
    if halves == 2:
        other = lax.ppermute(mine, "section", [(i, i ^ 1) for i in range(members)])
        lower = jnp.where(half == 0, mine, other)
        upper = jnp.where(half == 0, other, mine)
        arrived = jnp.concatenate([lower, upper], axis=1)
    else:
        arrived = mine

    staying = dest_owner == own_index
    source_of = (dest_local[None, :] == slot_ids[:, None]) & staying[None, :]
    source = jnp.sum(jnp.where(source_of, slot_ids[None, :], 0), axis=1)
    from_l = slot_ids == from_left[4]
    from_r = slot_ids == from_right[4]
    take = jnp.where(from_l, 1, jnp.where(from_r, 2, 0)).astype(jnp.int32)
    keys_old, values_old = route_caches(
        source, take, cache_keys, cache_values, left_box, right_box
    )
    picking = source_of.astype(jnp.bfloat16)

    def gathered(own_rows, left_row, right_row):
        rows = jnp.dot(picking, own_rows, preferred_element_type=jnp.float32)
        rows = rows.astype(own_rows.dtype)
        rows = jnp.where(from_l[:, None], left_row[None], rows)
        return jnp.where(from_r[:, None], right_row[None], rows)

    up_prev = gathered(up_state, from_left[2], from_right[2])
    conv_prev = gathered(conv_state, from_left[3], from_right[3])

    latent_f = arrived.astype(jnp.float32)
    prior_f = up_prev.astype(jnp.float32)
    residual_zero = jnp.stack(
        [
            latent_f * up_kernel[0] + prior_f * up_kernel[2],
            latent_f * up_kernel[1] + prior_f * up_kernel[3],
        ],
        axis=1,
    )
    normed_one = layer_norm(residual_zero, norm_gain_one).astype(jnp.bfloat16)
    projections = jnp.einsum(
        "sfd,kde->ksfe", normed_one, qkv_weight, preferred_element_type=jnp.float32
    )
    times = positions[:, None] + jnp.arange(2, dtype=jnp.int32)[None, :]
    queries = rotate(projections[0], times, HEAD_DIM).astype(jnp.bfloat16)
    fresh_keys = rotate(projections[1], times, HEAD_DIM).astype(jnp.bfloat16)
    fresh_values = projections[2].astype(jnp.bfloat16)
    attended = attend(
        queries,
        fresh_keys,
        fresh_values,
        keys_old,
        values_old,
        positions,
        head_share // HEAD_DIM,
        HEAD_DIM,
    )
    partial_heads = jnp.dot(
        attended.reshape(2 * streams, head_share), out_weight, preferred_element_type=jnp.float32
    )
    mixing = section_sum(partial_heads)
    residual_one = residual_zero + scale_attention * mixing.reshape(streams, 2, model_width)
    normed_two = (
        layer_norm(residual_one, norm_gain_two)
        .astype(jnp.bfloat16)
        .reshape(2 * streams, model_width)
    )
    inner_units = jax.nn.gelu(
        jnp.dot(normed_two, in_weight, preferred_element_type=jnp.float32), approximate=False
    ).astype(jnp.bfloat16)
    partial_units = jnp.dot(inner_units, down_weight, preferred_element_type=jnp.float32)
    feed_forward = section_sum(partial_units)
    residual_two = residual_one + scale_feedforward * feed_forward.reshape(streams, 2, model_width)
    excited = jax.nn.elu(residual_two).astype(jnp.bfloat16)
    earlier = jnp.stack([conv_prev, excited[:, 0]], axis=1)
    stride = conv_weight.shape[0] // 2
    audio_out = jnp.einsum(
        "sfi,rci->csfr", excited, conv_weight[:stride], preferred_element_type=jnp.float32
    )
    audio_out = audio_out + jnp.einsum(
        "sfi,rci->csfr", earlier, conv_weight[stride:], preferred_element_type=jnp.float32
    )
    audio_out = audio_out + conv_bias[:, None, None, None]
    audio_out = audio_out.reshape(conv_bias.shape[0], streams * 2 * stride)
    cycle = jnp.arange(window, dtype=jnp.int32)
    hit_first = (cycle[None, :] == jnp.mod(positions, window)[:, None])[..., None]
    hit_second = (cycle[None, :] == jnp.mod(positions + 1, window)[:, None])[..., None]
    new_keys = jnp.where(
        hit_second,
        fresh_keys[:, 1][:, None, :],
        jnp.where(hit_first, fresh_keys[:, 0][:, None, :], keys_old),
    )
    new_values = jnp.where(
        hit_second,
        fresh_values[:, 1][:, None, :],
        jnp.where(hit_first, fresh_values[:, 0][:, None, :], values_old),
    )
    return (audio_out, new_keys, new_values, arrived, excited[:, 1])
def solution(mesh):
    placed = (
        P("batch", None),
        P("batch"),
        P("batch", None, "section"),
        P("batch", None, "section"),
        P("batch", None),
        P("batch", None),
        P("batch"),
        P("batch"),
        P(),
        P(),
        P(None, None, "section"),
        P("section", None),
        P(),
        P(),
        P(None, "section"),
        P("section", None),
        P(),
        P(None, "section", None),
        P("section"),
    )
    return jax.shard_map(
        local,
        mesh=mesh,
        in_specs=placed,
        out_specs=(
            P("section", "batch"),
            P("batch", None, "section"),
            P("batch", None, "section"),
            P("batch", None),
            P("batch", None),
        ),
        check_vma=False,
    )
```

```python
import jax
import jax.numpy as jnp
from jax import lax
from jax.sharding import PartitionSpec as P
from jax.experimental import pallas as pl
from jax.experimental.pallas import tpu as pltpu

HEAD_DIM = 64
CAP = 2
CODE_LANES = 128


EPSILON = 1e-05
MAX_PERIOD = 10000.0


def layer_norm(hidden, weight_gain):
    average = jnp.mean(hidden, axis=-1, keepdims=True)
    centred = hidden - average
    variance = jnp.mean(centred * centred, axis=-1, keepdims=True)
    return centred * lax.rsqrt(variance + EPSILON) * weight_gain


def rotate(features, times, head_width):
    streams = features.shape[0]
    half = head_width // 2
    freqs = MAX_PERIOD ** (-2.0 * jnp.arange(half, dtype=jnp.float32) / head_width)
    angle = times.astype(jnp.float32)[:, :, None] * freqs[None, None, :]
    cosine = jnp.cos(angle)[:, :, None, :]
    sine = jnp.sin(angle)[:, :, None, :]
    paired = features.reshape(streams, 2, -1, half, 2)
    first = paired[..., 0]
    second = paired[..., 1]
    turned = jnp.stack([first * cosine - second * sine, first * sine + second * cosine], axis=-1)
    return turned.reshape(features.shape)


def attend(queries, fresh_keys, fresh_values, old_keys, old_values, starts, local_heads, head_width):
    streams, window, share = old_keys.shape
    head_of = jnp.arange(share, dtype=jnp.int32) // head_width
    head_ids = jnp.arange(local_heads, dtype=jnp.int32)
    in_head = head_of[None, :] == head_ids[:, None]
    lanes = in_head[None, :, None, :]
    masked = jnp.where(lanes, queries[:, None], jnp.zeros((), queries.dtype))
    masked = masked.reshape(streams, local_heads * 2, share)
    score_scale = head_width ** (-0.5)
    cache_scores = (
        jnp.einsum("sxd,swd->sxw", masked, old_keys, preferred_element_type=jnp.float32)
        * score_scale
    )
    fresh_scores = (
        jnp.einsum("sxd,sgd->sxg", masked, fresh_keys, preferred_element_type=jnp.float32)
        * score_scale
    )
    cycle_slots = jnp.arange(window, dtype=jnp.int32)
    held_time = starts[:, None] - window + jnp.mod(cycle_slots[None, :] - starts[:, None], window)
    query_times = starts[:, None] + jnp.arange(2, dtype=jnp.int32)[None, :]
    cache_ok = (held_time[:, None, :] >= 0) & (
        held_time[:, None, :] > query_times[:, :, None] - window
    )
    cache_ok = jnp.broadcast_to(cache_ok[:, None], (streams, local_heads, 2, window)).reshape(
        streams, local_heads * 2, window
    )
    frame_ids = jnp.arange(2, dtype=jnp.int32)
    fresh_ok = jnp.tile(frame_ids[None, :] <= frame_ids[:, None], (local_heads, 1))[None]
    cache_scores = jnp.where(cache_ok, cache_scores, -jnp.inf)
    fresh_scores = jnp.where(fresh_ok, fresh_scores, -jnp.inf)
    score_max = jnp.maximum(
        jnp.max(cache_scores, axis=-1, keepdims=True), jnp.max(fresh_scores, axis=-1, keepdims=True)
    )
    cache_weights = jnp.where(cache_ok, jnp.exp(cache_scores - score_max), 0.0)
    fresh_weights = jnp.where(fresh_ok, jnp.exp(fresh_scores - score_max), 0.0)
    denominator = jnp.sum(cache_weights, axis=-1, keepdims=True) + jnp.sum(
        fresh_weights, axis=-1, keepdims=True
    )
    spread = jnp.einsum(
        "sxw,swd->sxd",
        cache_weights.astype(jnp.bfloat16),
        old_values,
        preferred_element_type=jnp.float32,
    )
    spread = spread + jnp.einsum(
        "sxg,sgd->sxd",
        fresh_weights.astype(jnp.bfloat16),
        fresh_values,
        preferred_element_type=jnp.float32,
    )
    spread = (spread / denominator).reshape(streams, local_heads, 2, share)
    attended = jnp.sum(jnp.where(lanes, spread, 0.0), axis=1)
    return attended.astype(jnp.bfloat16)


def section_sum(partial):
    size = lax.axis_size("section")
    if size & (size - 1):
        return lax.psum(partial.astype(jnp.bfloat16), "section").astype(jnp.float32)
    total = partial.astype(jnp.bfloat16)
    bit = size // 2
    while bit >= 1:
        route = [(i, i ^ bit) for i in range(size)]
        other = lax.ppermute(total, "section", route)
        total = total.astype(jnp.float32) + other.astype(jnp.float32)
        bit //= 2
    return total


def cache_kernel(src_ref, take_ref, keys_ref, values_ref, lbox_ref, rbox_ref, ok_ref, ov_ref):
    streams, window, _ = keys_ref.shape

    def body(n, carry):
        src = src_ref[n]
        take = take_ref[n]
        ok_ref[n] = keys_ref[src]
        ov_ref[n] = values_ref[src]

        @pl.when(take == 1)
        def _():
            ok_ref[n] = lbox_ref[0:window]
            ov_ref[n] = lbox_ref[window : 2 * window]

        @pl.when(take == 2)
        def _():
            ok_ref[n] = rbox_ref[0:window]
            ov_ref[n] = rbox_ref[window : 2 * window]

        return carry

    lax.fori_loop(0, streams, body, 0, unroll=True)


def route_caches(src, take, keys, values, lbox, rbox):
    smem = pl.BlockSpec(memory_space=pltpu.SMEM)
    vmem = pl.BlockSpec(memory_space=pltpu.VMEM)
    shape = jax.ShapeDtypeStruct(keys.shape, keys.dtype)
    moved = 4 * keys.size * keys.dtype.itemsize
    return pl.pallas_call(
        cache_kernel,
        out_shape=(shape, shape),
        in_specs=[smem] * 2 + [vmem] * 4,
        out_specs=(vmem, vmem),
        cost_estimate=pl.CostEstimate(flops=0, transcendentals=0, bytes_accessed=moved),
    )(src, take, keys, values, lbox, rbox)


def one_hot(rows, columns):
    return (rows[:, None] == columns[None, :]).astype(jnp.bfloat16)


def local(
    latents,
    token_slot,
    cache_keys,
    cache_values,
    up_state,
    conv_state,
    cache_slot,
    positions,
    up_kernel,
    norm_gain_one,
    qkv_weight,
    out_weight,
    scale_attention,
    norm_gain_two,
    in_weight,
    down_weight,
    scale_feedforward,
    conv_weight,
    conv_bias,
):
    owners = lax.axis_size("batch")
    own_index = lax.axis_index("batch")
    streams = latents.shape[0]
    model_width = latents.shape[1]
    window = cache_keys.shape[1]
    head_share = cache_keys.shape[2]
    capacity = max(CAP, streams // owners)
    slot_ids = jnp.arange(streams, dtype=jnp.int32)

    dest_owner = cache_slot // streams
    dest_local = cache_slot % streams
    right_owner = jnp.mod(own_index + 1, owners)
    left_owner = jnp.mod(own_index + owners - 1, owners)
    state_rows = model_width // head_share

    def pack(direction_owner):
        chosen = dest_owner == direction_owner
        code = jnp.sum(jnp.where(chosen, dest_local + 1, 0))

        def pick(rows):
            shape = (streams,) + (1,) * (rows.ndim - 1)
            return jnp.sum(jnp.where(chosen.reshape(shape), rows, jnp.zeros((), rows.dtype)), axis=0)

        pieces = [
            pick(cache_keys),
            pick(cache_values),
            pick(up_state).reshape(state_rows, head_share),
            pick(conv_state).reshape(state_rows, head_share),
            jnp.full((8, head_share), code, jnp.int32).astype(jnp.bfloat16),
        ]
        return jnp.concatenate(pieces, axis=0)

    def unpack(box):
        keys = box[:window]
        values = box[window : 2 * window]
        up = box[2 * window : 2 * window + state_rows].reshape(model_width)
        conv = box[2 * window + state_rows : 2 * window + 2 * state_rows].reshape(model_width)
        code = box[2 * window + 2 * state_rows, 0].astype(jnp.int32) - 1
        return keys, values, up, conv, code

    left_box = lax.ppermute(
        pack(right_owner), "batch", [(i, (i + 1) % owners) for i in range(owners)]
    )
    right_box = lax.ppermute(
        pack(left_owner), "batch", [(i, (i - 1) % owners) for i in range(owners)]
    )
    from_left = unpack(left_box)
    from_right = unpack(right_box)

    target = token_slot // streams
    landing = token_slot % streams
    same_before = (target[None, :] == target[:, None]) & (slot_ids[None, :] < slot_ids[:, None])
    arrival_rank = jnp.sum(same_before.astype(jnp.int32), axis=1)
    owner_ids = jnp.arange(owners, dtype=jnp.int32)
    lane_ids = jnp.arange(CODE_LANES, dtype=jnp.int32)
    blocks = []
    code_block = jnp.zeros((owners, CODE_LANES), jnp.int32)
    for rank in range(capacity):
        chosen = (owner_ids[:, None] == target[None, :]) & (arrival_rank == rank)[None, :]
        blocks.append(
            jnp.dot(chosen.astype(jnp.bfloat16), latents, preferred_element_type=jnp.float32)
        )
        code = jnp.sum(jnp.where(chosen, landing[None, :] + 1, 0), axis=1)
        code_block = jnp.where(lane_ids[None, :] == rank, code[:, None], code_block)
    blocks.append(code_block.astype(jnp.float32))
    send = jnp.concatenate(blocks, axis=1).astype(jnp.bfloat16)
    got = lax.all_to_all(send, "batch", split_axis=0, concat_axis=0, tiled=True)
    arrived = jnp.zeros((streams, model_width), jnp.float32)
    for rank in range(capacity):
        got_code = got[:, capacity * model_width + rank].astype(jnp.int32) - 1
        arrived = arrived + jnp.dot(
            one_hot(slot_ids, got_code),
            got[:, rank * model_width : (rank + 1) * model_width],
            preferred_element_type=jnp.float32,
        )
    arrived = arrived.astype(jnp.bfloat16)

    staying = dest_owner == own_index
    source_of = (dest_local[None, :] == slot_ids[:, None]) & staying[None, :]
    source = jnp.sum(jnp.where(source_of, slot_ids[None, :], 0), axis=1)
    from_l = slot_ids == from_left[4]
    from_r = slot_ids == from_right[4]
    take = jnp.where(from_l, 1, jnp.where(from_r, 2, 0)).astype(jnp.int32)
    keys_old, values_old = route_caches(
        source, take, cache_keys, cache_values, left_box, right_box
    )
    picking = source_of.astype(jnp.bfloat16)

    def gathered(own_rows, left_row, right_row):
        rows = jnp.dot(picking, own_rows, preferred_element_type=jnp.float32)
        rows = rows.astype(own_rows.dtype)
        rows = jnp.where(from_l[:, None], left_row[None], rows)
        return jnp.where(from_r[:, None], right_row[None], rows)

    up_prev = gathered(up_state, from_left[2], from_right[2])
    conv_prev = gathered(conv_state, from_left[3], from_right[3])

    latent_f = arrived.astype(jnp.float32)
    prior_f = up_prev.astype(jnp.float32)
    residual_zero = jnp.stack(
        [
            latent_f * up_kernel[0] + prior_f * up_kernel[2],
            latent_f * up_kernel[1] + prior_f * up_kernel[3],
        ],
        axis=1,
    )
    normed_one = layer_norm(residual_zero, norm_gain_one).astype(jnp.bfloat16)
    projections = jnp.einsum(
        "sfd,kde->ksfe", normed_one, qkv_weight, preferred_element_type=jnp.float32
    )
    times = positions[:, None] + jnp.arange(2, dtype=jnp.int32)[None, :]
    queries = rotate(projections[0], times, HEAD_DIM).astype(jnp.bfloat16)
    fresh_keys = rotate(projections[1], times, HEAD_DIM).astype(jnp.bfloat16)
    fresh_values = projections[2].astype(jnp.bfloat16)
    attended = attend(
        queries,
        fresh_keys,
        fresh_values,
        keys_old,
        values_old,
        positions,
        head_share // HEAD_DIM,
        HEAD_DIM,
    )
    partial_heads = jnp.dot(
        attended.reshape(2 * streams, head_share), out_weight, preferred_element_type=jnp.float32
    )
    mixing = section_sum(partial_heads)
    residual_one = residual_zero + scale_attention * mixing.reshape(streams, 2, model_width)
    normed_two = (
        layer_norm(residual_one, norm_gain_two)
        .astype(jnp.bfloat16)
        .reshape(2 * streams, model_width)
    )
    inner_units = jax.nn.gelu(
        jnp.dot(normed_two, in_weight, preferred_element_type=jnp.float32), approximate=False
    ).astype(jnp.bfloat16)
    partial_units = jnp.dot(inner_units, down_weight, preferred_element_type=jnp.float32)
    feed_forward = section_sum(partial_units)
    residual_two = residual_one + scale_feedforward * feed_forward.reshape(streams, 2, model_width)
    excited = jax.nn.elu(residual_two).astype(jnp.bfloat16)
    earlier = jnp.stack([conv_prev, excited[:, 0]], axis=1)
    stride = conv_weight.shape[0] // 2
    audio_out = jnp.einsum(
        "sfi,rci->csfr", excited, conv_weight[:stride], preferred_element_type=jnp.float32
    )
    audio_out = audio_out + jnp.einsum(
        "sfi,rci->csfr", earlier, conv_weight[stride:], preferred_element_type=jnp.float32
    )
    audio_out = audio_out + conv_bias[:, None, None, None]
    audio_out = audio_out.reshape(conv_bias.shape[0], streams * 2 * stride)
    cycle = jnp.arange(window, dtype=jnp.int32)
    hit_first = (cycle[None, :] == jnp.mod(positions, window)[:, None])[..., None]
    hit_second = (cycle[None, :] == jnp.mod(positions + 1, window)[:, None])[..., None]
    new_keys = jnp.where(
        hit_second,
        fresh_keys[:, 1][:, None, :],
        jnp.where(hit_first, fresh_keys[:, 0][:, None, :], keys_old),
    )
    new_values = jnp.where(
        hit_second,
        fresh_values[:, 1][:, None, :],
        jnp.where(hit_first, fresh_values[:, 0][:, None, :], values_old),
    )
    return (audio_out, new_keys, new_values, arrived, excited[:, 1])
def solution(mesh):
    placed = (
        P("batch", None),
        P("batch"),
        P("batch", None, "section"),
        P("batch", None, "section"),
        P("batch", None),
        P("batch", None),
        P("batch"),
        P("batch"),
        P(),
        P(),
        P(None, None, "section"),
        P("section", None),
        P(),
        P(),
        P(None, "section"),
        P("section", None),
        P(),
        P(None, "section", None),
        P("section"),
    )
    return jax.shard_map(
        local,
        mesh=mesh,
        in_specs=placed,
        out_specs=(
            P("section", "batch"),
            P("batch", None, "section"),
            P("batch", None, "section"),
            P("batch", None),
            P("batch", None),
        ),
        check_vma=False,
    )
```

```python
import jax
import jax.numpy as jnp
from jax import lax
from jax.sharding import PartitionSpec as P
from jax.experimental import pallas as pl
from jax.experimental.pallas import tpu as pltpu

HEAD_DIM = 64
CAP = 2
CODE_LANES = 128


EPSILON = 1e-05
MAX_PERIOD = 10000.0


def layer_norm(hidden, weight_gain):
    average = jnp.mean(hidden, axis=-1, keepdims=True)
    centred = hidden - average
    variance = jnp.mean(centred * centred, axis=-1, keepdims=True)
    return centred * lax.rsqrt(variance + EPSILON) * weight_gain


def rotate(features, times, head_width):
    streams = features.shape[0]
    half = head_width // 2
    freqs = MAX_PERIOD ** (-2.0 * jnp.arange(half, dtype=jnp.float32) / head_width)
    angle = times.astype(jnp.float32)[:, :, None] * freqs[None, None, :]
    cosine = jnp.cos(angle)[:, :, None, :]
    sine = jnp.sin(angle)[:, :, None, :]
    paired = features.reshape(streams, 2, -1, half, 2)
    first = paired[..., 0]
    second = paired[..., 1]
    turned = jnp.stack([first * cosine - second * sine, first * sine + second * cosine], axis=-1)
    return turned.reshape(features.shape)


def attend(queries, fresh_keys, fresh_values, old_keys, old_values, starts, local_heads, head_width):
    streams, window, share = old_keys.shape
    head_of = jnp.arange(share, dtype=jnp.int32) // head_width
    head_ids = jnp.arange(local_heads, dtype=jnp.int32)
    in_head = head_of[None, :] == head_ids[:, None]
    lanes = in_head[None, :, None, :]
    masked = jnp.where(lanes, queries[:, None], jnp.zeros((), queries.dtype))
    masked = masked.reshape(streams, local_heads * 2, share)
    score_scale = head_width ** (-0.5)
    cache_scores = (
        jnp.einsum("sxd,swd->sxw", masked, old_keys, preferred_element_type=jnp.float32)
        * score_scale
    )
    fresh_scores = (
        jnp.einsum("sxd,sgd->sxg", masked, fresh_keys, preferred_element_type=jnp.float32)
        * score_scale
    )
    cycle_slots = jnp.arange(window, dtype=jnp.int32)
    held_time = starts[:, None] - window + jnp.mod(cycle_slots[None, :] - starts[:, None], window)
    query_times = starts[:, None] + jnp.arange(2, dtype=jnp.int32)[None, :]
    cache_ok = (held_time[:, None, :] >= 0) & (
        held_time[:, None, :] > query_times[:, :, None] - window
    )
    cache_ok = jnp.broadcast_to(cache_ok[:, None], (streams, local_heads, 2, window)).reshape(
        streams, local_heads * 2, window
    )
    frame_ids = jnp.arange(2, dtype=jnp.int32)
    fresh_ok = jnp.tile(frame_ids[None, :] <= frame_ids[:, None], (local_heads, 1))[None]
    cache_scores = jnp.where(cache_ok, cache_scores, -jnp.inf)
    fresh_scores = jnp.where(fresh_ok, fresh_scores, -jnp.inf)
    score_max = jnp.maximum(
        jnp.max(cache_scores, axis=-1, keepdims=True), jnp.max(fresh_scores, axis=-1, keepdims=True)
    )
    cache_weights = jnp.where(cache_ok, jnp.exp(cache_scores - score_max), 0.0)
    fresh_weights = jnp.where(fresh_ok, jnp.exp(fresh_scores - score_max), 0.0)
    denominator = jnp.sum(cache_weights, axis=-1, keepdims=True) + jnp.sum(
        fresh_weights, axis=-1, keepdims=True
    )
    spread = jnp.einsum(
        "sxw,swd->sxd",
        cache_weights.astype(jnp.bfloat16),
        old_values,
        preferred_element_type=jnp.float32,
    )
    spread = spread + jnp.einsum(
        "sxg,sgd->sxd",
        fresh_weights.astype(jnp.bfloat16),
        fresh_values,
        preferred_element_type=jnp.float32,
    )
    spread = (spread / denominator).reshape(streams, local_heads, 2, share)
    attended = jnp.sum(jnp.where(lanes, spread, 0.0), axis=1)
    return attended.astype(jnp.bfloat16)


def section_sum(partial):
    size = lax.axis_size("section")
    if size & (size - 1):
        return lax.psum(partial.astype(jnp.bfloat16), "section").astype(jnp.float32)
    total = partial.astype(jnp.bfloat16)
    bit = size // 2
    while bit >= 1:
        route = [(i, i ^ bit) for i in range(size)]
        other = lax.ppermute(total, "section", route)
        total = total.astype(jnp.float32) + other.astype(jnp.float32)
        bit //= 2
    return total


def cache_kernel(src_ref, take_ref, keys_hbm, values_hbm, lbox_ref, rbox_ref, ok_ref, ov_ref, sems):
    streams, window, _ = ok_ref.shape
    copies = []
    for n in range(streams):
        src = src_ref[n]
        for which, (source, target) in enumerate(((keys_hbm, ok_ref), (values_hbm, ov_ref))):
            copy = pltpu.make_async_copy(source.at[src], target.at[n], sems.at[which, n])
            copy.start()
            copies.append(copy)
    for copy in copies:
        copy.wait()
    for n in range(streams):
        take = take_ref[n]

        @pl.when(take == 1)
        def _():
            ok_ref[n] = lbox_ref[0:window]
            ov_ref[n] = lbox_ref[window : 2 * window]

        @pl.when(take == 2)
        def _():
            ok_ref[n] = rbox_ref[0:window]
            ov_ref[n] = rbox_ref[window : 2 * window]


def route_caches(src, take, keys, values, lbox, rbox):
    smem = pl.BlockSpec(memory_space=pltpu.SMEM)
    vmem = pl.BlockSpec(memory_space=pltpu.VMEM)
    hbm = pl.BlockSpec(memory_space=pl.ANY)
    shape = jax.ShapeDtypeStruct(keys.shape, keys.dtype)
    moved = 4 * keys.size * keys.dtype.itemsize
    return pl.pallas_call(
        cache_kernel,
        out_shape=(shape, shape),
        in_specs=[smem, smem, hbm, hbm, vmem, vmem],
        out_specs=(vmem, vmem),
        scratch_shapes=[pltpu.SemaphoreType.DMA((2, keys.shape[0]))],
        cost_estimate=pl.CostEstimate(flops=0, transcendentals=0, bytes_accessed=moved),
    )(src, take, keys, values, lbox, rbox)


def one_hot(rows, columns):
    return (rows[:, None] == columns[None, :]).astype(jnp.bfloat16)


def local(
    latents,
    token_slot,
    cache_keys,
    cache_values,
    up_state,
    conv_state,
    cache_slot,
    positions,
    up_kernel,
    norm_gain_one,
    qkv_weight,
    out_weight,
    scale_attention,
    norm_gain_two,
    in_weight,
    down_weight,
    scale_feedforward,
    conv_weight,
    conv_bias,
):
    owners = lax.axis_size("batch")
    own_index = lax.axis_index("batch")
    streams = latents.shape[0]
    model_width = latents.shape[1]
    window = cache_keys.shape[1]
    head_share = cache_keys.shape[2]
    capacity = max(CAP, streams // owners)
    slot_ids = jnp.arange(streams, dtype=jnp.int32)

    dest_owner = cache_slot // streams
    dest_local = cache_slot % streams
    right_owner = jnp.mod(own_index + 1, owners)
    left_owner = jnp.mod(own_index + owners - 1, owners)
    state_rows = model_width // head_share

    def pack(direction_owner):
        chosen = dest_owner == direction_owner
        code = jnp.sum(jnp.where(chosen, dest_local + 1, 0))

        def pick(rows):
            shape = (streams,) + (1,) * (rows.ndim - 1)
            return jnp.sum(jnp.where(chosen.reshape(shape), rows, jnp.zeros((), rows.dtype)), axis=0)

        pieces = [
            pick(cache_keys),
            pick(cache_values),
            pick(up_state).reshape(state_rows, head_share),
            pick(conv_state).reshape(state_rows, head_share),
            jnp.full((8, head_share), code, jnp.int32).astype(jnp.bfloat16),
        ]
        return jnp.concatenate(pieces, axis=0)

    def unpack(box):
        keys = box[:window]
        values = box[window : 2 * window]
        up = box[2 * window : 2 * window + state_rows].reshape(model_width)
        conv = box[2 * window + state_rows : 2 * window + 2 * state_rows].reshape(model_width)
        code = box[2 * window + 2 * state_rows, 0].astype(jnp.int32) - 1
        return keys, values, up, conv, code

    left_box = lax.ppermute(
        pack(right_owner), "batch", [(i, (i + 1) % owners) for i in range(owners)]
    )
    right_box = lax.ppermute(
        pack(left_owner), "batch", [(i, (i - 1) % owners) for i in range(owners)]
    )
    from_left = unpack(left_box)
    from_right = unpack(right_box)

    target = token_slot // streams
    landing = token_slot % streams
    same_before = (target[None, :] == target[:, None]) & (slot_ids[None, :] < slot_ids[:, None])
    arrival_rank = jnp.sum(same_before.astype(jnp.int32), axis=1)
    box_ids = target * capacity + arrival_rank
    placing = one_hot(jnp.arange(owners * capacity, dtype=jnp.int32), box_ids)
    send_rows = jnp.dot(placing, latents, preferred_element_type=jnp.float32).astype(jnp.bfloat16)
    send_codes = jnp.dot(
        placing,
        jnp.broadcast_to((landing + 1).astype(jnp.bfloat16)[:, None], (streams, CODE_LANES)),
        preferred_element_type=jnp.float32,
    ).astype(jnp.bfloat16)
    code_block = send_codes.reshape(owners, capacity, CODE_LANES)[:, :, 0]
    code_block = jnp.pad(code_block, ((0, 0), (0, CODE_LANES - capacity)))
    send = jnp.concatenate(
        [send_rows.reshape(owners, capacity * model_width), code_block], axis=1
    )
    got = lax.all_to_all(send, "batch", split_axis=0, concat_axis=0, tiled=True)
    got_codes = got[:, capacity * model_width : capacity * model_width + capacity]
    got_codes = got_codes.reshape(owners * capacity).astype(jnp.int32) - 1
    got_rows = got[:, : capacity * model_width].reshape(owners * capacity, model_width)
    arrived = jnp.dot(
        one_hot(slot_ids, got_codes), got_rows, preferred_element_type=jnp.float32
    ).astype(jnp.bfloat16)

    staying = dest_owner == own_index
    source_of = (dest_local[None, :] == slot_ids[:, None]) & staying[None, :]
    source = jnp.sum(jnp.where(source_of, slot_ids[None, :], 0), axis=1)
    from_l = slot_ids == from_left[4]
    from_r = slot_ids == from_right[4]
    take = jnp.where(from_l, 1, jnp.where(from_r, 2, 0)).astype(jnp.int32)
    keys_old, values_old = route_caches(
        source, take, cache_keys, cache_values, left_box, right_box
    )
    picking = source_of.astype(jnp.bfloat16)

    def gathered(own_rows, left_row, right_row):
        rows = jnp.dot(picking, own_rows, preferred_element_type=jnp.float32)
        rows = rows.astype(own_rows.dtype)
        rows = jnp.where(from_l[:, None], left_row[None], rows)
        return jnp.where(from_r[:, None], right_row[None], rows)

    up_prev = gathered(up_state, from_left[2], from_right[2])
    conv_prev = gathered(conv_state, from_left[3], from_right[3])

    latent_f = arrived.astype(jnp.float32)
    prior_f = up_prev.astype(jnp.float32)
    residual_zero = jnp.stack(
        [
            latent_f * up_kernel[0] + prior_f * up_kernel[2],
            latent_f * up_kernel[1] + prior_f * up_kernel[3],
        ],
        axis=1,
    )
    normed_one = layer_norm(residual_zero, norm_gain_one).astype(jnp.bfloat16)
    projections = jnp.einsum(
        "sfd,kde->ksfe", normed_one, qkv_weight, preferred_element_type=jnp.float32
    )
    times = positions[:, None] + jnp.arange(2, dtype=jnp.int32)[None, :]
    queries = rotate(projections[0], times, HEAD_DIM).astype(jnp.bfloat16)
    fresh_keys = rotate(projections[1], times, HEAD_DIM).astype(jnp.bfloat16)
    fresh_values = projections[2].astype(jnp.bfloat16)
    attended = attend(
        queries,
        fresh_keys,
        fresh_values,
        keys_old,
        values_old,
        positions,
        head_share // HEAD_DIM,
        HEAD_DIM,
    )
    partial_heads = jnp.dot(
        attended.reshape(2 * streams, head_share), out_weight, preferred_element_type=jnp.float32
    )
    mixing = section_sum(partial_heads)
    residual_one = residual_zero + scale_attention * mixing.reshape(streams, 2, model_width)
    normed_two = (
        layer_norm(residual_one, norm_gain_two)
        .astype(jnp.bfloat16)
        .reshape(2 * streams, model_width)
    )
    inner_units = jax.nn.gelu(
        jnp.dot(normed_two, in_weight, preferred_element_type=jnp.float32), approximate=False
    ).astype(jnp.bfloat16)
    partial_units = jnp.dot(inner_units, down_weight, preferred_element_type=jnp.float32)
    feed_forward = section_sum(partial_units)
    residual_two = residual_one + scale_feedforward * feed_forward.reshape(streams, 2, model_width)
    excited = jax.nn.elu(residual_two).astype(jnp.bfloat16)
    earlier = jnp.stack([conv_prev, excited[:, 0]], axis=1)
    stride = conv_weight.shape[0] // 2
    audio_out = jnp.einsum(
        "sfi,rci->csfr", excited, conv_weight[:stride], preferred_element_type=jnp.float32
    )
    audio_out = audio_out + jnp.einsum(
        "sfi,rci->csfr", earlier, conv_weight[stride:], preferred_element_type=jnp.float32
    )
    audio_out = audio_out + conv_bias[:, None, None, None]
    audio_out = audio_out.reshape(conv_bias.shape[0], streams * 2 * stride)
    cycle = jnp.arange(window, dtype=jnp.int32)
    hit_first = (cycle[None, :] == jnp.mod(positions, window)[:, None])[..., None]
    hit_second = (cycle[None, :] == jnp.mod(positions + 1, window)[:, None])[..., None]
    new_keys = jnp.where(
        hit_second,
        fresh_keys[:, 1][:, None, :],
        jnp.where(hit_first, fresh_keys[:, 0][:, None, :], keys_old),
    )
    new_values = jnp.where(
        hit_second,
        fresh_values[:, 1][:, None, :],
        jnp.where(hit_first, fresh_values[:, 0][:, None, :], values_old),
    )
    return (audio_out, new_keys, new_values, arrived, excited[:, 1])
def solution(mesh):
    placed = (
        P("batch", None),
        P("batch"),
        P("batch", None, "section"),
        P("batch", None, "section"),
        P("batch", None),
        P("batch", None),
        P("batch"),
        P("batch"),
        P(),
        P(),
        P(None, None, "section"),
        P("section", None),
        P(),
        P(),
        P(None, "section"),
        P("section", None),
        P(),
        P(None, "section", None),
        P("section"),
    )
    return jax.shard_map(
        local,
        mesh=mesh,
        in_specs=placed,
        out_specs=(
            P("section", "batch"),
            P("batch", None, "section"),
            P("batch", None, "section"),
            P("batch", None),
            P("batch", None),
        ),
        check_vma=False,
    )
```

```python
import jax
import jax.numpy as jnp
from jax import lax
from jax.sharding import PartitionSpec as P
from jax.experimental import pallas as pl
from jax.experimental.pallas import tpu as pltpu

HEAD_DIM = 64
CAP = 2
CODE_LANES = 128


EPSILON = 1e-05
MAX_PERIOD = 10000.0


def layer_norm(hidden, weight_gain):
    average = jnp.mean(hidden, axis=-1, keepdims=True)
    centred = hidden - average
    variance = jnp.mean(centred * centred, axis=-1, keepdims=True)
    return centred * lax.rsqrt(variance + EPSILON) * weight_gain


def rotate(features, times, head_width):
    streams = features.shape[0]
    half = head_width // 2
    freqs = MAX_PERIOD ** (-2.0 * jnp.arange(half, dtype=jnp.float32) / head_width)
    angle = times.astype(jnp.float32)[:, :, None] * freqs[None, None, :]
    cosine = jnp.cos(angle)[:, :, None, :]
    sine = jnp.sin(angle)[:, :, None, :]
    paired = features.reshape(streams, 2, -1, half, 2)
    first = paired[..., 0]
    second = paired[..., 1]
    turned = jnp.stack([first * cosine - second * sine, first * sine + second * cosine], axis=-1)
    return turned.reshape(features.shape)


def attend(queries, fresh_keys, fresh_values, old_keys, old_values, starts, local_heads, head_width):
    streams, window, share = old_keys.shape
    head_of = jnp.arange(share, dtype=jnp.int32) // head_width
    head_ids = jnp.arange(local_heads, dtype=jnp.int32)
    in_head = head_of[None, :] == head_ids[:, None]
    lanes = in_head[None, :, None, :]
    masked = jnp.where(lanes, queries[:, None], jnp.zeros((), queries.dtype))
    masked = masked.reshape(streams, local_heads * 2, share)
    score_scale = head_width ** (-0.5)
    cache_scores = (
        jnp.einsum("sxd,swd->sxw", masked, old_keys, preferred_element_type=jnp.float32)
        * score_scale
    )
    fresh_scores = (
        jnp.einsum("sxd,sgd->sxg", masked, fresh_keys, preferred_element_type=jnp.float32)
        * score_scale
    )
    cycle_slots = jnp.arange(window, dtype=jnp.int32)
    held_time = starts[:, None] - window + jnp.mod(cycle_slots[None, :] - starts[:, None], window)
    query_times = starts[:, None] + jnp.arange(2, dtype=jnp.int32)[None, :]
    cache_ok = (held_time[:, None, :] >= 0) & (
        held_time[:, None, :] > query_times[:, :, None] - window
    )
    cache_ok = jnp.broadcast_to(cache_ok[:, None], (streams, local_heads, 2, window)).reshape(
        streams, local_heads * 2, window
    )
    frame_ids = jnp.arange(2, dtype=jnp.int32)
    fresh_ok = jnp.tile(frame_ids[None, :] <= frame_ids[:, None], (local_heads, 1))[None]
    cache_scores = jnp.where(cache_ok, cache_scores, -jnp.inf)
    fresh_scores = jnp.where(fresh_ok, fresh_scores, -jnp.inf)
    score_max = jnp.maximum(
        jnp.max(cache_scores, axis=-1, keepdims=True), jnp.max(fresh_scores, axis=-1, keepdims=True)
    )
    cache_weights = jnp.where(cache_ok, jnp.exp(cache_scores - score_max), 0.0)
    fresh_weights = jnp.where(fresh_ok, jnp.exp(fresh_scores - score_max), 0.0)
    denominator = jnp.sum(cache_weights, axis=-1, keepdims=True) + jnp.sum(
        fresh_weights, axis=-1, keepdims=True
    )
    spread = jnp.einsum(
        "sxw,swd->sxd",
        cache_weights.astype(jnp.bfloat16),
        old_values,
        preferred_element_type=jnp.float32,
    )
    spread = spread + jnp.einsum(
        "sxg,sgd->sxd",
        fresh_weights.astype(jnp.bfloat16),
        fresh_values,
        preferred_element_type=jnp.float32,
    )
    spread = (spread / denominator).reshape(streams, local_heads, 2, share)
    attended = jnp.sum(jnp.where(lanes, spread, 0.0), axis=1)
    return attended.astype(jnp.bfloat16)


def section_sum(partial):
    size = lax.axis_size("section")
    if size & (size - 1):
        return lax.psum(partial.astype(jnp.bfloat16), "section").astype(jnp.float32)
    total = partial.astype(jnp.bfloat16)
    bit = 1
    while bit < size:
        route = [(i, i ^ bit) for i in range(size)]
        other = lax.ppermute(total, "section", route)
        total = total.astype(jnp.float32) + other.astype(jnp.float32)
        bit *= 2
    return total


def cache_kernel(src_ref, take_ref, keys_ref, values_ref, lbox_ref, rbox_ref, ok_ref, ov_ref):
    streams, window, _ = keys_ref.shape

    def body(n, carry):
        src = src_ref[n]
        take = take_ref[n]
        ok_ref[n] = keys_ref[src]
        ov_ref[n] = values_ref[src]

        @pl.when(take == 1)
        def _():
            ok_ref[n] = lbox_ref[0:window]
            ov_ref[n] = lbox_ref[window : 2 * window]

        @pl.when(take == 2)
        def _():
            ok_ref[n] = rbox_ref[0:window]
            ov_ref[n] = rbox_ref[window : 2 * window]

        return carry

    lax.fori_loop(0, streams, body, 0)


def route_caches(src, take, keys, values, lbox, rbox):
    smem = pl.BlockSpec(memory_space=pltpu.SMEM)
    vmem = pl.BlockSpec(memory_space=pltpu.VMEM)
    shape = jax.ShapeDtypeStruct(keys.shape, keys.dtype)
    moved = 4 * keys.size * keys.dtype.itemsize
    return pl.pallas_call(
        cache_kernel,
        out_shape=(shape, shape),
        in_specs=[smem] * 2 + [vmem] * 4,
        out_specs=(vmem, vmem),
        cost_estimate=pl.CostEstimate(flops=0, transcendentals=0, bytes_accessed=moved),
    )(src, take, keys, values, lbox, rbox)


def one_hot(rows, columns):
    return (rows[:, None] == columns[None, :]).astype(jnp.bfloat16)


def local(
    latents,
    token_slot,
    cache_keys,
    cache_values,
    up_state,
    conv_state,
    cache_slot,
    positions,
    up_kernel,
    norm_gain_one,
    qkv_weight,
    out_weight,
    scale_attention,
    norm_gain_two,
    in_weight,
    down_weight,
    scale_feedforward,
    conv_weight,
    conv_bias,
):
    owners = lax.axis_size("batch")
    own_index = lax.axis_index("batch")
    streams = latents.shape[0]
    model_width = latents.shape[1]
    window = cache_keys.shape[1]
    head_share = cache_keys.shape[2]
    capacity = max(CAP, streams // owners)
    slot_ids = jnp.arange(streams, dtype=jnp.int32)

    dest_owner = cache_slot // streams
    dest_local = cache_slot % streams
    right_owner = jnp.mod(own_index + 1, owners)
    left_owner = jnp.mod(own_index + owners - 1, owners)
    state_rows = model_width // head_share

    def pack(direction_owner):
        chosen = dest_owner == direction_owner
        code = jnp.sum(jnp.where(chosen, dest_local + 1, 0))

        def pick(rows):
            shape = (streams,) + (1,) * (rows.ndim - 1)
            return jnp.sum(jnp.where(chosen.reshape(shape), rows, jnp.zeros((), rows.dtype)), axis=0)

        pieces = [
            pick(cache_keys),
            pick(cache_values),
            pick(up_state).reshape(state_rows, head_share),
            pick(conv_state).reshape(state_rows, head_share),
            jnp.full((8, head_share), code, jnp.int32).astype(jnp.bfloat16),
        ]
        return jnp.concatenate(pieces, axis=0)

    def unpack(box):
        keys = box[:window]
        values = box[window : 2 * window]
        up = box[2 * window : 2 * window + state_rows].reshape(model_width)
        conv = box[2 * window + state_rows : 2 * window + 2 * state_rows].reshape(model_width)
        code = box[2 * window + 2 * state_rows, 0].astype(jnp.int32) - 1
        return keys, values, up, conv, code

    left_box = lax.ppermute(
        pack(right_owner), "batch", [(i, (i + 1) % owners) for i in range(owners)]
    )
    right_box = lax.ppermute(
        pack(left_owner), "batch", [(i, (i - 1) % owners) for i in range(owners)]
    )
    from_left = unpack(left_box)
    from_right = unpack(right_box)

    target = token_slot // streams
    landing = token_slot % streams
    same_before = (target[None, :] == target[:, None]) & (slot_ids[None, :] < slot_ids[:, None])
    arrival_rank = jnp.sum(same_before.astype(jnp.int32), axis=1)
    box_ids = target * capacity + arrival_rank
    placing = one_hot(jnp.arange(owners * capacity, dtype=jnp.int32), box_ids)
    send_rows = jnp.dot(placing, latents, preferred_element_type=jnp.float32).astype(jnp.bfloat16)
    send_codes = jnp.dot(
        placing,
        jnp.broadcast_to((landing + 1).astype(jnp.bfloat16)[:, None], (streams, CODE_LANES)),
        preferred_element_type=jnp.float32,
    ).astype(jnp.bfloat16)
    code_block = send_codes.reshape(owners, capacity, CODE_LANES)[:, :, 0]
    code_block = jnp.pad(code_block, ((0, 0), (0, CODE_LANES - capacity)))
    send = jnp.concatenate(
        [send_rows.reshape(owners, capacity * model_width), code_block], axis=1
    )
    got = lax.all_to_all(send, "batch", split_axis=0, concat_axis=0, tiled=True)
    got_codes = got[:, capacity * model_width : capacity * model_width + capacity]
    got_codes = got_codes.reshape(owners * capacity).astype(jnp.int32) - 1
    got_rows = got[:, : capacity * model_width].reshape(owners * capacity, model_width)
    arrived = jnp.dot(
        one_hot(slot_ids, got_codes), got_rows, preferred_element_type=jnp.float32
    ).astype(jnp.bfloat16)

    staying = dest_owner == own_index
    source_of = (dest_local[None, :] == slot_ids[:, None]) & staying[None, :]
    source = jnp.sum(jnp.where(source_of, slot_ids[None, :], 0), axis=1)
    from_l = slot_ids == from_left[4]
    from_r = slot_ids == from_right[4]
    take = jnp.where(from_l, 1, jnp.where(from_r, 2, 0)).astype(jnp.int32)
    keys_old, values_old = route_caches(
        source, take, cache_keys, cache_values, left_box, right_box
    )
    picking = source_of.astype(jnp.bfloat16)

    def gathered(own_rows, left_row, right_row):
        rows = jnp.dot(picking, own_rows, preferred_element_type=jnp.float32)
        rows = rows.astype(own_rows.dtype)
        rows = jnp.where(from_l[:, None], left_row[None], rows)
        return jnp.where(from_r[:, None], right_row[None], rows)

    up_prev = gathered(up_state, from_left[2], from_right[2])
    conv_prev = gathered(conv_state, from_left[3], from_right[3])

    latent_f = arrived.astype(jnp.float32)
    prior_f = up_prev.astype(jnp.float32)
    residual_zero = jnp.stack(
        [
            latent_f * up_kernel[0] + prior_f * up_kernel[2],
            latent_f * up_kernel[1] + prior_f * up_kernel[3],
        ],
        axis=1,
    )
    normed_one = layer_norm(residual_zero, norm_gain_one).astype(jnp.bfloat16)
    projections = jnp.einsum(
        "sfd,kde->ksfe", normed_one, qkv_weight, preferred_element_type=jnp.float32
    )
    times = positions[:, None] + jnp.arange(2, dtype=jnp.int32)[None, :]
    queries = rotate(projections[0], times, HEAD_DIM).astype(jnp.bfloat16)
    fresh_keys = rotate(projections[1], times, HEAD_DIM).astype(jnp.bfloat16)
    fresh_values = projections[2].astype(jnp.bfloat16)
    attended = attend(
        queries,
        fresh_keys,
        fresh_values,
        keys_old,
        values_old,
        positions,
        head_share // HEAD_DIM,
        HEAD_DIM,
    )
    partial_heads = jnp.dot(
        attended.reshape(2 * streams, head_share), out_weight, preferred_element_type=jnp.float32
    )
    mixing = section_sum(partial_heads)
    residual_one = residual_zero + scale_attention * mixing.reshape(streams, 2, model_width)
    normed_two = (
        layer_norm(residual_one, norm_gain_two)
        .astype(jnp.bfloat16)
        .reshape(2 * streams, model_width)
    )
    inner_units = jax.nn.gelu(
        jnp.dot(normed_two, in_weight, preferred_element_type=jnp.float32), approximate=False
    ).astype(jnp.bfloat16)
    partial_units = jnp.dot(inner_units, down_weight, preferred_element_type=jnp.float32)
    feed_forward = section_sum(partial_units)
    residual_two = residual_one + scale_feedforward * feed_forward.reshape(streams, 2, model_width)
    excited = jax.nn.elu(residual_two).astype(jnp.bfloat16)
    earlier = jnp.stack([conv_prev, excited[:, 0]], axis=1)
    stride = conv_weight.shape[0] // 2
    audio_out = jnp.einsum(
        "sfi,rci->csfr", excited, conv_weight[:stride], preferred_element_type=jnp.float32
    )
    audio_out = audio_out + jnp.einsum(
        "sfi,rci->csfr", earlier, conv_weight[stride:], preferred_element_type=jnp.float32
    )
    audio_out = audio_out + conv_bias[:, None, None, None]
    audio_out = audio_out.reshape(conv_bias.shape[0], streams * 2 * stride)
    cycle = jnp.arange(window, dtype=jnp.int32)
    hit_first = (cycle[None, :] == jnp.mod(positions, window)[:, None])[..., None]
    hit_second = (cycle[None, :] == jnp.mod(positions + 1, window)[:, None])[..., None]
    new_keys = jnp.where(
        hit_second,
        fresh_keys[:, 1][:, None, :],
        jnp.where(hit_first, fresh_keys[:, 0][:, None, :], keys_old),
    )
    new_values = jnp.where(
        hit_second,
        fresh_values[:, 1][:, None, :],
        jnp.where(hit_first, fresh_values[:, 0][:, None, :], values_old),
    )
    return (audio_out, new_keys, new_values, arrived, excited[:, 1])
def solution(mesh):
    placed = (
        P("batch", None),
        P("batch"),
        P("batch", None, "section"),
        P("batch", None, "section"),
        P("batch", None),
        P("batch", None),
        P("batch"),
        P("batch"),
        P(),
        P(),
        P(None, None, "section"),
        P("section", None),
        P(),
        P(),
        P(None, "section"),
        P("section", None),
        P(),
        P(None, "section", None),
        P("section"),
    )
    return jax.shard_map(
        local,
        mesh=mesh,
        in_specs=placed,
        out_specs=(
            P("section", "batch"),
            P("batch", None, "section"),
            P("batch", None, "section"),
            P("batch", None),
            P("batch", None),
        ),
        check_vma=False,
    )
```

```python
import jax
import jax.numpy as jnp
from jax import lax
from jax.sharding import PartitionSpec as P
from jax.experimental import pallas as pl
from jax.experimental.pallas import tpu as pltpu

HEAD_DIM = 64
CAP = 2
CODE_LANES = 128


EPSILON = 1e-05
MAX_PERIOD = 10000.0


def layer_norm(hidden, weight_gain):
    average = jnp.mean(hidden, axis=-1, keepdims=True)
    centred = hidden - average
    variance = jnp.mean(centred * centred, axis=-1, keepdims=True)
    return centred * lax.rsqrt(variance + EPSILON) * weight_gain


def rotate(features, times, head_width):
    streams = features.shape[0]
    half = head_width // 2
    freqs = MAX_PERIOD ** (-2.0 * jnp.arange(half, dtype=jnp.float32) / head_width)
    angle = times.astype(jnp.float32)[:, :, None] * freqs[None, None, :]
    cosine = jnp.cos(angle)[:, :, None, :]
    sine = jnp.sin(angle)[:, :, None, :]
    paired = features.reshape(streams, 2, -1, half, 2)
    first = paired[..., 0]
    second = paired[..., 1]
    turned = jnp.stack([first * cosine - second * sine, first * sine + second * cosine], axis=-1)
    return turned.reshape(features.shape)


def attend(queries, fresh_keys, fresh_values, old_keys, old_values, starts, local_heads, head_width):
    streams, window, share = old_keys.shape
    head_of = jnp.arange(share, dtype=jnp.int32) // head_width
    head_ids = jnp.arange(local_heads, dtype=jnp.int32)
    in_head = head_of[None, :] == head_ids[:, None]
    lanes = in_head[None, :, None, :]
    masked = jnp.where(lanes, queries[:, None], jnp.zeros((), queries.dtype))
    masked = masked.reshape(streams, local_heads * 2, share)
    score_scale = head_width ** (-0.5)
    cache_scores = (
        jnp.einsum("sxd,swd->sxw", masked, old_keys, preferred_element_type=jnp.float32)
        * score_scale
    )
    fresh_scores = (
        jnp.einsum("sxd,sgd->sxg", masked, fresh_keys, preferred_element_type=jnp.float32)
        * score_scale
    )
    cycle_slots = jnp.arange(window, dtype=jnp.int32)
    held_time = starts[:, None] - window + jnp.mod(cycle_slots[None, :] - starts[:, None], window)
    query_times = starts[:, None] + jnp.arange(2, dtype=jnp.int32)[None, :]
    cache_ok = (held_time[:, None, :] >= 0) & (
        held_time[:, None, :] > query_times[:, :, None] - window
    )
    cache_ok = jnp.broadcast_to(cache_ok[:, None], (streams, local_heads, 2, window)).reshape(
        streams, local_heads * 2, window
    )
    frame_ids = jnp.arange(2, dtype=jnp.int32)
    fresh_ok = jnp.tile(frame_ids[None, :] <= frame_ids[:, None], (local_heads, 1))[None]
    cache_scores = jnp.where(cache_ok, cache_scores, -jnp.inf)
    fresh_scores = jnp.where(fresh_ok, fresh_scores, -jnp.inf)
    score_max = jnp.maximum(
        jnp.max(cache_scores, axis=-1, keepdims=True), jnp.max(fresh_scores, axis=-1, keepdims=True)
    )
    cache_weights = jnp.where(cache_ok, jnp.exp(cache_scores - score_max), 0.0)
    fresh_weights = jnp.where(fresh_ok, jnp.exp(fresh_scores - score_max), 0.0)
    denominator = jnp.sum(cache_weights, axis=-1, keepdims=True) + jnp.sum(
        fresh_weights, axis=-1, keepdims=True
    )
    spread = jnp.einsum(
        "sxw,swd->sxd",
        cache_weights.astype(jnp.bfloat16),
        old_values,
        preferred_element_type=jnp.float32,
    )
    spread = spread + jnp.einsum(
        "sxg,sgd->sxd",
        fresh_weights.astype(jnp.bfloat16),
        fresh_values,
        preferred_element_type=jnp.float32,
    )
    spread = (spread / denominator).reshape(streams, local_heads, 2, share)
    attended = jnp.sum(jnp.where(lanes, spread, 0.0), axis=1)
    return attended.astype(jnp.bfloat16)


def section_sum(partial):
    size = lax.axis_size("section")
    if size & (size - 1):
        return lax.psum(partial.astype(jnp.bfloat16), "section").astype(jnp.float32)
    total = partial.astype(jnp.bfloat16)
    bit = 1
    while bit < size:
        route = [(i, i ^ bit) for i in range(size)]
        total = total.astype(jnp.bfloat16)
        other = lax.ppermute(total, "section", route)
        total = total.astype(jnp.float32) + other.astype(jnp.float32)
        bit *= 2
    return total


def cache_kernel(src_ref, take_ref, keys_ref, values_ref, lbox_ref, rbox_ref, ok_ref, ov_ref):
    streams, window, _ = keys_ref.shape

    def body(n, carry):
        src = src_ref[n]
        take = take_ref[n]
        ok_ref[n] = keys_ref[src]
        ov_ref[n] = values_ref[src]

        @pl.when(take == 1)
        def _():
            ok_ref[n] = lbox_ref[0:window]
            ov_ref[n] = lbox_ref[window : 2 * window]

        @pl.when(take == 2)
        def _():
            ok_ref[n] = rbox_ref[0:window]
            ov_ref[n] = rbox_ref[window : 2 * window]

        return carry

    lax.fori_loop(0, streams, body, 0)


def route_caches(src, take, keys, values, lbox, rbox):
    smem = pl.BlockSpec(memory_space=pltpu.SMEM)
    vmem = pl.BlockSpec(memory_space=pltpu.VMEM)
    shape = jax.ShapeDtypeStruct(keys.shape, keys.dtype)
    moved = 4 * keys.size * keys.dtype.itemsize
    return pl.pallas_call(
        cache_kernel,
        out_shape=(shape, shape),
        in_specs=[smem] * 2 + [vmem] * 4,
        out_specs=(vmem, vmem),
        cost_estimate=pl.CostEstimate(flops=0, transcendentals=0, bytes_accessed=moved),
    )(src, take, keys, values, lbox, rbox)


def one_hot(rows, columns):
    return (rows[:, None] == columns[None, :]).astype(jnp.bfloat16)


def local(
    latents,
    token_slot,
    cache_keys,
    cache_values,
    up_state,
    conv_state,
    cache_slot,
    positions,
    up_kernel,
    norm_gain_one,
    qkv_weight,
    out_weight,
    scale_attention,
    norm_gain_two,
    in_weight,
    down_weight,
    scale_feedforward,
    conv_weight,
    conv_bias,
):
    owners = lax.axis_size("batch")
    own_index = lax.axis_index("batch")
    streams = latents.shape[0]
    model_width = latents.shape[1]
    window = cache_keys.shape[1]
    head_share = cache_keys.shape[2]
    capacity = max(CAP, streams // owners)
    slot_ids = jnp.arange(streams, dtype=jnp.int32)

    dest_owner = cache_slot // streams
    dest_local = cache_slot % streams
    right_owner = jnp.mod(own_index + 1, owners)
    left_owner = jnp.mod(own_index + owners - 1, owners)
    state_rows = model_width // head_share

    def pack(direction_owner):
        chosen = dest_owner == direction_owner
        code = jnp.sum(jnp.where(chosen, dest_local + 1, 0))

        def pick(rows):
            shape = (streams,) + (1,) * (rows.ndim - 1)
            return jnp.sum(jnp.where(chosen.reshape(shape), rows, jnp.zeros((), rows.dtype)), axis=0)

        pieces = [
            pick(cache_keys),
            pick(cache_values),
            pick(up_state).reshape(state_rows, head_share),
            pick(conv_state).reshape(state_rows, head_share),
            jnp.full((8, head_share), code, jnp.int32).astype(jnp.bfloat16),
        ]
        return jnp.concatenate(pieces, axis=0)

    def unpack(box):
        keys = box[:window]
        values = box[window : 2 * window]
        up = box[2 * window : 2 * window + state_rows].reshape(model_width)
        conv = box[2 * window + state_rows : 2 * window + 2 * state_rows].reshape(model_width)
        code = box[2 * window + 2 * state_rows, 0].astype(jnp.int32) - 1
        return keys, values, up, conv, code

    left_box = lax.ppermute(
        pack(right_owner), "batch", [(i, (i + 1) % owners) for i in range(owners)]
    )
    right_box = lax.ppermute(
        pack(left_owner), "batch", [(i, (i - 1) % owners) for i in range(owners)]
    )
    from_left = unpack(left_box)
    from_right = unpack(right_box)

    target = token_slot // streams
    landing = token_slot % streams
    same_before = (target[None, :] == target[:, None]) & (slot_ids[None, :] < slot_ids[:, None])
    arrival_rank = jnp.sum(same_before.astype(jnp.int32), axis=1)
    box_ids = target * capacity + arrival_rank
    placing = one_hot(jnp.arange(owners * capacity, dtype=jnp.int32), box_ids)
    send_rows = jnp.dot(placing, latents, preferred_element_type=jnp.float32).astype(jnp.bfloat16)
    send_codes = jnp.dot(
        placing,
        jnp.broadcast_to((landing + 1).astype(jnp.bfloat16)[:, None], (streams, CODE_LANES)),
        preferred_element_type=jnp.float32,
    ).astype(jnp.bfloat16)
    code_block = send_codes.reshape(owners, capacity, CODE_LANES)[:, :, 0]
    code_block = jnp.pad(code_block, ((0, 0), (0, CODE_LANES - capacity)))
    send = jnp.concatenate(
        [send_rows.reshape(owners, capacity * model_width), code_block], axis=1
    )
    got = lax.all_to_all(send, "batch", split_axis=0, concat_axis=0, tiled=True)
    got_codes = got[:, capacity * model_width : capacity * model_width + capacity]
    got_codes = got_codes.reshape(owners * capacity).astype(jnp.int32) - 1
    got_rows = got[:, : capacity * model_width].reshape(owners * capacity, model_width)
    arrived = jnp.dot(
        one_hot(slot_ids, got_codes), got_rows, preferred_element_type=jnp.float32
    ).astype(jnp.bfloat16)

    staying = dest_owner == own_index
    source_of = (dest_local[None, :] == slot_ids[:, None]) & staying[None, :]
    source = jnp.sum(jnp.where(source_of, slot_ids[None, :], 0), axis=1)
    from_l = slot_ids == from_left[4]
    from_r = slot_ids == from_right[4]
    take = jnp.where(from_l, 1, jnp.where(from_r, 2, 0)).astype(jnp.int32)
    keys_old, values_old = route_caches(
        source, take, cache_keys, cache_values, left_box, right_box
    )
    picking = source_of.astype(jnp.bfloat16)

    def gathered(own_rows, left_row, right_row):
        rows = jnp.dot(picking, own_rows, preferred_element_type=jnp.float32)
        rows = rows.astype(own_rows.dtype)
        rows = jnp.where(from_l[:, None], left_row[None], rows)
        return jnp.where(from_r[:, None], right_row[None], rows)

    up_prev = gathered(up_state, from_left[2], from_right[2])
    conv_prev = gathered(conv_state, from_left[3], from_right[3])

    latent_f = arrived.astype(jnp.float32)
    prior_f = up_prev.astype(jnp.float32)
    residual_zero = jnp.stack(
        [
            latent_f * up_kernel[0] + prior_f * up_kernel[2],
            latent_f * up_kernel[1] + prior_f * up_kernel[3],
        ],
        axis=1,
    )
    normed_one = layer_norm(residual_zero, norm_gain_one).astype(jnp.bfloat16)
    projections = jnp.einsum(
        "sfd,kde->ksfe", normed_one, qkv_weight, preferred_element_type=jnp.float32
    )
    times = positions[:, None] + jnp.arange(2, dtype=jnp.int32)[None, :]
    queries = rotate(projections[0], times, HEAD_DIM).astype(jnp.bfloat16)
    fresh_keys = rotate(projections[1], times, HEAD_DIM).astype(jnp.bfloat16)
    fresh_values = projections[2].astype(jnp.bfloat16)
    attended = attend(
        queries,
        fresh_keys,
        fresh_values,
        keys_old,
        values_old,
        positions,
        head_share // HEAD_DIM,
        HEAD_DIM,
    )
    partial_heads = jnp.dot(
        attended.reshape(2 * streams, head_share), out_weight, preferred_element_type=jnp.float32
    )
    mixing = section_sum(partial_heads)
    residual_one = residual_zero + scale_attention * mixing.reshape(streams, 2, model_width)
    normed_two = (
        layer_norm(residual_one, norm_gain_two)
        .astype(jnp.bfloat16)
        .reshape(2 * streams, model_width)
    )
    inner_units = jax.nn.gelu(
        jnp.dot(normed_two, in_weight, preferred_element_type=jnp.float32), approximate=False
    ).astype(jnp.bfloat16)
    partial_units = jnp.dot(inner_units, down_weight, preferred_element_type=jnp.float32)
    feed_forward = section_sum(partial_units)
    residual_two = residual_one + scale_feedforward * feed_forward.reshape(streams, 2, model_width)
    excited = jax.nn.elu(residual_two).astype(jnp.bfloat16)
    earlier = jnp.stack([conv_prev, excited[:, 0]], axis=1)
    stride = conv_weight.shape[0] // 2
    audio_out = jnp.einsum(
        "sfi,rci->csfr", excited, conv_weight[:stride], preferred_element_type=jnp.float32
    )
    audio_out = audio_out + jnp.einsum(
        "sfi,rci->csfr", earlier, conv_weight[stride:], preferred_element_type=jnp.float32
    )
    audio_out = audio_out + conv_bias[:, None, None, None]
    audio_out = audio_out.reshape(conv_bias.shape[0], streams * 2 * stride)
    cycle = jnp.arange(window, dtype=jnp.int32)
    hit_first = (cycle[None, :] == jnp.mod(positions, window)[:, None])[..., None]
    hit_second = (cycle[None, :] == jnp.mod(positions + 1, window)[:, None])[..., None]
    new_keys = jnp.where(
        hit_second,
        fresh_keys[:, 1][:, None, :],
        jnp.where(hit_first, fresh_keys[:, 0][:, None, :], keys_old),
    )
    new_values = jnp.where(
        hit_second,
        fresh_values[:, 1][:, None, :],
        jnp.where(hit_first, fresh_values[:, 0][:, None, :], values_old),
    )
    return (audio_out, new_keys, new_values, arrived, excited[:, 1])
def solution(mesh):
    placed = (
        P("batch", None),
        P("batch"),
        P("batch", None, "section"),
        P("batch", None, "section"),
        P("batch", None),
        P("batch", None),
        P("batch"),
        P("batch"),
        P(),
        P(),
        P(None, None, "section"),
        P("section", None),
        P(),
        P(),
        P(None, "section"),
        P("section", None),
        P(),
        P(None, "section", None),
        P("section"),
    )
    return jax.shard_map(
        local,
        mesh=mesh,
        in_specs=placed,
        out_specs=(
            P("section", "batch"),
            P("batch", None, "section"),
            P("batch", None, "section"),
            P("batch", None),
            P("batch", None),
        ),
        check_vma=False,
    )
```

```python
import jax
import jax.numpy as jnp
from jax import lax
from jax.sharding import PartitionSpec as P
from jax.experimental import pallas as pl
from jax.experimental.pallas import tpu as pltpu

HEAD_DIM = 64
CAP = 2
CODE_LANES = 128


EPSILON = 1e-05
MAX_PERIOD = 10000.0


def layer_norm(hidden, weight_gain):
    average = jnp.mean(hidden, axis=-1, keepdims=True)
    centred = hidden - average
    variance = jnp.mean(centred * centred, axis=-1, keepdims=True)
    return centred * lax.rsqrt(variance + EPSILON) * weight_gain


def rotate(features, times, head_width):
    streams = features.shape[0]
    half = head_width // 2
    freqs = MAX_PERIOD ** (-2.0 * jnp.arange(half, dtype=jnp.float32) / head_width)
    angle = times.astype(jnp.float32)[:, :, None] * freqs[None, None, :]
    cosine = jnp.cos(angle)[:, :, None, :]
    sine = jnp.sin(angle)[:, :, None, :]
    paired = features.reshape(streams, 2, -1, half, 2)
    first = paired[..., 0]
    second = paired[..., 1]
    turned = jnp.stack([first * cosine - second * sine, first * sine + second * cosine], axis=-1)
    return turned.reshape(features.shape)


def attend(queries, fresh_keys, fresh_values, old_keys, old_values, starts, local_heads, head_width):
    streams, window, share = old_keys.shape
    head_of = jnp.arange(share, dtype=jnp.int32) // head_width
    head_ids = jnp.arange(local_heads, dtype=jnp.int32)
    in_head = head_of[None, :] == head_ids[:, None]
    lanes = in_head[None, :, None, :]
    masked = jnp.where(lanes, queries[:, None], jnp.zeros((), queries.dtype))
    masked = masked.reshape(streams, local_heads * 2, share)
    score_scale = head_width ** (-0.5)
    cache_scores = (
        jnp.einsum("sxd,swd->sxw", masked, old_keys, preferred_element_type=jnp.float32)
        * score_scale
    )
    fresh_scores = (
        jnp.einsum("sxd,sgd->sxg", masked, fresh_keys, preferred_element_type=jnp.float32)
        * score_scale
    )
    cycle_slots = jnp.arange(window, dtype=jnp.int32)
    held_time = starts[:, None] - window + jnp.mod(cycle_slots[None, :] - starts[:, None], window)
    query_times = starts[:, None] + jnp.arange(2, dtype=jnp.int32)[None, :]
    cache_ok = (held_time[:, None, :] >= 0) & (
        held_time[:, None, :] > query_times[:, :, None] - window
    )
    cache_ok = jnp.broadcast_to(cache_ok[:, None], (streams, local_heads, 2, window)).reshape(
        streams, local_heads * 2, window
    )
    frame_ids = jnp.arange(2, dtype=jnp.int32)
    fresh_ok = jnp.tile(frame_ids[None, :] <= frame_ids[:, None], (local_heads, 1))[None]
    cache_scores = jnp.where(cache_ok, cache_scores, -jnp.inf)
    fresh_scores = jnp.where(fresh_ok, fresh_scores, -jnp.inf)
    score_max = jnp.maximum(
        jnp.max(cache_scores, axis=-1, keepdims=True), jnp.max(fresh_scores, axis=-1, keepdims=True)
    )
    cache_weights = jnp.where(cache_ok, jnp.exp(cache_scores - score_max), 0.0)
    fresh_weights = jnp.where(fresh_ok, jnp.exp(fresh_scores - score_max), 0.0)
    denominator = jnp.sum(cache_weights, axis=-1, keepdims=True) + jnp.sum(
        fresh_weights, axis=-1, keepdims=True
    )
    spread = jnp.einsum(
        "sxw,swd->sxd",
        cache_weights.astype(jnp.bfloat16),
        old_values,
        preferred_element_type=jnp.float32,
    )
    spread = spread + jnp.einsum(
        "sxg,sgd->sxd",
        fresh_weights.astype(jnp.bfloat16),
        fresh_values,
        preferred_element_type=jnp.float32,
    )
    spread = (spread / denominator).reshape(streams, local_heads, 2, share)
    attended = jnp.sum(jnp.where(lanes, spread, 0.0), axis=1)
    return attended.astype(jnp.bfloat16)


def section_sum(partial):
    size = lax.axis_size("section")
    if size & (size - 1):
        return lax.psum(partial.astype(jnp.bfloat16), "section").astype(jnp.float32)
    total = partial.astype(jnp.bfloat16)
    bit = 1
    while bit < size:
        route = [(i, i ^ bit) for i in range(size)]
        total = total.astype(jnp.bfloat16)
        other = lax.ppermute(total, "section", route)
        total = total.astype(jnp.float32) + other.astype(jnp.float32)
        bit *= 2
    return total


def cache_kernel(src_ref, take_ref, keys_ref, values_ref, lbox_ref, rbox_ref, ok_ref, ov_ref):
    streams, window, _ = keys_ref.shape

    def body(n, carry):
        src = src_ref[n]
        take = take_ref[n]
        ok_ref[n] = keys_ref[src]
        ov_ref[n] = values_ref[src]

        @pl.when(take == 1)
        def _():
            ok_ref[n] = lbox_ref[0:window]
            ov_ref[n] = lbox_ref[window : 2 * window]

        @pl.when(take == 2)
        def _():
            ok_ref[n] = rbox_ref[0:window]
            ov_ref[n] = rbox_ref[window : 2 * window]

        return carry

    lax.fori_loop(0, streams, body, 0, unroll=True)


def route_caches(src, take, keys, values, lbox, rbox):
    smem = pl.BlockSpec(memory_space=pltpu.SMEM)
    vmem = pl.BlockSpec(memory_space=pltpu.VMEM)
    shape = jax.ShapeDtypeStruct(keys.shape, keys.dtype)
    moved = 4 * keys.size * keys.dtype.itemsize
    return pl.pallas_call(
        cache_kernel,
        out_shape=(shape, shape),
        in_specs=[smem] * 2 + [vmem] * 4,
        out_specs=(vmem, vmem),
        cost_estimate=pl.CostEstimate(flops=0, transcendentals=0, bytes_accessed=moved),
    )(src, take, keys, values, lbox, rbox)


def one_hot(rows, columns):
    return (rows[:, None] == columns[None, :]).astype(jnp.bfloat16)


def local(
    latents,
    token_slot,
    cache_keys,
    cache_values,
    up_state,
    conv_state,
    cache_slot,
    positions,
    up_kernel,
    norm_gain_one,
    qkv_weight,
    out_weight,
    scale_attention,
    norm_gain_two,
    in_weight,
    down_weight,
    scale_feedforward,
    conv_weight,
    conv_bias,
):
    owners = lax.axis_size("batch")
    own_index = lax.axis_index("batch")
    streams = latents.shape[0]
    model_width = latents.shape[1]
    window = cache_keys.shape[1]
    head_share = cache_keys.shape[2]
    capacity = max(CAP, streams // owners)
    slot_ids = jnp.arange(streams, dtype=jnp.int32)

    dest_owner = cache_slot // streams
    dest_local = cache_slot % streams
    right_owner = jnp.mod(own_index + 1, owners)
    left_owner = jnp.mod(own_index + owners - 1, owners)
    state_rows = model_width // head_share

    def pack(direction_owner):
        chosen = dest_owner == direction_owner
        code = jnp.sum(jnp.where(chosen, dest_local + 1, 0))

        def pick(rows):
            shape = (streams,) + (1,) * (rows.ndim - 1)
            return jnp.sum(jnp.where(chosen.reshape(shape), rows, jnp.zeros((), rows.dtype)), axis=0)

        pieces = [
            pick(cache_keys),
            pick(cache_values),
            pick(up_state).reshape(state_rows, head_share),
            pick(conv_state).reshape(state_rows, head_share),
            jnp.full((8, head_share), code, jnp.int32).astype(jnp.bfloat16),
        ]
        return jnp.concatenate(pieces, axis=0)

    def unpack(box):
        keys = box[:window]
        values = box[window : 2 * window]
        up = box[2 * window : 2 * window + state_rows].reshape(model_width)
        conv = box[2 * window + state_rows : 2 * window + 2 * state_rows].reshape(model_width)
        code = box[2 * window + 2 * state_rows, 0].astype(jnp.int32) - 1
        return keys, values, up, conv, code

    left_box = lax.ppermute(
        pack(right_owner), "batch", [(i, (i + 1) % owners) for i in range(owners)]
    )
    right_box = lax.ppermute(
        pack(left_owner), "batch", [(i, (i - 1) % owners) for i in range(owners)]
    )
    from_left = unpack(left_box)
    from_right = unpack(right_box)

    target = token_slot // streams
    landing = token_slot % streams
    same_before = (target[None, :] == target[:, None]) & (slot_ids[None, :] < slot_ids[:, None])
    arrival_rank = jnp.sum(same_before.astype(jnp.int32), axis=1)
    box_ids = target * capacity + arrival_rank
    placing = one_hot(jnp.arange(owners * capacity, dtype=jnp.int32), box_ids)
    send_rows = jnp.dot(placing, latents, preferred_element_type=jnp.float32).astype(jnp.bfloat16)
    send_codes = jnp.dot(
        placing,
        jnp.broadcast_to((landing + 1).astype(jnp.bfloat16)[:, None], (streams, CODE_LANES)),
        preferred_element_type=jnp.float32,
    ).astype(jnp.bfloat16)
    code_block = send_codes.reshape(owners, capacity, CODE_LANES)[:, :, 0]
    code_block = jnp.pad(code_block, ((0, 0), (0, CODE_LANES - capacity)))
    send = jnp.concatenate(
        [send_rows.reshape(owners, capacity * model_width), code_block], axis=1
    )
    got = lax.all_to_all(send, "batch", split_axis=0, concat_axis=0, tiled=True)
    got_codes = got[:, capacity * model_width : capacity * model_width + capacity]
    got_codes = got_codes.reshape(owners * capacity).astype(jnp.int32) - 1
    got_rows = got[:, : capacity * model_width].reshape(owners * capacity, model_width)
    arrived = jnp.dot(
        one_hot(slot_ids, got_codes), got_rows, preferred_element_type=jnp.float32
    ).astype(jnp.bfloat16)

    staying = dest_owner == own_index
    source_of = (dest_local[None, :] == slot_ids[:, None]) & staying[None, :]
    source = jnp.sum(jnp.where(source_of, slot_ids[None, :], 0), axis=1)
    from_l = slot_ids == from_left[4]
    from_r = slot_ids == from_right[4]
    take = jnp.where(from_l, 1, jnp.where(from_r, 2, 0)).astype(jnp.int32)
    keys_old, values_old = route_caches(
        source, take, cache_keys, cache_values, left_box, right_box
    )
    picking = source_of.astype(jnp.bfloat16)

    def gathered(own_rows, left_row, right_row):
        rows = jnp.dot(picking, own_rows, preferred_element_type=jnp.float32)
        rows = rows.astype(own_rows.dtype)
        rows = jnp.where(from_l[:, None], left_row[None], rows)
        return jnp.where(from_r[:, None], right_row[None], rows)

    up_prev = gathered(up_state, from_left[2], from_right[2])
    conv_prev = gathered(conv_state, from_left[3], from_right[3])

    latent_f = arrived.astype(jnp.float32)
    prior_f = up_prev.astype(jnp.float32)
    residual_zero = jnp.stack(
        [
            latent_f * up_kernel[0] + prior_f * up_kernel[2],
            latent_f * up_kernel[1] + prior_f * up_kernel[3],
        ],
        axis=1,
    )
    normed_one = layer_norm(residual_zero, norm_gain_one).astype(jnp.bfloat16)
    projections = jnp.einsum(
        "sfd,kde->ksfe", normed_one, qkv_weight, preferred_element_type=jnp.float32
    )
    times = positions[:, None] + jnp.arange(2, dtype=jnp.int32)[None, :]
    queries = rotate(projections[0], times, HEAD_DIM).astype(jnp.bfloat16)
    fresh_keys = rotate(projections[1], times, HEAD_DIM).astype(jnp.bfloat16)
    fresh_values = projections[2].astype(jnp.bfloat16)
    attended = attend(
        queries,
        fresh_keys,
        fresh_values,
        keys_old,
        values_old,
        positions,
        head_share // HEAD_DIM,
        HEAD_DIM,
    )
    partial_heads = jnp.dot(
        attended.reshape(2 * streams, head_share), out_weight, preferred_element_type=jnp.float32
    )
    mixing = section_sum(partial_heads)
    residual_one = residual_zero + scale_attention * mixing.reshape(streams, 2, model_width)
    normed_two = (
        layer_norm(residual_one, norm_gain_two)
        .astype(jnp.bfloat16)
        .reshape(2 * streams, model_width)
    )
    inner_units = jax.nn.gelu(
        jnp.dot(normed_two, in_weight, preferred_element_type=jnp.float32), approximate=False
    ).astype(jnp.bfloat16)
    partial_units = jnp.dot(inner_units, down_weight, preferred_element_type=jnp.float32)
    feed_forward = section_sum(partial_units)
    residual_two = residual_one + scale_feedforward * feed_forward.reshape(streams, 2, model_width)
    excited = jax.nn.elu(residual_two).astype(jnp.bfloat16)
    earlier = jnp.stack([conv_prev, excited[:, 0]], axis=1)
    stride = conv_weight.shape[0] // 2
    audio_out = jnp.einsum(
        "sfi,rci->csfr", excited, conv_weight[:stride], preferred_element_type=jnp.float32
    )
    audio_out = audio_out + jnp.einsum(
        "sfi,rci->csfr", earlier, conv_weight[stride:], preferred_element_type=jnp.float32
    )
    audio_out = audio_out + conv_bias[:, None, None, None]
    audio_out = audio_out.reshape(conv_bias.shape[0], streams * 2 * stride)
    cycle = jnp.arange(window, dtype=jnp.int32)
    hit_first = (cycle[None, :] == jnp.mod(positions, window)[:, None])[..., None]
    hit_second = (cycle[None, :] == jnp.mod(positions + 1, window)[:, None])[..., None]
    new_keys = jnp.where(
        hit_second,
        fresh_keys[:, 1][:, None, :],
        jnp.where(hit_first, fresh_keys[:, 0][:, None, :], keys_old),
    )
    new_values = jnp.where(
        hit_second,
        fresh_values[:, 1][:, None, :],
        jnp.where(hit_first, fresh_values[:, 0][:, None, :], values_old),
    )
    return (audio_out, new_keys, new_values, arrived, excited[:, 1])
def solution(mesh):
    placed = (
        P("batch", None),
        P("batch"),
        P("batch", None, "section"),
        P("batch", None, "section"),
        P("batch", None),
        P("batch", None),
        P("batch"),
        P("batch"),
        P(),
        P(),
        P(None, None, "section"),
        P("section", None),
        P(),
        P(),
        P(None, "section"),
        P("section", None),
        P(),
        P(None, "section", None),
        P("section"),
    )
    return jax.shard_map(
        local,
        mesh=mesh,
        in_specs=placed,
        out_specs=(
            P("section", "batch"),
            P("batch", None, "section"),
            P("batch", None, "section"),
            P("batch", None),
            P("batch", None),
        ),
        check_vma=False,
    )
```
